32 devices in a mesh: groups: 2 (over y), seq: 4 (over z), head: 2 (over x), rep: 2 (over core).
Axes of the slice: x: 2, y: 2, z: 4, core: 2. Of those that a mesh axis runs over, the one named last changes fastest.
Arguments:
- queries: bfloat16 [4, 3072, 1536], P(('groups', 'rep'), 'seq', 'head'), parts along dimension 0, may hold values from -320 to 320
- key_matrix: bfloat16 [4, 3072, 1536], P(('groups', 'rep'), 'seq', 'head'), parts along dimension 0, may hold values from -8 to 8
- values: bfloat16 [4, 3072, 1536], P(('groups', 'rep'), 'seq', 'head'), parts along dimension 0, may hold values from -6 to 6
- output_gradient: bfloat16 [4, 3072, 1536], P(('groups', 'rep'), 'seq', 'head'), parts along dimension 0, may hold values from -288 to 288
- normed: bfloat16 [4, 3072, 1536], P(('groups', 'rep'), 'seq', 'head'), parts along dimension 0, may hold values from -6 to 6
- adapter_down_weight: bfloat16 [1536, 64], P('head'), may hold values from -0.15625 to 0.15625
- adapter_up_weight: bfloat16 [64, 1536], P(None, 'head'), may hold values from -0.1796875 to 0.1796875
- listed_key_tiles: int32 [16, 3], P('groups'), parts along dimension 0, may hold values from 0 to 7, as said below
- listed_tile_count: int32 [16], P('groups'), parts along dimension 0, may hold values from 1 to 3
Outputs:
- query_grad: bfloat16 [4, 3072, 1536], P(('groups', 'rep'), 'seq', 'head'), parts along dimension 0
- key_grad: bfloat16 [4, 3072, 1536], P(('groups', 'rep'), 'seq', 'head'), parts along dimension 0
- value_gradient: bfloat16 [4, 3072, 1536], P(('groups', 'rep'), 'seq', 'head'), parts along dimension 0
- down_projection_grad: float32 [3072, 64], P(('groups', 'head')), parts along dimension 0
- up_projection_grad: float32 [128, 1536], P('groups', 'head'), parts along dimension 0
The draws below stay inside these ranges and needn't reach their ends.
There are 2 independent parts, one for each index of `groups`. The reference program is written for one: setup_inputs(seed, part) draws one part's arguments, and reference() takes and returns one part's arrays. A program takes and returns all parts, laid end to end along the dimension named above; an argument that names none is the same for every part. Nothing has to cross between parts.
Inputs may be any that keep to these rules, and one draw needn't show every extreme that they name: `listed_key_tiles`: for query tile i the first listed_tile_count[i] entries are distinct tiles within 1 tiles of i, one of them i itself; the remaining entries equal i.
All inputs are finite; a program needn't handle non-finite values.
Results may differ from the reference program's by a relative error of at most 0.0078.
Values may be sent and summed in bfloat16 or wider, within the bound.
No kernel may reach another device: no remote copies, remote signals or barrier semaphores. Data moves between devices by JAX's collectives and lax.ppermute only.
A program may use at most 64 MiB of HBM per device.

```python
import jax
import jax.numpy as jnp
from jax import lax

TILE = 384
TILES_DEV = 2
REACH = 1
HEAD_SLICE = 12
HEAD_SIZE = 128
FEATURE_SLICE = 1536
ADAPTER_RANK = 64
NTILES = 8
TOKENS = 3072
CLIPS = 2
N_SEQ = 4


def attention_pair(key):
    array_shape = (CLIPS, TOKENS, HEAD_SLICE * HEAD_SIZE)
    base_query = jax.random.truncated_normal(jax.random.fold_in(key, 11), -4.0, 4.0, array_shape, jnp.float32)
    base_key = jax.random.truncated_normal(jax.random.fold_in(key, 12), -4.0, 4.0, array_shape, jnp.float32)
    key_out = base_key
    query_out = base_query
    return (query_out, key_out)


def draw_queries(key, part):
    return attention_pair(key)[0].astype(jnp.bfloat16)


def draw_key_matrix(key, part):
    return attention_pair(key)[1].astype(jnp.bfloat16)


def block_lists(key):
    window_len = 2 * REACH + 1
    offsets = jnp.arange(window_len, dtype=jnp.int32) - REACH
    tile_ids = jnp.arange(NTILES, dtype=jnp.int32)
    window = tile_ids[:, None] + offsets[None, :]
    inside = ((window >= 0) & (window < NTILES)).astype(jnp.int32)
    coin_flip = jax.random.randint(jax.random.fold_in(key, 21), (NTILES, window_len), 0, 2, jnp.int32)
    lowest = min(REACH, NTILES - 1)
    highest = max(NTILES - 1 - REACH, lowest)
    full_tile = jax.random.randint(jax.random.fold_in(key, 22), (), lowest, highest + 1, jnp.int32)
    forced = ((tile_ids[:, None] == full_tile) | (offsets[None, :] == 0)).astype(jnp.int32)
    picked = jnp.maximum(coin_flip, forced) * inside
    sort_order = jnp.argsort((1 - picked) * window_len + jnp.arange(window_len, dtype=jnp.int32)[None, :], axis=1)
    counted = jnp.sum(picked, axis=1)
    chosen = jnp.take_along_axis(window, sort_order, axis=1)
    slot_ids = jnp.arange(window_len, dtype=jnp.int32)[None, :]
    listed = jnp.where(slot_ids < counted[:, None], chosen, tile_ids[:, None])
    return (listed.astype(jnp.int32), counted.astype(jnp.int32))


def draw_listed_key_tiles(key, part):
    return block_lists(key)[0]


def draw_listed_tile_count(key, part):
    return block_lists(key)[1]


def level_of(own_key, extent, cuts, least, largest):
    gain, own = 1.0, jax.random.fold_in(own_key, 6)
    for axis_at, blocks in cuts:
        steps = jnp.exp(jax.random.uniform(jax.random.fold_in(own, axis_at), (blocks,), jnp.float32, least / len(cuts), largest / len(cuts)))
        gain = gain * jnp.repeat(steps, extent[axis_at] // blocks).reshape([-1 if axis == axis_at else 1 for axis in range(len(extent))])
    return gain


def centred(own_key, extent, width, most, pieces=(), kind=jnp.bfloat16):
    array = width * jax.random.normal(own_key, extent, jnp.float32)
    if pieces:
        array = array * level_of(own_key, extent, pieces, -0.22, 0.18)
    return jnp.clip(array, -most, most).astype(kind)


def setup_inputs(seed: int = 0, part: int = 0) -> dict:
    streams_of = jax.random.split(jax.random.key(seed), 10)
    part_keys = jax.random.split(jax.random.fold_in(streams_of[9], part), 10)
    return {
        "queries": draw_queries(jax.random.fold_in(jax.random.fold_in(streams_of[9], part), 71), part),
        "key_matrix": draw_key_matrix(jax.random.fold_in(jax.random.fold_in(streams_of[9], part), 71), part),
        "values": centred(part_keys[2], (CLIPS, TOKENS, HEAD_SLICE * HEAD_SIZE), 1.0, 6.0, ((0, 2), (1, 4), (2, 2))),
        "output_gradient": centred(part_keys[3], (CLIPS, TOKENS, HEAD_SLICE * HEAD_SIZE), 48.0, 288.0, ((0, 2), (1, 4), (2, 2))),
        "normed": centred(part_keys[4], (CLIPS, TOKENS, FEATURE_SLICE), 1.0, 6.0, ((0, 2), (1, 4), (2, 2))),
        "adapter_down_weight": centred(streams_of[5], (FEATURE_SLICE, ADAPTER_RANK), FEATURE_SLICE ** -0.5, 0.15625, ((0, 2),)),
        "adapter_up_weight": centred(streams_of[6], (ADAPTER_RANK, HEAD_SLICE * HEAD_SIZE), 0.03, 0.1796875, ((1, 2),)),
        "listed_key_tiles": draw_listed_key_tiles(jax.random.fold_in(jax.random.fold_in(streams_of[9], part), 71), part),
        "listed_tile_count": draw_listed_tile_count(jax.random.fold_in(jax.random.fold_in(streams_of[9], part), 71), part),
    }


adapter_scale = 0.0078125
masked_score = -1.0e30


def halved_rounding(tensor):
    return lax.optimization_barrier(tensor.astype(jnp.bfloat16)).astype(jnp.float32)


def selection(listed_key_tiles, listed_tile_count):
    slot_ids = jnp.arange(listed_key_tiles.shape[1], dtype=jnp.int32)
    live_slot = slot_ids[None, :] < listed_tile_count[:, None]
    targets = jnp.arange(listed_key_tiles.shape[0], dtype=jnp.int32)
    matched = (listed_key_tiles[:, :, None] == targets[None, None, :]) & live_slot[:, :, None]
    return jnp.any(matched, axis=1)


def one_clip(queries, key_matrix, values, output_gradient, allowed):
    score_scale = HEAD_SIZE ** -0.5
    window_len = 2 * REACH + 1
    block_len = TILES_DEV * TILE
    rim_len = REACH * TILE
    wide_len = block_len + 2 * rim_len
    query_f = queries.astype(jnp.float32).reshape(TOKENS, HEAD_SLICE, HEAD_SIZE)
    grad_f = output_gradient.astype(jnp.float32).reshape(TOKENS, HEAD_SLICE, HEAD_SIZE)
    key_pad = jnp.pad(key_matrix.astype(jnp.float32).reshape(TOKENS, HEAD_SLICE, HEAD_SIZE), ((rim_len, rim_len), (0, 0), (0, 0)))
    value_pad = jnp.pad(values.astype(jnp.float32).reshape(TOKENS, HEAD_SLICE, HEAD_SIZE), ((rim_len, rim_len), (0, 0), (0, 0)))
    allowed_pad = jnp.pad(allowed, ((0, 0), (REACH, REACH)))

    def block_step(state_pair, block_num):
        key_acc, value_acc = state_pair
        row_start = (block_num * block_len).astype(jnp.int32)
        wide_keys = lax.dynamic_slice_in_dim(key_pad, row_start, wide_len, 0)
        wide_values = lax.dynamic_slice_in_dim(value_pad, row_start, wide_len, 0)
        block_query = lax.dynamic_slice_in_dim(query_f, row_start, block_len, 0)
        block_grad = lax.dynamic_slice_in_dim(grad_f, row_start, block_len, 0)
        key_part = jnp.zeros((wide_len, HEAD_SLICE, HEAD_SIZE), jnp.float32)
        value_part = jnp.zeros((wide_len, HEAD_SLICE, HEAD_SIZE), jnp.float32)
        query_parts = []
        for tile_num in range(TILES_DEV):
            tile_index = (block_num * TILES_DEV + tile_num).astype(jnp.int32)
            tile_query = block_query[tile_num * TILE:(tile_num + 1) * TILE]
            tile_grad = block_grad[tile_num * TILE:(tile_num + 1) * TILE]
            near_keys = wide_keys[tile_num * TILE:(tile_num + window_len) * TILE]
            near_values = wide_values[tile_num * TILE:(tile_num + window_len) * TILE]
            allowed_row = lax.dynamic_index_in_dim(allowed_pad, tile_index, 0, keepdims=False)
            window_ok = lax.dynamic_slice_in_dim(allowed_row, tile_index, window_len, 0)
            score_bias = jnp.repeat(jnp.where(window_ok, 0.0, masked_score).astype(jnp.float32), TILE)
            scores = score_scale * jnp.einsum('qhd,khd->hqk', tile_query, near_keys) + score_bias[None, None, :]
            row_max = jnp.max(scores, axis=-1, keepdims=True)
            log_total = row_max + jnp.log(jnp.sum(jnp.exp(scores - row_max), axis=-1, keepdims=True))
            weights = halved_rounding(jnp.exp(scores - log_total))
            grad_weights = jnp.einsum('qhd,khd->hqk', tile_grad, near_values)
            row_dot = jnp.sum(weights * grad_weights, axis=-1, keepdims=True)
            grad_scores = halved_rounding(weights * (grad_weights - row_dot))
            query_parts.append(score_scale * jnp.einsum('hqk,khd->qhd', grad_scores, near_keys))
            key_part = key_part.at[tile_num * TILE:(tile_num + window_len) * TILE].add(
                score_scale * jnp.einsum('hqk,qhd->khd', grad_scores, tile_query))
            value_part = value_part.at[tile_num * TILE:(tile_num + window_len) * TILE].add(
                jnp.einsum('hqk,qhd->khd', weights, tile_grad))
        old_keys = lax.dynamic_slice_in_dim(key_acc, row_start, wide_len, 0)
        old_values = lax.dynamic_slice_in_dim(value_acc, row_start, wide_len, 0)
        key_acc = lax.dynamic_update_slice_in_dim(key_acc, old_keys + halved_rounding(key_part), row_start, 0)
        value_acc = lax.dynamic_update_slice_in_dim(value_acc, old_values + halved_rounding(value_part), row_start, 0)
        return (key_acc, value_acc), jnp.concatenate(query_parts, 0).astype(jnp.bfloat16)

    start_acc = jnp.zeros((TOKENS + 2 * rim_len, HEAD_SLICE, HEAD_SIZE), jnp.float32)
    final_pair, query_blocks = lax.scan(block_step, (start_acc, start_acc), jnp.arange(N_SEQ, dtype=jnp.int32))
    key_acc, value_acc = final_pair
    query_grad = query_blocks.reshape(TOKENS, HEAD_SLICE * HEAD_SIZE)
    key_grad = key_acc[rim_len:rim_len + TOKENS].astype(jnp.bfloat16).reshape(TOKENS, HEAD_SLICE * HEAD_SIZE)
    value_gradient = value_acc[rim_len:rim_len + TOKENS].astype(jnp.bfloat16).reshape(TOKENS, HEAD_SLICE * HEAD_SIZE)
    return query_grad, key_grad, value_gradient


def reference(queries, key_matrix, values, output_gradient, normed, adapter_down_weight, adapter_up_weight, listed_key_tiles, listed_tile_count):
    allowed = selection(listed_key_tiles, listed_tile_count)
    query_list, key_list, value_list = [], [], []
    for clip_num in range(CLIPS):
        query_grad, key_grad, value_gradient = one_clip(queries[clip_num], key_matrix[clip_num], values[clip_num],
                                                    output_gradient[clip_num], allowed)
        query_list.append(query_grad)
        key_list.append(key_grad)
        value_list.append(value_gradient)
    query_grad = jnp.stack(query_list, 0)
    key_grad = jnp.stack(key_list, 0)
    value_gradient = jnp.stack(value_list, 0)
    normed_single = normed.astype(jnp.float32)
    value_single = value_gradient.astype(jnp.float32)
    lowered_rows = halved_rounding(jnp.einsum('pqg,gv->pqv', normed_single, adapter_down_weight.astype(jnp.float32)))
    backward_rows = halved_rounding(jnp.einsum('dsi,ji->dsj', value_single, adapter_up_weight.astype(jnp.float32)))
    down_projection_grad = adapter_scale * jnp.einsum('yhm,yhz->mz', normed_single, backward_rows)
    up_projection_grad = adapter_scale * jnp.einsum('igb,igu->bu', lowered_rows, value_single)
    return (query_grad, key_grad, value_gradient, down_projection_grad, up_projection_grad)
```

```python
import jax
import jax.numpy as jnp
from jax import lax
from jax.sharding import PartitionSpec as P

TILE = 384
TILES_DEV = 2
REACH = 1
HEAD_SIZE = 128


adapter_scale = 0.0078125
masked_score = -1e30


def shifted(shard, axis, by):
    peers = lax.axis_size(axis)
    pairs = [(i, i + by) for i in range(peers) if 0 <= i + by < peers]
    return lax.ppermute(shard, axis, pairs)


def butterfly_sum(tree, axis):
    peers = lax.axis_size(axis)
    if peers & (peers - 1):
        return lax.psum(tree, axis)
    step = 1
    while step < peers:
        pairs = [(i, i ^ step) for i in range(peers)]
        other = lax.ppermute(tree, axis, pairs)
        tree = jax.tree.map(lambda a, b: a + b, tree, other)
        step *= 2
    return tree


def chosen_pairs(listed_key_tiles, listed_tile_count, query_tiles, key_tiles):
    total_tiles = listed_key_tiles.shape[0]
    clipped = jnp.clip(query_tiles, 0, total_tiles - 1)
    one_hot = (clipped[:, None] == jnp.arange(total_tiles, dtype=jnp.int32)[None, :]).astype(
        jnp.int32
    )
    key_lists = jnp.sum(one_hot[:, :, None] * listed_key_tiles[None, :, :], axis=1)
    counts = jnp.sum(one_hot * listed_tile_count[None, :], axis=1)
    slot_ids = jnp.arange(listed_key_tiles.shape[1], dtype=jnp.int32)
    matched = (key_lists == key_tiles[:, None]) & (slot_ids[None, :] < counts[:, None])
    inside = (query_tiles >= 0) & (query_tiles < total_tiles)
    return jnp.any(matched, axis=1) & inside


def block_scores(tile_query, keys, bias):
    score_scale = HEAD_SIZE ** (-0.5)
    raw = jnp.einsum("cqhd,ckhd->chqk", tile_query, keys, preferred_element_type=jnp.float32)
    return score_scale * raw + bias


def tile_backward(tile_query, tile_grad, keys, values, biases):
    scores = [block_scores(tile_query, k, b) for k, b in zip(keys, biases)]
    row_max = scores[0].max(axis=-1, keepdims=True)
    for s in scores[1:]:
        row_max = jnp.maximum(row_max, s.max(axis=-1, keepdims=True))
    total = sum(jnp.sum(jnp.exp(s - row_max), axis=-1, keepdims=True) for s in scores)
    log_total = row_max + jnp.log(total)
    weights = [jnp.exp(s - log_total).astype(jnp.bfloat16) for s in scores]
    grad_weights = [
        jnp.einsum("cqhd,ckhd->chqk", tile_grad, v, preferred_element_type=jnp.float32)
        for v in values
    ]
    row_dot = sum(
        jnp.sum(w.astype(jnp.float32) * g, axis=-1, keepdims=True)
        for w, g in zip(weights, grad_weights)
    )
    grad_scores = [
        (w.astype(jnp.float32) * (g - row_dot)).astype(jnp.bfloat16)
        for w, g in zip(weights, grad_weights)
    ]
    return weights, grad_scores


def key_terms(grad_scores, weights, tile_query, tile_grad):
    score_scale = HEAD_SIZE ** (-0.5)
    key_term = score_scale * jnp.einsum(
        "chqk,cqhd->ckhd", grad_scores, tile_query, preferred_element_type=jnp.float32
    )
    value_term = jnp.einsum(
        "chqk,cqhd->ckhd", weights, tile_grad, preferred_element_type=jnp.float32
    )
    return key_term, value_term


def on_device(
    queries,
    key_matrix,
    values,
    output_gradient,
    normed,
    adapter_down_weight,
    adapter_up_weight,
    listed_key_tiles,
    listed_tile_count,
):
    score_scale = HEAD_SIZE ** (-0.5)
    clip_count, block_len, width = queries.shape
    local_heads = width // HEAD_SIZE
    position = lax.axis_index("seq")
    first_tile = position * TILES_DEV

    def heads(x, t):
        return x[:, t * TILE:(t + 1) * TILE].reshape(clip_count, TILE, local_heads, HEAD_SIZE)

    down_piece = jnp.einsum(
        "pqg,gv->pqv", normed, adapter_down_weight, preferred_element_type=jnp.float32
    )
    lowered_rows = butterfly_sum(down_piece, "head").astype(jnp.bfloat16)

    left_kv = shifted(
        jnp.stack((key_matrix[:, block_len - TILE:], values[:, block_len - TILE:]), 0), "seq", 1
    )
    right_kv = shifted(jnp.stack((key_matrix[:, :TILE], values[:, :TILE]), 0), "seq", -1)

    q_a, q_b = heads(queries, 0), heads(queries, 1)
    g_a, g_b = heads(output_gradient, 0), heads(output_gradient, 1)
    k_a, k_b = heads(key_matrix, 0), heads(key_matrix, 1)
    v_a, v_b = heads(values, 0), heads(values, 1)
    k_l = left_kv[0].reshape(clip_count, TILE, local_heads, HEAD_SIZE)
    v_l = left_kv[1].reshape(clip_count, TILE, local_heads, HEAD_SIZE)
    k_r = right_kv[0].reshape(clip_count, TILE, local_heads, HEAD_SIZE)
    v_r = right_kv[1].reshape(clip_count, TILE, local_heads, HEAD_SIZE)

    tile_a, tile_b = first_tile, first_tile + 1
    allowed = chosen_pairs(
        listed_key_tiles,
        listed_tile_count,
        jnp.stack([tile_a, tile_a, tile_a, tile_b, tile_b, tile_b]).astype(jnp.int32),
        jnp.stack([tile_a - 1, tile_a, tile_b, tile_a, tile_b, tile_b + 1]).astype(jnp.int32),
    )
    bias = jnp.where(allowed, 0.0, masked_score).astype(jnp.float32)

    w_a, ds_a = tile_backward(q_a, g_a, (k_l, k_a, k_b), (v_l, v_a, v_b), bias[0:3])
    w_b, ds_b = tile_backward(q_b, g_b, (k_a, k_b, k_r), (v_a, v_b, v_r), bias[3:6])

    dk_l, dv_l = key_terms(ds_a[0], w_a[0], q_a, g_a)
    dk_r, dv_r = key_terms(ds_b[2], w_b[2], q_b, g_b)
    to_left = jnp.stack((dk_l, dv_l), 0).astype(jnp.bfloat16)
    to_right = jnp.stack((dk_r, dv_r), 0).astype(jnp.bfloat16)
    from_right = shifted(to_left, "seq", -1)
    from_left = shifted(to_right, "seq", 1)

    def query_term(ds, keys):
        return sum(
            jnp.einsum("chqk,ckhd->cqhd", d, k, preferred_element_type=jnp.float32)
            for d, k in zip(ds, keys)
        )

    dq_a = score_scale * query_term(ds_a, (k_l, k_a, k_b))
    dq_b = score_scale * query_term(ds_b, (k_a, k_b, k_r))
    query_grad = jnp.concatenate((dq_a, dq_b), 1).reshape(clip_count, block_len, width)
    query_grad = query_grad.astype(jnp.bfloat16)

    dk_aa, dv_aa = key_terms(ds_a[1], w_a[1], q_a, g_a)
    dk_ba, dv_ba = key_terms(ds_b[0], w_b[0], q_b, g_b)
    dk_ab, dv_ab = key_terms(ds_a[2], w_a[2], q_a, g_a)
    dk_bb, dv_bb = key_terms(ds_b[1], w_b[1], q_b, g_b)

    def finish(own, arrived):
        own = own.reshape(clip_count, TILE, width).astype(jnp.bfloat16).astype(jnp.float32)
        return own + arrived.reshape(clip_count, TILE, width).astype(jnp.float32)

    key_grad = jnp.concatenate(
        (finish(dk_aa + dk_ba, from_left[0]), finish(dk_ab + dk_bb, from_right[0])), 1
    ).astype(jnp.bfloat16)
    value_gradient = jnp.concatenate(
        (finish(dv_aa + dv_ba, from_left[1]), finish(dv_ab + dv_bb, from_right[1])), 1
    ).astype(jnp.bfloat16)

    backward_piece = jnp.einsum(
        "dsi,ji->dsj", value_gradient, adapter_up_weight, preferred_element_type=jnp.float32
    )
    backward_rows = butterfly_sum(backward_piece, "head").astype(jnp.bfloat16)
    gradient_down_local = adapter_scale * jnp.einsum(
        "yhm,yhz->mz", normed, backward_rows, preferred_element_type=jnp.float32
    )
    gradient_up_local = adapter_scale * jnp.einsum(
        "igb,igu->bu", lowered_rows, value_gradient, preferred_element_type=jnp.float32
    )
    down_projection_grad, up_projection_grad = butterfly_sum(
        butterfly_sum((gradient_down_local, gradient_up_local), "rep"), "seq"
    )
    return (query_grad, key_grad, value_gradient, down_projection_grad, up_projection_grad)


def solution(mesh):
    in_specs = (
        P(("groups", "rep"), "seq", "head"),
        P(("groups", "rep"), "seq", "head"),
        P(("groups", "rep"), "seq", "head"),
        P(("groups", "rep"), "seq", "head"),
        P(("groups", "rep"), "seq", "head"),
        P("head", None),
        P(None, "head"),
        P("groups", None),
        P("groups"),
    )
    out_specs = (
        P(("groups", "rep"), "seq", "head"),
        P(("groups", "rep"), "seq", "head"),
        P(("groups", "rep"), "seq", "head"),
        P(("groups", "head"), None),
        P("groups", "head"),
    )
    return jax.shard_map(
        on_device, mesh=mesh, in_specs=in_specs, out_specs=out_specs, check_vma=False
    )
```

```python
import jax
import jax.numpy as jnp
from jax import lax
from jax.sharding import PartitionSpec as P
from jax.experimental import pallas as pl
from jax.experimental.pallas import tpu as pltpu

TILE = 384
TILES_DEV = 2
REACH = 1
HEAD_SIZE = 128


adapter_scale = 0.0078125
masked_score = -1e30


def shifted(shard, axis, by):
    peers = lax.axis_size(axis)
    pairs = [(i, i + by) for i in range(peers) if 0 <= i + by < peers]
    return lax.ppermute(shard, axis, pairs)


def butterfly_sum(tree, axis):
    peers = lax.axis_size(axis)
    if peers & (peers - 1):
        return lax.psum(tree, axis)
    step = 1
    while step < peers:
        pairs = [(i, i ^ step) for i in range(peers)]
        other = lax.ppermute(tree, axis, pairs)
        tree = jax.tree.map(lambda a, b: a + b, tree, other)
        step *= 2
    return tree


def chosen_pairs(listed_key_tiles, listed_tile_count, query_tiles, key_tiles):
    total_tiles = listed_key_tiles.shape[0]
    clipped = jnp.clip(query_tiles, 0, total_tiles - 1)
    one_hot = (clipped[:, None] == jnp.arange(total_tiles, dtype=jnp.int32)[None, :]).astype(
        jnp.int32
    )
    key_lists = jnp.sum(one_hot[:, :, None] * listed_key_tiles[None, :, :], axis=1)
    counts = jnp.sum(one_hot * listed_tile_count[None, :], axis=1)
    slot_ids = jnp.arange(listed_key_tiles.shape[1], dtype=jnp.int32)
    matched = (key_lists == key_tiles[:, None]) & (slot_ids[None, :] < counts[:, None])
    inside = (query_tiles >= 0) & (query_tiles < total_tiles)
    return jnp.any(matched, axis=1) & inside


def nt_dot(a, b):
    return lax.dot_general(a, b, (((1,), (1,)), ((), ())), preferred_element_type=jnp.float32)


def tn_dot(a, b):
    return lax.dot_general(a, b, (((0,), (0,)), ((), ())), preferred_element_type=jnp.float32)


def nn_dot(a, b):
    return lax.dot_general(a, b, (((1,), (0,)), ((), ())), preferred_element_type=jnp.float32)


def tile_pass(bias_ref, first, tile_query, tile_grad, keys, values):
    score_scale = HEAD_SIZE ** (-0.5)
    scores = [
        score_scale * nt_dot(tile_query, k) + bias_ref[first + i] for i, k in enumerate(keys)
    ]
    row_max = jnp.max(scores[0], axis=-1, keepdims=True)
    for s in scores[1:]:
        row_max = jnp.maximum(row_max, jnp.max(s, axis=-1, keepdims=True))
    total = sum(jnp.sum(jnp.exp(s - row_max), axis=-1, keepdims=True) for s in scores)
    log_total = row_max + jnp.log(total)
    weights = [jnp.exp(s - log_total).astype(jnp.bfloat16) for s in scores]
    grad_weights = [nt_dot(tile_grad, v) for v in values]
    row_dot = sum(
        jnp.sum(w.astype(jnp.float32) * g, axis=-1, keepdims=True)
        for w, g in zip(weights, grad_weights)
    )
    grad_scores = [
        (w.astype(jnp.float32) * (g - row_dot)).astype(jnp.bfloat16)
        for w, g in zip(weights, grad_weights)
    ]
    query_term = score_scale * sum(nn_dot(d, k) for d, k in zip(grad_scores, keys))
    key_terms = [score_scale * tn_dot(d, tile_query) for d in grad_scores]
    value_terms = [tn_dot(w, tile_grad) for w in weights]
    return query_term, key_terms, value_terms


def attention_kernel(
    bias_ref, q_ref, g_ref, k_ref, v_ref, kl_ref, vl_ref, kr_ref, vr_ref,
    dq_ref, dk_ref, dv_ref, dkl_ref, dvl_ref, dkr_ref, dvr_ref,
):
    q_a, q_b = q_ref[0, :TILE], q_ref[0, TILE:]
    g_a, g_b = g_ref[0, :TILE], g_ref[0, TILE:]
    k_a, k_b = k_ref[0, :TILE], k_ref[0, TILE:]
    v_a, v_b = v_ref[0, :TILE], v_ref[0, TILE:]
    k_l, v_l, k_r, v_r = kl_ref[0], vl_ref[0], kr_ref[0], vr_ref[0]
    dq_a, dk_a3, dv_a3 = tile_pass(bias_ref, 0, q_a, g_a, (k_l, k_a, k_b), (v_l, v_a, v_b))
    dq_b, dk_b3, dv_b3 = tile_pass(bias_ref, 3, q_b, g_b, (k_a, k_b, k_r), (v_a, v_b, v_r))
    dq_ref[0, :TILE] = dq_a.astype(jnp.bfloat16)
    dq_ref[0, TILE:] = dq_b.astype(jnp.bfloat16)
    dk_ref[0, :TILE] = (dk_a3[1] + dk_b3[0]).astype(jnp.bfloat16)
    dk_ref[0, TILE:] = (dk_a3[2] + dk_b3[1]).astype(jnp.bfloat16)
    dv_ref[0, :TILE] = (dv_a3[1] + dv_b3[0]).astype(jnp.bfloat16)
    dv_ref[0, TILE:] = (dv_a3[2] + dv_b3[1]).astype(jnp.bfloat16)
    dkl_ref[0] = dk_a3[0].astype(jnp.bfloat16)
    dvl_ref[0] = dv_a3[0].astype(jnp.bfloat16)
    dkr_ref[0] = dk_b3[2].astype(jnp.bfloat16)
    dvr_ref[0] = dv_b3[2].astype(jnp.bfloat16)


def attention_backward(bias, queries, output_gradient, key_matrix, values, k_l, v_l, k_r, v_r):
    clip_count, block_len, width = queries.shape
    local_heads = width // HEAD_SIZE
    whole = pl.BlockSpec((1, block_len, HEAD_SIZE), lambda c, h: (c, 0, h))
    rim = pl.BlockSpec((1, TILE, HEAD_SIZE), lambda c, h: (c, 0, h))
    whole_shape = jax.ShapeDtypeStruct(queries.shape, jnp.bfloat16)
    rim_shape = jax.ShapeDtypeStruct((clip_count, TILE, width), jnp.bfloat16)
    return pl.pallas_call(
        attention_kernel,
        grid=(clip_count, local_heads),
        in_specs=[pl.BlockSpec(memory_space=pltpu.MemorySpace.SMEM)]
        + [whole] * 4
        + [rim] * 4,
        out_specs=[whole] * 3 + [rim] * 4,
        out_shape=[whole_shape] * 3 + [rim_shape] * 4,
    )(bias, queries, output_gradient, key_matrix, values, k_l, v_l, k_r, v_r)


def on_device(
    queries,
    key_matrix,
    values,
    output_gradient,
    normed,
    adapter_down_weight,
    adapter_up_weight,
    listed_key_tiles,
    listed_tile_count,
):
    block_len = queries.shape[1]
    position = lax.axis_index("seq")
    first_tile = position * TILES_DEV

    down_piece = jnp.einsum(
        "pqg,gv->pqv", normed, adapter_down_weight, preferred_element_type=jnp.float32
    )
    lowered_rows = butterfly_sum(down_piece, "head").astype(jnp.bfloat16)

    left_kv = shifted(
        jnp.stack((key_matrix[:, block_len - TILE:], values[:, block_len - TILE:]), 0), "seq", 1
    )
    right_kv = shifted(jnp.stack((key_matrix[:, :TILE], values[:, :TILE]), 0), "seq", -1)

    tile_a, tile_b = first_tile, first_tile + 1
    allowed = chosen_pairs(
        listed_key_tiles,
        listed_tile_count,
        jnp.stack([tile_a, tile_a, tile_a, tile_b, tile_b, tile_b]).astype(jnp.int32),
        jnp.stack([tile_a - 1, tile_a, tile_b, tile_a, tile_b, tile_b + 1]).astype(jnp.int32),
    )
    bias = jnp.where(allowed, 0.0, masked_score).astype(jnp.float32)

    query_grad, dk_own, dv_own, dk_l, dv_l, dk_r, dv_r = attention_backward(
        bias, queries, output_gradient, key_matrix, values,
        left_kv[0], left_kv[1], right_kv[0], right_kv[1],
    )
    from_right = shifted(jnp.stack((dk_l, dv_l), 0), "seq", -1)
    from_left = shifted(jnp.stack((dk_r, dv_r), 0), "seq", 1)
    arrived = jnp.concatenate((from_left, from_right), 2).astype(jnp.float32)
    key_grad = (dk_own.astype(jnp.float32) + arrived[0]).astype(jnp.bfloat16)
    value_gradient = (dv_own.astype(jnp.float32) + arrived[1]).astype(jnp.bfloat16)

    backward_piece = jnp.einsum(
        "dsi,ji->dsj", value_gradient, adapter_up_weight, preferred_element_type=jnp.float32
    )
    backward_rows = butterfly_sum(backward_piece, "head").astype(jnp.bfloat16)
    gradient_down_local = adapter_scale * jnp.einsum(
        "yhm,yhz->mz", normed, backward_rows, preferred_element_type=jnp.float32
    )
    gradient_up_local = adapter_scale * jnp.einsum(
        "igb,igu->bu", lowered_rows, value_gradient, preferred_element_type=jnp.float32
    )
    down_projection_grad, up_projection_grad = butterfly_sum(
        butterfly_sum((gradient_down_local, gradient_up_local), "rep"), "seq"
    )
    return (query_grad, key_grad, value_gradient, down_projection_grad, up_projection_grad)


def solution(mesh):
    in_specs = (
        P(("groups", "rep"), "seq", "head"),
        P(("groups", "rep"), "seq", "head"),
        P(("groups", "rep"), "seq", "head"),
        P(("groups", "rep"), "seq", "head"),
        P(("groups", "rep"), "seq", "head"),
        P("head", None),
        P(None, "head"),
        P("groups", None),
        P("groups"),
    )
    out_specs = (
        P(("groups", "rep"), "seq", "head"),
        P(("groups", "rep"), "seq", "head"),
        P(("groups", "rep"), "seq", "head"),
        P(("groups", "head"), None),
        P("groups", "head"),
    )
    return jax.shard_map(
        on_device, mesh=mesh, in_specs=in_specs, out_specs=out_specs, check_vma=False
    )
```

```python
import jax
import jax.numpy as jnp
from jax import lax
from jax.sharding import PartitionSpec as P
from jax.experimental import pallas as pl
from jax.experimental.pallas import tpu as pltpu

TILE = 384
TILES_DEV = 2
REACH = 1
HEAD_SIZE = 128


adapter_scale = 0.0078125
masked_score = -1e30


def shifted(shard, axis, by):
    peers = lax.axis_size(axis)
    pairs = [(i, i + by) for i in range(peers) if 0 <= i + by < peers]
    return lax.ppermute(shard, axis, pairs)


def butterfly_sum(tree, axis):
    peers = lax.axis_size(axis)
    if peers & (peers - 1):
        return lax.psum(tree, axis)
    step = 1
    while step < peers:
        pairs = [(i, i ^ step) for i in range(peers)]
        other = lax.ppermute(tree, axis, pairs)
        tree = jax.tree.map(lambda a, b: a + b, tree, other)
        step *= 2
    return tree


def chosen_pairs(listed_key_tiles, listed_tile_count, query_tiles, key_tiles):
    total_tiles = listed_key_tiles.shape[0]
    clipped = jnp.clip(query_tiles, 0, total_tiles - 1)
    one_hot = (clipped[:, None] == jnp.arange(total_tiles, dtype=jnp.int32)[None, :]).astype(
        jnp.int32
    )
    key_lists = jnp.sum(one_hot[:, :, None] * listed_key_tiles[None, :, :], axis=1)
    counts = jnp.sum(one_hot * listed_tile_count[None, :], axis=1)
    slot_ids = jnp.arange(listed_key_tiles.shape[1], dtype=jnp.int32)
    matched = (key_lists == key_tiles[:, None]) & (slot_ids[None, :] < counts[:, None])
    inside = (query_tiles >= 0) & (query_tiles < total_tiles)
    return jnp.any(matched, axis=1) & inside


def nt_dot(a, b):
    return lax.dot_general(a, b, (((1,), (1,)), ((), ())), preferred_element_type=jnp.float32)


def tn_dot(a, b):
    return lax.dot_general(a, b, (((0,), (0,)), ((), ())), preferred_element_type=jnp.float32)


def nn_dot(a, b):
    return lax.dot_general(a, b, (((1,), (0,)), ((), ())), preferred_element_type=jnp.float32)


def tile_pass(bias_ref, first, tile_query, tile_grad, keys, values):
    score_scale = HEAD_SIZE ** (-0.5)
    scores = [
        score_scale * nt_dot(tile_query, k) + bias_ref[first + i] for i, k in enumerate(keys)
    ]
    row_max = jnp.max(scores[0], axis=-1, keepdims=True)
    for s in scores[1:]:
        row_max = jnp.maximum(row_max, jnp.max(s, axis=-1, keepdims=True))
    total = sum(jnp.sum(jnp.exp(s - row_max), axis=-1, keepdims=True) for s in scores)
    log_total = row_max + jnp.log(total)
    weights = [jnp.exp(s - log_total).astype(jnp.bfloat16) for s in scores]
    grad_weights = [nt_dot(tile_grad, v) for v in values]
    row_dot = sum(
        jnp.sum(w.astype(jnp.float32) * g, axis=-1, keepdims=True)
        for w, g in zip(weights, grad_weights)
    )
    grad_scores = [
        (w.astype(jnp.float32) * (g - row_dot)).astype(jnp.bfloat16)
        for w, g in zip(weights, grad_weights)
    ]
    query_term = score_scale * sum(nn_dot(d, k) for d, k in zip(grad_scores, keys))
    key_terms = [score_scale * tn_dot(d, tile_query) for d in grad_scores]
    value_terms = [tn_dot(w, tile_grad) for w in weights]
    return query_term, key_terms, value_terms


def attention_kernel(
    bias_ref, q_ref, g_ref, k_ref, v_ref, kl_ref, vl_ref, kr_ref, vr_ref,
    dq_ref, dk_ref, dv_ref, dkl_ref, dvl_ref, dkr_ref, dvr_ref,
):
    q_a, q_b = q_ref[0, :TILE], q_ref[0, TILE:]
    g_a, g_b = g_ref[0, :TILE], g_ref[0, TILE:]
    k_a, k_b = k_ref[0, :TILE], k_ref[0, TILE:]
    v_a, v_b = v_ref[0, :TILE], v_ref[0, TILE:]
    k_l, v_l, k_r, v_r = kl_ref[0, 0], vl_ref[0, 0], kr_ref[0, 0], vr_ref[0, 0]
    dq_a, dk_a3, dv_a3 = tile_pass(bias_ref, 0, q_a, g_a, (k_l, k_a, k_b), (v_l, v_a, v_b))
    dq_b, dk_b3, dv_b3 = tile_pass(bias_ref, 3, q_b, g_b, (k_a, k_b, k_r), (v_a, v_b, v_r))
    dq_ref[0, :TILE] = dq_a.astype(jnp.bfloat16)
    dq_ref[0, TILE:] = dq_b.astype(jnp.bfloat16)
    dk_ref[0, :TILE] = (dk_a3[1] + dk_b3[0]).astype(jnp.bfloat16)
    dk_ref[0, TILE:] = (dk_a3[2] + dk_b3[1]).astype(jnp.bfloat16)
    dv_ref[0, :TILE] = (dv_a3[1] + dv_b3[0]).astype(jnp.bfloat16)
    dv_ref[0, TILE:] = (dv_a3[2] + dv_b3[1]).astype(jnp.bfloat16)
    dkl_ref[0] = dk_a3[0].astype(jnp.bfloat16)
    dvl_ref[0] = dv_a3[0].astype(jnp.bfloat16)
    dkr_ref[0] = dk_b3[2].astype(jnp.bfloat16)
    dvr_ref[0] = dv_b3[2].astype(jnp.bfloat16)


def attention_backward(bias, chunk, heads, queries, output_gradient, key_matrix, values, halo):
    clip_count, block_len, _ = queries.shape
    whole = pl.BlockSpec((1, block_len, HEAD_SIZE), lambda c, h: (c, 0, h + chunk * heads))
    rims = [pl.BlockSpec((1, 1, TILE, HEAD_SIZE), lambda c, h, i=i: (i, c, 0, h)) for i in range(4)]
    out_whole = pl.BlockSpec((1, block_len, HEAD_SIZE), lambda c, h: (c, 0, h))
    out_rim = pl.BlockSpec((1, TILE, HEAD_SIZE), lambda c, h: (c, 0, h))
    whole_shape = jax.ShapeDtypeStruct((clip_count, block_len, heads * HEAD_SIZE), jnp.bfloat16)
    rim_shape = jax.ShapeDtypeStruct((clip_count, TILE, heads * HEAD_SIZE), jnp.bfloat16)
    return pl.pallas_call(
        attention_kernel,
        grid=(clip_count, heads),
        in_specs=[pl.BlockSpec(memory_space=pltpu.MemorySpace.SMEM)] + [whole] * 4 + rims,
        out_specs=[out_whole] * 3 + [out_rim] * 4,
        out_shape=[whole_shape] * 3 + [rim_shape] * 4,
    )(bias, queries, output_gradient, key_matrix, values, halo, halo, halo, halo)


def on_device(
    queries,
    key_matrix,
    values,
    output_gradient,
    normed,
    adapter_down_weight,
    adapter_up_weight,
    listed_key_tiles,
    listed_tile_count,
):
    block_len = queries.shape[1]
    position = lax.axis_index("seq")
    first_tile = position * TILES_DEV

    down_piece = jnp.einsum(
        "pqg,gv->pqv", normed, adapter_down_weight, preferred_element_type=jnp.float32
    )
    lowered_rows = butterfly_sum(down_piece, "head").astype(jnp.bfloat16)

    tile_a, tile_b = first_tile, first_tile + 1
    allowed = chosen_pairs(
        listed_key_tiles,
        listed_tile_count,
        jnp.stack([tile_a, tile_a, tile_a, tile_b, tile_b, tile_b]).astype(jnp.int32),
        jnp.stack([tile_a - 1, tile_a, tile_b, tile_a, tile_b, tile_b + 1]).astype(jnp.int32),
    )
    bias = jnp.where(allowed, 0.0, masked_score).astype(jnp.float32)

    local_heads = queries.shape[2] // HEAD_SIZE
    chunks = 3 if local_heads % 3 == 0 else (2 if local_heads % 2 == 0 else 1)
    per_chunk = local_heads // chunks
    outs = []
    for chunk in range(chunks):
        cols = slice(chunk * per_chunk * HEAD_SIZE, (chunk + 1) * per_chunk * HEAD_SIZE)
        left_kv = shifted(
            jnp.stack((key_matrix[:, block_len - TILE:, cols], values[:, block_len - TILE:, cols])),
            "seq",
            1,
        )
        right_kv = shifted(
            jnp.stack((key_matrix[:, :TILE, cols], values[:, :TILE, cols]), 0), "seq", -1
        )
        halo = jnp.concatenate((left_kv, right_kv), 0)
        dq, dk_own, dv_own, dk_l, dv_l, dk_r, dv_r = attention_backward(
            bias, chunk, per_chunk, queries, output_gradient, key_matrix, values, halo
        )
        from_right = shifted(jnp.stack((dk_l, dv_l), 0), "seq", -1)
        from_left = shifted(jnp.stack((dk_r, dv_r), 0), "seq", 1)
        arrived = jnp.concatenate((from_left, from_right), 2).astype(jnp.float32)
        dk = (dk_own.astype(jnp.float32) + arrived[0]).astype(jnp.bfloat16)
        dv = (dv_own.astype(jnp.float32) + arrived[1]).astype(jnp.bfloat16)
        outs.append((dq, dk, dv))
    query_grad, key_grad, value_gradient = (
        jnp.concatenate([o[i] for o in outs], 2) for i in range(3)
    )

    backward_piece = jnp.einsum(
        "dsi,ji->dsj", value_gradient, adapter_up_weight, preferred_element_type=jnp.float32
    )
    backward_rows = butterfly_sum(backward_piece, "head").astype(jnp.bfloat16)
    gradient_down_local = adapter_scale * jnp.einsum(
        "yhm,yhz->mz", normed, backward_rows, preferred_element_type=jnp.float32
    )
    gradient_up_local = adapter_scale * jnp.einsum(
        "igb,igu->bu", lowered_rows, value_gradient, preferred_element_type=jnp.float32
    )
    both = jnp.stack((gradient_down_local, gradient_up_local.T), 0)
    both = butterfly_sum(butterfly_sum(both, "rep"), "seq")
    down_projection_grad, up_projection_grad = both[0], both[1].T
    return (query_grad, key_grad, value_gradient, down_projection_grad, up_projection_grad)


def solution(mesh):
    in_specs = (
        P(("groups", "rep"), "seq", "head"),
        P(("groups", "rep"), "seq", "head"),
        P(("groups", "rep"), "seq", "head"),
        P(("groups", "rep"), "seq", "head"),
        P(("groups", "rep"), "seq", "head"),
        P("head", None),
        P(None, "head"),
        P("groups", None),
        P("groups"),
    )
    out_specs = (
        P(("groups", "rep"), "seq", "head"),
        P(("groups", "rep"), "seq", "head"),
        P(("groups", "rep"), "seq", "head"),
        P(("groups", "head"), None),
        P("groups", "head"),
    )
    return jax.shard_map(
        on_device, mesh=mesh, in_specs=in_specs, out_specs=out_specs, check_vma=False
    )
```

```python
import jax
import jax.numpy as jnp
from jax import lax
from jax.sharding import PartitionSpec as P
from jax.experimental import pallas as pl
from jax.experimental.pallas import tpu as pltpu

TILE = 384
TILES_DEV = 2
REACH = 1
HEAD_SIZE = 128


adapter_scale = 0.0078125
masked_score = -1e30


def shifted(shard, axis, by):
    peers = lax.axis_size(axis)
    pairs = [(i, i + by) for i in range(peers) if 0 <= i + by < peers]
    return lax.ppermute(shard, axis, pairs)


def butterfly_sum(tree, axis):
    peers = lax.axis_size(axis)
    if peers & (peers - 1):
        return lax.psum(tree, axis)
    step = 1
    while step < peers:
        pairs = [(i, i ^ step) for i in range(peers)]
        other = lax.ppermute(tree, axis, pairs)
        tree = jax.tree.map(lambda a, b: a + b, tree, other)
        step *= 2
    return tree


def scatter_sum(flat, axis, distances):
    peers = lax.axis_size(axis)
    index = lax.axis_index(axis)
    for step in distances:
        half = flat.shape[0] // 2
        upper = (index & step) != 0
        keep = jnp.where(upper, flat[half:], flat[:half])
        send = jnp.where(upper, flat[:half], flat[half:])
        flat = keep + lax.ppermute(send, axis, [(i, i ^ step) for i in range(peers)])
    return flat


def gather_back(flat, axis, distances):
    peers = lax.axis_size(axis)
    index = lax.axis_index(axis)
    for step in reversed(distances):
        other = lax.ppermute(flat, axis, [(i, i ^ step) for i in range(peers)])
        upper = (index & step) != 0
        flat = jnp.where(upper, jnp.concatenate((other, flat)), jnp.concatenate((flat, other)))
    return flat


def all_sum(array, axes):
    plan = []
    for axis in axes:
        peers = lax.axis_size(axis)
        if peers & (peers - 1):
            return lax.psum(array, axes)
        plan.append((axis, [1 << k for k in range(peers.bit_length() - 1)]))
    pieces = 1
    for _, distances in plan:
        pieces *= 1 << len(distances)
    flat = array.reshape(-1)
    if flat.shape[0] % pieces:
        return lax.psum(array, axes)
    for axis, distances in plan:
        flat = scatter_sum(flat, axis, distances)
    for axis, distances in reversed(plan):
        flat = gather_back(flat, axis, distances)
    return flat.reshape(array.shape)


def chosen_pairs(listed_key_tiles, listed_tile_count, query_tiles, key_tiles):
    total_tiles = listed_key_tiles.shape[0]
    clipped = jnp.clip(query_tiles, 0, total_tiles - 1)
    one_hot = (clipped[:, None] == jnp.arange(total_tiles, dtype=jnp.int32)[None, :]).astype(
        jnp.int32
    )
    key_lists = jnp.sum(one_hot[:, :, None] * listed_key_tiles[None, :, :], axis=1)
    counts = jnp.sum(one_hot * listed_tile_count[None, :], axis=1)
    slot_ids = jnp.arange(listed_key_tiles.shape[1], dtype=jnp.int32)
    matched = (key_lists == key_tiles[:, None]) & (slot_ids[None, :] < counts[:, None])
    inside = (query_tiles >= 0) & (query_tiles < total_tiles)
    return jnp.any(matched, axis=1) & inside


def nt_dot(a, b):
    return lax.dot_general(a, b, (((1,), (1,)), ((), ())), preferred_element_type=jnp.float32)


def tn_dot(a, b):
    return lax.dot_general(a, b, (((0,), (0,)), ((), ())), preferred_element_type=jnp.float32)


def nn_dot(a, b):
    return lax.dot_general(a, b, (((1,), (0,)), ((), ())), preferred_element_type=jnp.float32)


def tile_pass(bias_ref, first, tile_query, tile_grad, keys, values):
    score_scale = HEAD_SIZE ** (-0.5)
    scores = [
        score_scale * nt_dot(tile_query, k) + bias_ref[first + i] for i, k in enumerate(keys)
    ]
    row_max = jnp.max(scores[0], axis=-1, keepdims=True)
    for s in scores[1:]:
        row_max = jnp.maximum(row_max, jnp.max(s, axis=-1, keepdims=True))
    total = sum(jnp.sum(jnp.exp(s - row_max), axis=-1, keepdims=True) for s in scores)
    log_total = row_max + jnp.log(total)
    weights = [jnp.exp(s - log_total).astype(jnp.bfloat16) for s in scores]
    grad_weights = [nt_dot(tile_grad, v) for v in values]
    row_dot = sum(
        jnp.sum(w.astype(jnp.float32) * g, axis=-1, keepdims=True)
        for w, g in zip(weights, grad_weights)
    )
    grad_scores = [
        (w.astype(jnp.float32) * (g - row_dot)).astype(jnp.bfloat16)
        for w, g in zip(weights, grad_weights)
    ]
    query_term = score_scale * sum(nn_dot(d, k) for d, k in zip(grad_scores, keys))
    key_terms = [score_scale * tn_dot(d, tile_query) for d in grad_scores]
    value_terms = [tn_dot(w, tile_grad) for w in weights]
    return query_term, key_terms, value_terms


def attention_kernel(
    bias_ref, q_ref, g_ref, k_ref, v_ref, kl_ref, vl_ref, kr_ref, vr_ref,
    dq_ref, dk_ref, dv_ref, dkl_ref, dvl_ref, dkr_ref, dvr_ref,
):
    q_a, q_b = q_ref[0, :TILE], q_ref[0, TILE:]
    g_a, g_b = g_ref[0, :TILE], g_ref[0, TILE:]
    k_a, k_b = k_ref[0, :TILE], k_ref[0, TILE:]
    v_a, v_b = v_ref[0, :TILE], v_ref[0, TILE:]
    k_l, v_l, k_r, v_r = kl_ref[0, 0], vl_ref[0, 0], kr_ref[0, 0], vr_ref[0, 0]
    dq_a, dk_a3, dv_a3 = tile_pass(bias_ref, 0, q_a, g_a, (k_l, k_a, k_b), (v_l, v_a, v_b))
    dq_b, dk_b3, dv_b3 = tile_pass(bias_ref, 3, q_b, g_b, (k_a, k_b, k_r), (v_a, v_b, v_r))
    dq_ref[0, :TILE] = dq_a.astype(jnp.bfloat16)
    dq_ref[0, TILE:] = dq_b.astype(jnp.bfloat16)
    dk_ref[0, :TILE] = (dk_a3[1] + dk_b3[0]).astype(jnp.bfloat16)
    dk_ref[0, TILE:] = (dk_a3[2] + dk_b3[1]).astype(jnp.bfloat16)
    dv_ref[0, :TILE] = (dv_a3[1] + dv_b3[0]).astype(jnp.bfloat16)
    dv_ref[0, TILE:] = (dv_a3[2] + dv_b3[1]).astype(jnp.bfloat16)
    dkl_ref[0] = dk_a3[0].astype(jnp.bfloat16)
    dvl_ref[0] = dv_a3[0].astype(jnp.bfloat16)
    dkr_ref[0] = dk_b3[2].astype(jnp.bfloat16)
    dvr_ref[0] = dv_b3[2].astype(jnp.bfloat16)


def attention_backward(bias, chunk, heads, queries, output_gradient, key_matrix, values, halo):
    clip_count, block_len, _ = queries.shape
    whole = pl.BlockSpec((1, block_len, HEAD_SIZE), lambda c, h: (c, 0, h + chunk * heads))
    rims = [pl.BlockSpec((1, 1, TILE, HEAD_SIZE), lambda c, h, i=i: (i, c, 0, h)) for i in range(4)]
    out_whole = pl.BlockSpec((1, block_len, HEAD_SIZE), lambda c, h: (c, 0, h))
    out_rim = pl.BlockSpec((1, TILE, HEAD_SIZE), lambda c, h: (c, 0, h))
    whole_shape = jax.ShapeDtypeStruct((clip_count, block_len, heads * HEAD_SIZE), jnp.bfloat16)
    rim_shape = jax.ShapeDtypeStruct((clip_count, TILE, heads * HEAD_SIZE), jnp.bfloat16)
    return pl.pallas_call(
        attention_kernel,
        grid=(clip_count, heads),
        in_specs=[pl.BlockSpec(memory_space=pltpu.MemorySpace.SMEM)] + [whole] * 4 + rims,
        out_specs=[out_whole] * 3 + [out_rim] * 4,
        out_shape=[whole_shape] * 3 + [rim_shape] * 4,
    )(bias, queries, output_gradient, key_matrix, values, halo, halo, halo, halo)


def on_device(
    queries,
    key_matrix,
    values,
    output_gradient,
    normed,
    adapter_down_weight,
    adapter_up_weight,
    listed_key_tiles,
    listed_tile_count,
):
    block_len = queries.shape[1]
    position = lax.axis_index("seq")
    first_tile = position * TILES_DEV

    down_piece = jnp.einsum(
        "pqg,gv->pqv", normed, adapter_down_weight, preferred_element_type=jnp.float32
    )
    lowered_rows = butterfly_sum(down_piece, "head").astype(jnp.bfloat16)

    tile_a, tile_b = first_tile, first_tile + 1
    allowed = chosen_pairs(
        listed_key_tiles,
        listed_tile_count,
        jnp.stack([tile_a, tile_a, tile_a, tile_b, tile_b, tile_b]).astype(jnp.int32),
        jnp.stack([tile_a - 1, tile_a, tile_b, tile_a, tile_b, tile_b + 1]).astype(jnp.int32),
    )
    bias = jnp.where(allowed, 0.0, masked_score).astype(jnp.float32)

    local_heads = queries.shape[2] // HEAD_SIZE
    chunks = 1
    per_chunk = local_heads // chunks
    outs = []
    for chunk in range(chunks):
        cols = slice(chunk * per_chunk * HEAD_SIZE, (chunk + 1) * per_chunk * HEAD_SIZE)
        left_kv = shifted(
            jnp.stack((key_matrix[:, block_len - TILE:, cols], values[:, block_len - TILE:, cols])),
            "seq",
            1,
        )
        right_kv = shifted(
            jnp.stack((key_matrix[:, :TILE, cols], values[:, :TILE, cols]), 0), "seq", -1
        )
        halo = jnp.concatenate((left_kv, right_kv), 0)
        dq, dk_own, dv_own, dk_l, dv_l, dk_r, dv_r = attention_backward(
            bias, chunk, per_chunk, queries, output_gradient, key_matrix, values, halo
        )
        from_right = shifted(jnp.stack((dk_l, dv_l), 0), "seq", -1)
        from_left = shifted(jnp.stack((dk_r, dv_r), 0), "seq", 1)
        arrived = jnp.concatenate((from_left, from_right), 2).astype(jnp.float32)
        dk = (dk_own.astype(jnp.float32) + arrived[0]).astype(jnp.bfloat16)
        dv = (dv_own.astype(jnp.float32) + arrived[1]).astype(jnp.bfloat16)
        outs.append((dq, dk, dv))
    query_grad, key_grad, value_gradient = (
        jnp.concatenate([o[i] for o in outs], 2) for i in range(3)
    )

    backward_piece = jnp.einsum(
        "dsi,ji->dsj", value_gradient, adapter_up_weight, preferred_element_type=jnp.float32
    )
    backward_rows = butterfly_sum(backward_piece, "head").astype(jnp.bfloat16)
    gradient_down_local = adapter_scale * jnp.einsum(
        "yhm,yhz->mz", normed, backward_rows, preferred_element_type=jnp.float32
    )
    gradient_up_local = adapter_scale * jnp.einsum(
        "igb,igu->bu", lowered_rows, value_gradient, preferred_element_type=jnp.float32
    )
    both = jnp.stack((gradient_down_local, gradient_up_local.T), 0)
    both = all_sum(both, ("rep", "seq"))
    down_projection_grad, up_projection_grad = both[0], both[1].T
    return (query_grad, key_grad, value_gradient, down_projection_grad, up_projection_grad)


def solution(mesh):
    in_specs = (
        P(("groups", "rep"), "seq", "head"),
        P(("groups", "rep"), "seq", "head"),
        P(("groups", "rep"), "seq", "head"),
        P(("groups", "rep"), "seq", "head"),
        P(("groups", "rep"), "seq", "head"),
        P("head", None),
        P(None, "head"),
        P("groups", None),
        P("groups"),
    )
    out_specs = (
        P(("groups", "rep"), "seq", "head"),
        P(("groups", "rep"), "seq", "head"),
        P(("groups", "rep"), "seq", "head"),
        P(("groups", "head"), None),
        P("groups", "head"),
    )
    return jax.shard_map(
        on_device, mesh=mesh, in_specs=in_specs, out_specs=out_specs, check_vma=False
    )
```

```python
import jax
import jax.numpy as jnp
from jax import lax
from jax.sharding import PartitionSpec as P
from jax.experimental import pallas as pl
from jax.experimental.pallas import tpu as pltpu

TILE = 384
TILES_DEV = 2
REACH = 1
HEAD_SIZE = 128


adapter_scale = 0.0078125
masked_score = -1e30


def shifted(shard, axis, by):
    peers = lax.axis_size(axis)
    pairs = [(i, i + by) for i in range(peers) if 0 <= i + by < peers]
    return lax.ppermute(shard, axis, pairs)


def butterfly_sum(tree, axis):
    peers = lax.axis_size(axis)
    if peers & (peers - 1):
        return lax.psum(tree, axis)
    step = 1
    while step < peers:
        pairs = [(i, i ^ step) for i in range(peers)]
        other = lax.ppermute(tree, axis, pairs)
        tree = jax.tree.map(lambda a, b: a + b, tree, other)
        step *= 2
    return tree


def scatter_sum(flat, axis, distances):
    peers = lax.axis_size(axis)
    index = lax.axis_index(axis)
    for step in distances:
        half = flat.shape[0] // 2
        upper = (index & step) != 0
        keep = jnp.where(upper, flat[half:], flat[:half])
        send = jnp.where(upper, flat[:half], flat[half:])
        flat = keep + lax.ppermute(send, axis, [(i, i ^ step) for i in range(peers)])
    return flat


def gather_back(flat, axis, distances):
    peers = lax.axis_size(axis)
    index = lax.axis_index(axis)
    for step in reversed(distances):
        other = lax.ppermute(flat, axis, [(i, i ^ step) for i in range(peers)])
        upper = (index & step) != 0
        flat = jnp.where(upper, jnp.concatenate((other, flat)), jnp.concatenate((flat, other)))
    return flat


def all_sum(array, axes):
    plan = []
    for axis in axes:
        peers = lax.axis_size(axis)
        if peers & (peers - 1):
            return lax.psum(array, axes)
        plan.append((axis, [1 << k for k in range(peers.bit_length() - 1)]))
    pieces = 1
    for _, distances in plan:
        pieces *= 1 << len(distances)
    flat = array.reshape(-1)
    if flat.shape[0] % pieces:
        return lax.psum(array, axes)
    for axis, distances in plan:
        flat = scatter_sum(flat, axis, distances)
    for axis, distances in reversed(plan):
        flat = gather_back(flat, axis, distances)
    return flat.reshape(array.shape)


def chosen_pairs(listed_key_tiles, listed_tile_count, query_tiles, key_tiles):
    total_tiles = listed_key_tiles.shape[0]
    clipped = jnp.clip(query_tiles, 0, total_tiles - 1)
    one_hot = (clipped[:, None] == jnp.arange(total_tiles, dtype=jnp.int32)[None, :]).astype(
        jnp.int32
    )
    key_lists = jnp.sum(one_hot[:, :, None] * listed_key_tiles[None, :, :], axis=1)
    counts = jnp.sum(one_hot * listed_tile_count[None, :], axis=1)
    slot_ids = jnp.arange(listed_key_tiles.shape[1], dtype=jnp.int32)
    matched = (key_lists == key_tiles[:, None]) & (slot_ids[None, :] < counts[:, None])
    inside = (query_tiles >= 0) & (query_tiles < total_tiles)
    return jnp.any(matched, axis=1) & inside


def nt_dot(a, b):
    return lax.dot_general(a, b, (((1,), (1,)), ((), ())), preferred_element_type=jnp.float32)


def tn_dot(a, b):
    return lax.dot_general(a, b, (((0,), (0,)), ((), ())), preferred_element_type=jnp.float32)


def nn_dot(a, b):
    return lax.dot_general(a, b, (((1,), (0,)), ((), ())), preferred_element_type=jnp.float32)


def tile_pass(bias_ref, first, tile_query, tile_grad, keys, values):
    score_scale = HEAD_SIZE ** (-0.5)
    scores = [
        score_scale * nt_dot(tile_query, k) + bias_ref[first + i] for i, k in enumerate(keys)
    ]
    row_max = jnp.max(scores[0], axis=-1, keepdims=True)
    for s in scores[1:]:
        row_max = jnp.maximum(row_max, jnp.max(s, axis=-1, keepdims=True))
    total = sum(jnp.sum(jnp.exp(s - row_max), axis=-1, keepdims=True) for s in scores)
    log_total = row_max + jnp.log(total)
    weights = [jnp.exp(s - log_total).astype(jnp.bfloat16) for s in scores]
    grad_weights = [nt_dot(tile_grad, v) for v in values]
    row_dot = sum(
        jnp.sum(w.astype(jnp.float32) * g, axis=-1, keepdims=True)
        for w, g in zip(weights, grad_weights)
    )
    grad_scores = [
        (w.astype(jnp.float32) * (g - row_dot)).astype(jnp.bfloat16)
        for w, g in zip(weights, grad_weights)
    ]
    query_term = score_scale * sum(nn_dot(d, k) for d, k in zip(grad_scores, keys))
    key_terms = [score_scale * tn_dot(d, tile_query) for d in grad_scores]
    value_terms = [tn_dot(w, tile_grad) for w in weights]
    return query_term, key_terms, value_terms


def attention_kernel(
    bias_ref, q_ref, g_ref, k_ref, v_ref, kl_ref, vl_ref, kr_ref, vr_ref,
    dq_ref, dk_ref, dv_ref, dkl_ref, dvl_ref, dkr_ref, dvr_ref,
):
    q_a, q_b = q_ref[0, :TILE], q_ref[0, TILE:]
    g_a, g_b = g_ref[0, :TILE], g_ref[0, TILE:]
    k_a, k_b = k_ref[0, :TILE], k_ref[0, TILE:]
    v_a, v_b = v_ref[0, :TILE], v_ref[0, TILE:]
    k_l, v_l, k_r, v_r = kl_ref[0, 0], vl_ref[0, 0], kr_ref[0, 0], vr_ref[0, 0]
    dq_a, dk_a3, dv_a3 = tile_pass(bias_ref, 0, q_a, g_a, (k_l, k_a, k_b), (v_l, v_a, v_b))
    dq_b, dk_b3, dv_b3 = tile_pass(bias_ref, 3, q_b, g_b, (k_a, k_b, k_r), (v_a, v_b, v_r))
    dq_ref[0, :TILE] = dq_a.astype(jnp.bfloat16)
    dq_ref[0, TILE:] = dq_b.astype(jnp.bfloat16)
    dk_ref[0, :TILE] = (dk_a3[1] + dk_b3[0]).astype(jnp.bfloat16)
    dk_ref[0, TILE:] = (dk_a3[2] + dk_b3[1]).astype(jnp.bfloat16)
    dv_ref[0, :TILE] = (dv_a3[1] + dv_b3[0]).astype(jnp.bfloat16)
    dv_ref[0, TILE:] = (dv_a3[2] + dv_b3[1]).astype(jnp.bfloat16)
    dkl_ref[0] = dk_a3[0].astype(jnp.bfloat16)
    dvl_ref[0] = dv_a3[0].astype(jnp.bfloat16)
    dkr_ref[0] = dk_b3[2].astype(jnp.bfloat16)
    dvr_ref[0] = dv_b3[2].astype(jnp.bfloat16)


def attention_backward(bias, chunk, heads, queries, output_gradient, key_matrix, values, halo):
    clip_count, block_len, _ = queries.shape
    whole = pl.BlockSpec((1, block_len, HEAD_SIZE), lambda c, h: (c, 0, h + chunk * heads))
    rims = [pl.BlockSpec((1, 1, TILE, HEAD_SIZE), lambda c, h, i=i: (i, c, 0, h)) for i in range(4)]
    out_whole = pl.BlockSpec((1, block_len, HEAD_SIZE), lambda c, h: (c, 0, h))
    out_rim = pl.BlockSpec((1, TILE, HEAD_SIZE), lambda c, h: (c, 0, h))
    whole_shape = jax.ShapeDtypeStruct((clip_count, block_len, heads * HEAD_SIZE), jnp.bfloat16)
    rim_shape = jax.ShapeDtypeStruct((clip_count, TILE, heads * HEAD_SIZE), jnp.bfloat16)
    return pl.pallas_call(
        attention_kernel,
        grid=(clip_count, heads),
        in_specs=[pl.BlockSpec(memory_space=pltpu.MemorySpace.SMEM)] + [whole] * 4 + rims,
        out_specs=[out_whole] * 3 + [out_rim] * 4,
        out_shape=[whole_shape] * 3 + [rim_shape] * 4,
    )(bias, queries, output_gradient, key_matrix, values, halo, halo, halo, halo)


def on_device(
    queries,
    key_matrix,
    values,
    output_gradient,
    normed,
    adapter_down_weight,
    adapter_up_weight,
    listed_key_tiles,
    listed_tile_count,
):
    block_len = queries.shape[1]
    position = lax.axis_index("seq")
    first_tile = position * TILES_DEV

    down_piece = jnp.einsum(
        "pqg,gv->pqv", normed, adapter_down_weight, preferred_element_type=jnp.float32
    )
    lowered_rows = butterfly_sum(down_piece, "head").astype(jnp.bfloat16)

    tile_a, tile_b = first_tile, first_tile + 1
    allowed = chosen_pairs(
        listed_key_tiles,
        listed_tile_count,
        jnp.stack([tile_a, tile_a, tile_a, tile_b, tile_b, tile_b]).astype(jnp.int32),
        jnp.stack([tile_a - 1, tile_a, tile_b, tile_a, tile_b, tile_b + 1]).astype(jnp.int32),
    )
    bias = jnp.where(allowed, 0.0, masked_score).astype(jnp.float32)

    low_left = shifted(lowered_rows[:, block_len - TILE:], "seq", 1)
    low_right = shifted(lowered_rows[:, :TILE], "seq", -1)

    left_kv = shifted(
        jnp.stack((key_matrix[:, block_len - TILE:], values[:, block_len - TILE:])), "seq", 1
    )
    right_kv = shifted(jnp.stack((key_matrix[:, :TILE], values[:, :TILE])), "seq", -1)
    halo = jnp.concatenate((left_kv, right_kv), 0)
    query_grad, dk_own, dv_own, dk_l, dv_l, dk_r, dv_r = attention_backward(
        bias, 0, queries.shape[2] // HEAD_SIZE, queries, output_gradient, key_matrix, values, halo
    )

    def project(term):
        return jnp.einsum(
            "dsi,ji->dsj", term, adapter_up_weight, preferred_element_type=jnp.float32
        )

    proj_from_right = shifted(project(dv_l), "seq", -1)
    proj_from_left = shifted(project(dv_r), "seq", 1)
    backward_piece = project(dv_own) + jnp.concatenate((proj_from_left, proj_from_right), 1)
    backward_rows = butterfly_sum(backward_piece, "head").astype(jnp.bfloat16)
    gradient_down_local = adapter_scale * jnp.einsum(
        "yhm,yhz->mz", normed, backward_rows, preferred_element_type=jnp.float32
    )
    up_terms = (
        jnp.einsum("igb,igu->bu", lowered_rows, dv_own, preferred_element_type=jnp.float32)
        + jnp.einsum("igb,igu->bu", low_left, dv_l, preferred_element_type=jnp.float32)
        + jnp.einsum("igb,igu->bu", low_right, dv_r, preferred_element_type=jnp.float32)
    )
    gradient_up_local = adapter_scale * up_terms

    from_right = shifted(jnp.stack((dk_l, dv_l), 0), "seq", -1)
    from_left = shifted(jnp.stack((dk_r, dv_r), 0), "seq", 1)
    arrived = jnp.concatenate((from_left, from_right), 2).astype(jnp.float32)
    key_grad = (dk_own.astype(jnp.float32) + arrived[0]).astype(jnp.bfloat16)
    value_gradient = (dv_own.astype(jnp.float32) + arrived[1]).astype(jnp.bfloat16)

    both = jnp.stack((gradient_down_local, gradient_up_local.T), 0)
    both = all_sum(both, ("rep", "seq"))
    down_projection_grad, up_projection_grad = both[0], both[1].T
    return (query_grad, key_grad, value_gradient, down_projection_grad, up_projection_grad)


def solution(mesh):
    in_specs = (
        P(("groups", "rep"), "seq", "head"),
        P(("groups", "rep"), "seq", "head"),
        P(("groups", "rep"), "seq", "head"),
        P(("groups", "rep"), "seq", "head"),
        P(("groups", "rep"), "seq", "head"),
        P("head", None),
        P(None, "head"),
        P("groups", None),
        P("groups"),
    )
    out_specs = (
        P(("groups", "rep"), "seq", "head"),
        P(("groups", "rep"), "seq", "head"),
        P(("groups", "rep"), "seq", "head"),
        P(("groups", "head"), None),
        P("groups", "head"),
    )
    return jax.shard_map(
        on_device, mesh=mesh, in_specs=in_specs, out_specs=out_specs, check_vma=False
    )
```

```python
import jax
import jax.numpy as jnp
from jax import lax
from jax.sharding import PartitionSpec as P
from jax.experimental import pallas as pl
from jax.experimental.pallas import tpu as pltpu

TILE = 384
TILES_DEV = 2
REACH = 1
HEAD_SIZE = 128


adapter_scale = 0.0078125
masked_score = -1e30


def shifted(shard, axis, by):
    peers = lax.axis_size(axis)
    pairs = [(i, i + by) for i in range(peers) if 0 <= i + by < peers]
    return lax.ppermute(shard, axis, pairs)


def butterfly_sum(tree, axis):
    peers = lax.axis_size(axis)
    if peers & (peers - 1):
        return lax.psum(tree, axis)
    step = 1
    while step < peers:
        pairs = [(i, i ^ step) for i in range(peers)]
        other = lax.ppermute(tree, axis, pairs)
        tree = jax.tree.map(lambda a, b: a + b, tree, other)
        step *= 2
    return tree


def scatter_sum(flat, axis, distances):
    peers = lax.axis_size(axis)
    index = lax.axis_index(axis)
    for step in distances:
        half = flat.shape[0] // 2
        upper = (index & step) != 0
        keep = jnp.where(upper, flat[half:], flat[:half])
        send = jnp.where(upper, flat[:half], flat[half:])
        flat = keep + lax.ppermute(send, axis, [(i, i ^ step) for i in range(peers)])
    return flat


def gather_back(flat, axis, distances):
    peers = lax.axis_size(axis)
    index = lax.axis_index(axis)
    for step in reversed(distances):
        other = lax.ppermute(flat, axis, [(i, i ^ step) for i in range(peers)])
        upper = (index & step) != 0
        flat = jnp.where(upper, jnp.concatenate((other, flat)), jnp.concatenate((flat, other)))
    return flat


def all_sum(array, axes):
    plan = []
    for axis in axes:
        peers = lax.axis_size(axis)
        if peers & (peers - 1):
            return lax.psum(array, axes)
        plan.append((axis, [1 << k for k in range(peers.bit_length() - 1)]))
    pieces = 1
    for _, distances in plan:
        pieces *= 1 << len(distances)
    flat = array.reshape(-1)
    if flat.shape[0] % pieces:
        return lax.psum(array, axes)
    for axis, distances in plan:
        flat = scatter_sum(flat, axis, distances)
    for axis, distances in reversed(plan):
        flat = gather_back(flat, axis, distances)
    return flat.reshape(array.shape)


def chosen_pairs(listed_key_tiles, listed_tile_count, query_tiles, key_tiles):
    total_tiles = listed_key_tiles.shape[0]
    clipped = jnp.clip(query_tiles, 0, total_tiles - 1)
    one_hot = (clipped[:, None] == jnp.arange(total_tiles, dtype=jnp.int32)[None, :]).astype(
        jnp.int32
    )
    key_lists = jnp.sum(one_hot[:, :, None] * listed_key_tiles[None, :, :], axis=1)
    counts = jnp.sum(one_hot * listed_tile_count[None, :], axis=1)
    slot_ids = jnp.arange(listed_key_tiles.shape[1], dtype=jnp.int32)
    matched = (key_lists == key_tiles[:, None]) & (slot_ids[None, :] < counts[:, None])
    inside = (query_tiles >= 0) & (query_tiles < total_tiles)
    return jnp.any(matched, axis=1) & inside


def nt_dot(a, b):
    return lax.dot_general(a, b, (((1,), (1,)), ((), ())), preferred_element_type=jnp.float32)


def tn_dot(a, b):
    return lax.dot_general(a, b, (((0,), (0,)), ((), ())), preferred_element_type=jnp.float32)


def nn_dot(a, b):
    return lax.dot_general(a, b, (((1,), (0,)), ((), ())), preferred_element_type=jnp.float32)


def tile_pass(bias_ref, first, tile_query, tile_grad, keys, values):
    score_scale = HEAD_SIZE ** (-0.5)
    scores = [
        score_scale * nt_dot(tile_query, k) + bias_ref[first + i] for i, k in enumerate(keys)
    ]
    row_max = jnp.max(scores[0], axis=-1, keepdims=True)
    for s in scores[1:]:
        row_max = jnp.maximum(row_max, jnp.max(s, axis=-1, keepdims=True))
    total = sum(jnp.sum(jnp.exp(s - row_max), axis=-1, keepdims=True) for s in scores)
    log_total = row_max + jnp.log(total)
    weights = [jnp.exp(s - log_total).astype(jnp.bfloat16) for s in scores]
    grad_weights = [nt_dot(tile_grad, v) for v in values]
    row_dot = sum(
        jnp.sum(w.astype(jnp.float32) * g, axis=-1, keepdims=True)
        for w, g in zip(weights, grad_weights)
    )
    grad_scores = [
        (w.astype(jnp.float32) * (g - row_dot)).astype(jnp.bfloat16)
        for w, g in zip(weights, grad_weights)
    ]
    query_term = score_scale * sum(nn_dot(d, k) for d, k in zip(grad_scores, keys))
    key_terms = [score_scale * tn_dot(d, tile_query) for d in grad_scores]
    value_terms = [tn_dot(w, tile_grad) for w in weights]
    return query_term, key_terms, value_terms


def attention_kernel(
    bias_ref, q_ref, g_ref, k_ref, v_ref, kl_ref, vl_ref, kr_ref, vr_ref,
    dq_ref, dk_ref, dv_ref, dkl_ref, dvl_ref, dkr_ref, dvr_ref,
):
    q_a, q_b = q_ref[0, :TILE], q_ref[0, TILE:]
    g_a, g_b = g_ref[0, :TILE], g_ref[0, TILE:]
    k_a, k_b = k_ref[0, :TILE], k_ref[0, TILE:]
    v_a, v_b = v_ref[0, :TILE], v_ref[0, TILE:]
    k_l, v_l, k_r, v_r = kl_ref[0, 0], vl_ref[0, 0], kr_ref[0, 0], vr_ref[0, 0]
    dq_a, dk_a3, dv_a3 = tile_pass(bias_ref, 0, q_a, g_a, (k_l, k_a, k_b), (v_l, v_a, v_b))
    dq_b, dk_b3, dv_b3 = tile_pass(bias_ref, 3, q_b, g_b, (k_a, k_b, k_r), (v_a, v_b, v_r))
    dq_ref[0, :TILE] = dq_a.astype(jnp.bfloat16)
    dq_ref[0, TILE:] = dq_b.astype(jnp.bfloat16)
    dk_ref[0, :TILE] = (dk_a3[1] + dk_b3[0]).astype(jnp.bfloat16)
    dk_ref[0, TILE:] = (dk_a3[2] + dk_b3[1]).astype(jnp.bfloat16)
    dv_ref[0, :TILE] = (dv_a3[1] + dv_b3[0]).astype(jnp.bfloat16)
    dv_ref[0, TILE:] = (dv_a3[2] + dv_b3[1]).astype(jnp.bfloat16)
    dkl_ref[0] = dk_a3[0].astype(jnp.bfloat16)
    dvl_ref[0] = dv_a3[0].astype(jnp.bfloat16)
    dkr_ref[0] = dk_b3[2].astype(jnp.bfloat16)
    dvr_ref[0] = dv_b3[2].astype(jnp.bfloat16)


def attention_backward(bias, chunk, heads, queries, output_gradient, key_matrix, values, halo):
    clip_count, block_len, _ = queries.shape
    whole = pl.BlockSpec((1, block_len, HEAD_SIZE), lambda c, h: (c, 0, h + chunk * heads))
    rims = [pl.BlockSpec((1, 1, TILE, HEAD_SIZE), lambda c, h, i=i: (i, c, 0, h)) for i in range(4)]
    out_whole = pl.BlockSpec((1, block_len, HEAD_SIZE), lambda c, h: (c, 0, h))
    out_rim = pl.BlockSpec((1, TILE, HEAD_SIZE), lambda c, h: (c, 0, h))
    whole_shape = jax.ShapeDtypeStruct((clip_count, block_len, heads * HEAD_SIZE), jnp.bfloat16)
    rim_shape = jax.ShapeDtypeStruct((clip_count, TILE, heads * HEAD_SIZE), jnp.bfloat16)
    return pl.pallas_call(
        attention_kernel,
        grid=(clip_count, heads),
        in_specs=[pl.BlockSpec(memory_space=pltpu.MemorySpace.SMEM)] + [whole] * 4 + rims,
        out_specs=[out_whole] * 3 + [out_rim] * 4,
        out_shape=[whole_shape] * 3 + [rim_shape] * 4,
    )(bias, queries, output_gradient, key_matrix, values, halo, halo, halo, halo)


def on_device(
    queries,
    key_matrix,
    values,
    output_gradient,
    normed,
    adapter_down_weight,
    adapter_up_weight,
    listed_key_tiles,
    listed_tile_count,
):
    block_len = queries.shape[1]
    position = lax.axis_index("seq")
    first_tile = position * TILES_DEV

    down_piece = jnp.einsum(
        "pqg,gv->pqv", normed, adapter_down_weight, preferred_element_type=jnp.float32
    )
    lowered_rows = butterfly_sum(down_piece, "head").astype(jnp.bfloat16)

    tile_a, tile_b = first_tile, first_tile + 1
    allowed = chosen_pairs(
        listed_key_tiles,
        listed_tile_count,
        jnp.stack([tile_a, tile_a, tile_a, tile_b, tile_b, tile_b]).astype(jnp.int32),
        jnp.stack([tile_a - 1, tile_a, tile_b, tile_a, tile_b, tile_b + 1]).astype(jnp.int32),
    )
    bias = jnp.where(allowed, 0.0, masked_score).astype(jnp.float32)

    low_left = shifted(lowered_rows[:, block_len - TILE:], "seq", 1)
    low_right = shifted(lowered_rows[:, :TILE], "seq", -1)

    left_kv = shifted(
        jnp.stack((key_matrix[:, block_len - TILE:], values[:, block_len - TILE:])), "seq", 1
    )
    right_kv = shifted(jnp.stack((key_matrix[:, :TILE], values[:, :TILE])), "seq", -1)
    halo = jnp.concatenate((left_kv, right_kv), 0)
    query_grad, dk_own, dv_own, dk_l, dv_l, dk_r, dv_r = attention_backward(
        bias, 0, queries.shape[2] // HEAD_SIZE, queries, output_gradient, key_matrix, values, halo
    )

    def project(term):
        return jnp.einsum(
            "dsi,ji->dsj", term, adapter_up_weight, preferred_element_type=jnp.float32
        )

    proj_from_right = shifted(project(dv_l), "seq", -1)
    proj_from_left = shifted(project(dv_r), "seq", 1)
    backward_piece = project(dv_own) + jnp.concatenate((proj_from_left, proj_from_right), 1)
    backward_rows = butterfly_sum(backward_piece, "head").astype(jnp.bfloat16)
    gradient_down_local = adapter_scale * jnp.einsum(
        "yhm,yhz->mz", normed, backward_rows, preferred_element_type=jnp.float32
    )
    up_terms = (
        jnp.einsum("igb,igu->bu", lowered_rows, dv_own, preferred_element_type=jnp.float32)
        + jnp.einsum("igb,igu->bu", low_left, dv_l, preferred_element_type=jnp.float32)
        + jnp.einsum("igb,igu->bu", low_right, dv_r, preferred_element_type=jnp.float32)
    )
    gradient_up_local = adapter_scale * up_terms

    from_right = shifted(jnp.stack((dk_l, dv_l), 0), "seq", -1)
    from_left = shifted(jnp.stack((dk_r, dv_r), 0), "seq", 1)
    both = jnp.stack((gradient_down_local, gradient_up_local.T), 0)
    both, from_left, from_right = lax.optimization_barrier((both, from_left, from_right))
    arrived = jnp.concatenate((from_left, from_right), 2).astype(jnp.float32)
    key_grad = (dk_own.astype(jnp.float32) + arrived[0]).astype(jnp.bfloat16)
    value_gradient = (dv_own.astype(jnp.float32) + arrived[1]).astype(jnp.bfloat16)

    both = all_sum(both, ("rep", "seq"))
    down_projection_grad, up_projection_grad = both[0], both[1].T
    return (query_grad, key_grad, value_gradient, down_projection_grad, up_projection_grad)


def solution(mesh):
    in_specs = (
        P(("groups", "rep"), "seq", "head"),
        P(("groups", "rep"), "seq", "head"),
        P(("groups", "rep"), "seq", "head"),
        P(("groups", "rep"), "seq", "head"),
        P(("groups", "rep"), "seq", "head"),
        P("head", None),
        P(None, "head"),
        P("groups", None),
        P("groups"),
    )
    out_specs = (
        P(("groups", "rep"), "seq", "head"),
        P(("groups", "rep"), "seq", "head"),
        P(("groups", "rep"), "seq", "head"),
        P(("groups", "head"), None),
        P("groups", "head"),
    )
    return jax.shard_map(
        on_device, mesh=mesh, in_specs=in_specs, out_specs=out_specs, check_vma=False
    )
```

```python
import jax
import jax.numpy as jnp
from jax import lax
from jax.sharding import PartitionSpec as P
from jax.experimental import pallas as pl
from jax.experimental.pallas import tpu as pltpu

TILE = 384
TILES_DEV = 2
REACH = 1
HEAD_SIZE = 128


adapter_scale = 0.0078125
masked_score = -1e30


def shifted(shard, axis, by):
    peers = lax.axis_size(axis)
    pairs = [(i, i + by) for i in range(peers) if 0 <= i + by < peers]
    return lax.ppermute(shard, axis, pairs)


def butterfly_sum(tree, axis):
    peers = lax.axis_size(axis)
    if peers & (peers - 1):
        return lax.psum(tree, axis)
    step = 1
    while step < peers:
        pairs = [(i, i ^ step) for i in range(peers)]
        other = lax.ppermute(tree, axis, pairs)
        tree = jax.tree.map(lambda a, b: a + b, tree, other)
        step *= 2
    return tree


def scatter_sum(flat, axis, distances):
    peers = lax.axis_size(axis)
    index = lax.axis_index(axis)
    for step in distances:
        half = flat.shape[0] // 2
        upper = (index & step) != 0
        keep = jnp.where(upper, flat[half:], flat[:half])
        send = jnp.where(upper, flat[:half], flat[half:])
        flat = keep + lax.ppermute(send, axis, [(i, i ^ step) for i in range(peers)])
    return flat


def gather_back(flat, axis, distances):
    peers = lax.axis_size(axis)
    index = lax.axis_index(axis)
    for step in reversed(distances):
        other = lax.ppermute(flat, axis, [(i, i ^ step) for i in range(peers)])
        upper = (index & step) != 0
        flat = jnp.where(upper, jnp.concatenate((other, flat)), jnp.concatenate((flat, other)))
    return flat


def all_sum(array, axes):
    plan = []
    for axis in axes:
        peers = lax.axis_size(axis)
        if peers & (peers - 1):
            return lax.psum(array, axes)
        plan.append((axis, [1 << k for k in range(peers.bit_length() - 1)]))
    pieces = 1
    for _, distances in plan:
        pieces *= 1 << len(distances)
    flat = array.reshape(-1)
    if flat.shape[0] % pieces:
        return lax.psum(array, axes)
    for axis, distances in plan:
        flat = scatter_sum(flat, axis, distances)
    for axis, distances in reversed(plan):
        flat = gather_back(flat, axis, distances)
    return flat.reshape(array.shape)


def chosen_pairs(listed_key_tiles, listed_tile_count, query_tiles, key_tiles):
    total_tiles = listed_key_tiles.shape[0]
    clipped = jnp.clip(query_tiles, 0, total_tiles - 1)
    one_hot = (clipped[:, None] == jnp.arange(total_tiles, dtype=jnp.int32)[None, :]).astype(
        jnp.int32
    )
    key_lists = jnp.sum(one_hot[:, :, None] * listed_key_tiles[None, :, :], axis=1)
    counts = jnp.sum(one_hot * listed_tile_count[None, :], axis=1)
    slot_ids = jnp.arange(listed_key_tiles.shape[1], dtype=jnp.int32)
    matched = (key_lists == key_tiles[:, None]) & (slot_ids[None, :] < counts[:, None])
    inside = (query_tiles >= 0) & (query_tiles < total_tiles)
    return jnp.any(matched, axis=1) & inside


def nt_dot(a, b):
    return lax.dot_general(a, b, (((1,), (1,)), ((), ())), preferred_element_type=jnp.float32)


def tn_dot(a, b):
    return lax.dot_general(a, b, (((0,), (0,)), ((), ())), preferred_element_type=jnp.float32)


def nn_dot(a, b):
    return lax.dot_general(a, b, (((1,), (0,)), ((), ())), preferred_element_type=jnp.float32)


def tile_pass(bias_ref, first, tile_query, tile_grad, keys, values):
    score_scale = HEAD_SIZE ** (-0.5)
    scores = [
        score_scale * nt_dot(tile_query, k) + bias_ref[first + i] for i, k in enumerate(keys)
    ]
    row_max = jnp.max(scores[0], axis=-1, keepdims=True)
    for s in scores[1:]:
        row_max = jnp.maximum(row_max, jnp.max(s, axis=-1, keepdims=True))
    total = sum(jnp.sum(jnp.exp(s - row_max), axis=-1, keepdims=True) for s in scores)
    log_total = row_max + jnp.log(total)
    weights = [jnp.exp(s - log_total).astype(jnp.bfloat16) for s in scores]
    grad_weights = [nt_dot(tile_grad, v) for v in values]
    row_dot = sum(
        jnp.sum(w.astype(jnp.float32) * g, axis=-1, keepdims=True)
        for w, g in zip(weights, grad_weights)
    )
    grad_scores = [
        (w.astype(jnp.float32) * (g - row_dot)).astype(jnp.bfloat16)
        for w, g in zip(weights, grad_weights)
    ]
    query_term = score_scale * sum(nn_dot(d, k) for d, k in zip(grad_scores, keys))
    key_terms = [score_scale * tn_dot(d, tile_query) for d in grad_scores]
    value_terms = [tn_dot(w, tile_grad) for w in weights]
    return query_term, key_terms, value_terms


def attention_kernel(
    bias_ref, q_ref, g_ref, k_ref, v_ref, left_ref, right_ref,
    dq_ref, dk_ref, dv_ref, to_left_ref, to_right_ref,
):
    q_a, q_b = q_ref[0, :TILE], q_ref[0, TILE:]
    g_a, g_b = g_ref[0, :TILE], g_ref[0, TILE:]
    k_a, k_b = k_ref[0, :TILE], k_ref[0, TILE:]
    v_a, v_b = v_ref[0, :TILE], v_ref[0, TILE:]
    k_l, v_l, k_r, v_r = left_ref[0, 0], left_ref[1, 0], right_ref[0, 0], right_ref[1, 0]
    dq_a, dk_a3, dv_a3 = tile_pass(bias_ref, 0, q_a, g_a, (k_l, k_a, k_b), (v_l, v_a, v_b))
    dq_b, dk_b3, dv_b3 = tile_pass(bias_ref, 3, q_b, g_b, (k_a, k_b, k_r), (v_a, v_b, v_r))
    dq_ref[0, :TILE] = dq_a.astype(jnp.bfloat16)
    dq_ref[0, TILE:] = dq_b.astype(jnp.bfloat16)
    dk_ref[0, :TILE] = (dk_a3[1] + dk_b3[0]).astype(jnp.bfloat16)
    dk_ref[0, TILE:] = (dk_a3[2] + dk_b3[1]).astype(jnp.bfloat16)
    dv_ref[0, :TILE] = (dv_a3[1] + dv_b3[0]).astype(jnp.bfloat16)
    dv_ref[0, TILE:] = (dv_a3[2] + dv_b3[1]).astype(jnp.bfloat16)
    to_left_ref[0, 0] = dk_a3[0].astype(jnp.bfloat16)
    to_left_ref[1, 0] = dv_a3[0].astype(jnp.bfloat16)
    to_right_ref[0, 0] = dk_b3[2].astype(jnp.bfloat16)
    to_right_ref[1, 0] = dv_b3[2].astype(jnp.bfloat16)


def attention_backward(bias, chunk, heads, queries, output_gradient, key_matrix, values, left, right):
    clip_count, block_len, _ = queries.shape
    whole = pl.BlockSpec((1, block_len, HEAD_SIZE), lambda c, h: (c, 0, h + chunk * heads))
    rim = pl.BlockSpec((2, 1, TILE, HEAD_SIZE), lambda c, h: (0, c, 0, h))
    out_whole = pl.BlockSpec((1, block_len, HEAD_SIZE), lambda c, h: (c, 0, h))
    whole_shape = jax.ShapeDtypeStruct((clip_count, block_len, heads * HEAD_SIZE), jnp.bfloat16)
    rim_shape = jax.ShapeDtypeStruct((2, clip_count, TILE, heads * HEAD_SIZE), jnp.bfloat16)
    return pl.pallas_call(
        attention_kernel,
        grid=(clip_count, heads),
        in_specs=[pl.BlockSpec(memory_space=pltpu.MemorySpace.SMEM)] + [whole] * 4 + [rim] * 2,
        out_specs=[out_whole] * 3 + [rim] * 2,
        out_shape=[whole_shape] * 3 + [rim_shape] * 2,
    )(bias, queries, output_gradient, key_matrix, values, left, right)


def on_device(
    queries,
    key_matrix,
    values,
    output_gradient,
    normed,
    adapter_down_weight,
    adapter_up_weight,
    listed_key_tiles,
    listed_tile_count,
):
    block_len = queries.shape[1]
    position = lax.axis_index("seq")
    first_tile = position * TILES_DEV

    down_piece = jnp.einsum(
        "pqg,gv->pqv", normed, adapter_down_weight, preferred_element_type=jnp.float32
    )
    lowered_rows = butterfly_sum(down_piece, "head").astype(jnp.bfloat16)

    tile_a, tile_b = first_tile, first_tile + 1
    allowed = chosen_pairs(
        listed_key_tiles,
        listed_tile_count,
        jnp.stack([tile_a, tile_a, tile_a, tile_b, tile_b, tile_b]).astype(jnp.int32),
        jnp.stack([tile_a - 1, tile_a, tile_b, tile_a, tile_b, tile_b + 1]).astype(jnp.int32),
    )
    bias = jnp.where(allowed, 0.0, masked_score).astype(jnp.float32)

    local_heads = queries.shape[2] // HEAD_SIZE
    chunks = 1
    per_chunk = local_heads // chunks
    outs = []
    for chunk in range(chunks):
        cols = slice(chunk * per_chunk * HEAD_SIZE, (chunk + 1) * per_chunk * HEAD_SIZE)
        left_kv = shifted(
            jnp.stack((key_matrix[:, block_len - TILE:, cols], values[:, block_len - TILE:, cols])),
            "seq",
            1,
        )
        right_kv = shifted(
            jnp.stack((key_matrix[:, :TILE, cols], values[:, :TILE, cols]), 0), "seq", -1
        )
        dq, dk_own, dv_own, to_left, to_right = attention_backward(
            bias, chunk, per_chunk, queries, output_gradient, key_matrix, values, left_kv, right_kv
        )
        from_right = shifted(to_left, "seq", -1)
        from_left = shifted(to_right, "seq", 1)
        arrived = jnp.concatenate((from_left, from_right), 2).astype(jnp.float32)
        dk = (dk_own.astype(jnp.float32) + arrived[0]).astype(jnp.bfloat16)
        dv = (dv_own.astype(jnp.float32) + arrived[1]).astype(jnp.bfloat16)
        outs.append((dq, dk, dv))
    query_grad, key_grad, value_gradient = (
        jnp.concatenate([o[i] for o in outs], 2) for i in range(3)
    )

    backward_piece = jnp.einsum(
        "dsi,ji->dsj", value_gradient, adapter_up_weight, preferred_element_type=jnp.float32
    )
    backward_rows = butterfly_sum(backward_piece, "head").astype(jnp.bfloat16)
    gradient_down_local = adapter_scale * jnp.einsum(
        "yhm,yhz->mz", normed, backward_rows, preferred_element_type=jnp.float32
    )
    gradient_up_local = adapter_scale * jnp.einsum(
        "igb,igu->bu", lowered_rows, value_gradient, preferred_element_type=jnp.float32
    )
    both = jnp.stack((gradient_down_local, gradient_up_local.T), 0)
    both = all_sum(both, ("rep", "seq"))
    down_projection_grad, up_projection_grad = both[0], both[1].T
    return (query_grad, key_grad, value_gradient, down_projection_grad, up_projection_grad)


def solution(mesh):
    in_specs = (
        P(("groups", "rep"), "seq", "head"),
        P(("groups", "rep"), "seq", "head"),
        P(("groups", "rep"), "seq", "head"),
        P(("groups", "rep"), "seq", "head"),
        P(("groups", "rep"), "seq", "head"),
        P("head", None),
        P(None, "head"),
        P("groups", None),
        P("groups"),
    )
    out_specs = (
        P(("groups", "rep"), "seq", "head"),
        P(("groups", "rep"), "seq", "head"),
        P(("groups", "rep"), "seq", "head"),
        P(("groups", "head"), None),
        P("groups", "head"),
    )
    return jax.shard_map(
        on_device, mesh=mesh, in_specs=in_specs, out_specs=out_specs, check_vma=False
    )
```

```python
import jax
import jax.numpy as jnp
from jax import lax
from jax.sharding import PartitionSpec as P
from jax.experimental import pallas as pl
from jax.experimental.pallas import tpu as pltpu

TILE = 384
TILES_DEV = 2
REACH = 1
HEAD_SIZE = 128


adapter_scale = 0.0078125
masked_score = -1e30


def shifted(shard, axis, by):
    peers = lax.axis_size(axis)
    pairs = [(i, i + by) for i in range(peers) if 0 <= i + by < peers]
    return lax.ppermute(shard, axis, pairs)


def butterfly_sum(tree, axis):
    peers = lax.axis_size(axis)
    if peers & (peers - 1):
        return lax.psum(tree, axis)
    step = 1
    while step < peers:
        pairs = [(i, i ^ step) for i in range(peers)]
        other = lax.ppermute(tree, axis, pairs)
        tree = jax.tree.map(lambda a, b: a + b, tree, other)
        step *= 2
    return tree


def scatter_sum(flat, axis, distances):
    peers = lax.axis_size(axis)
    index = lax.axis_index(axis)
    for step in distances:
        half = flat.shape[0] // 2
        upper = (index & step) != 0
        keep = jnp.where(upper, flat[half:], flat[:half])
        send = jnp.where(upper, flat[:half], flat[half:])
        flat = keep + lax.ppermute(send, axis, [(i, i ^ step) for i in range(peers)])
    return flat


def gather_back(flat, axis, distances):
    peers = lax.axis_size(axis)
    index = lax.axis_index(axis)
    for step in reversed(distances):
        other = lax.ppermute(flat, axis, [(i, i ^ step) for i in range(peers)])
        upper = (index & step) != 0
        flat = jnp.where(upper, jnp.concatenate((other, flat)), jnp.concatenate((flat, other)))
    return flat


def all_sum(array, axes):
    plan = []
    for axis in axes:
        peers = lax.axis_size(axis)
        if peers & (peers - 1):
            return lax.psum(array, axes)
        plan.append((axis, [1 << k for k in range(peers.bit_length() - 1)]))
    pieces = 1
    for _, distances in plan:
        pieces *= 1 << len(distances)
    flat = array.reshape(-1)
    if flat.shape[0] % pieces:
        return lax.psum(array, axes)
    for axis, distances in plan:
        flat = scatter_sum(flat, axis, distances)
    for axis, distances in reversed(plan):
        flat = gather_back(flat, axis, distances)
    return flat.reshape(array.shape)


def chosen_pairs(listed_key_tiles, listed_tile_count, query_tiles, key_tiles):
    total_tiles = listed_key_tiles.shape[0]
    clipped = jnp.clip(query_tiles, 0, total_tiles - 1)
    one_hot = (clipped[:, None] == jnp.arange(total_tiles, dtype=jnp.int32)[None, :]).astype(
        jnp.int32
    )
    key_lists = jnp.sum(one_hot[:, :, None] * listed_key_tiles[None, :, :], axis=1)
    counts = jnp.sum(one_hot * listed_tile_count[None, :], axis=1)
    slot_ids = jnp.arange(listed_key_tiles.shape[1], dtype=jnp.int32)
    matched = (key_lists == key_tiles[:, None]) & (slot_ids[None, :] < counts[:, None])
    inside = (query_tiles >= 0) & (query_tiles < total_tiles)
    return jnp.any(matched, axis=1) & inside


def nt_dot(a, b):
    return lax.dot_general(a, b, (((1,), (1,)), ((), ())), preferred_element_type=jnp.float32)


def tn_dot(a, b):
    return lax.dot_general(a, b, (((0,), (0,)), ((), ())), preferred_element_type=jnp.float32)


def nn_dot(a, b):
    return lax.dot_general(a, b, (((1,), (0,)), ((), ())), preferred_element_type=jnp.float32)


def tile_pass(bias_ref, first, tile_query, tile_grad, keys, values):
    score_scale = HEAD_SIZE ** (-0.5)
    scores = [
        score_scale * nt_dot(tile_query, k) + bias_ref[first + i] for i, k in enumerate(keys)
    ]
    row_max = jnp.max(scores[0], axis=-1, keepdims=True)
    for s in scores[1:]:
        row_max = jnp.maximum(row_max, jnp.max(s, axis=-1, keepdims=True))
    total = sum(jnp.sum(jnp.exp(s - row_max), axis=-1, keepdims=True) for s in scores)
    log_total = row_max + jnp.log(total)
    weights = [jnp.exp(s - log_total).astype(jnp.bfloat16) for s in scores]
    grad_weights = [nt_dot(tile_grad, v) for v in values]
    row_dot = sum(
        jnp.sum(w.astype(jnp.float32) * g, axis=-1, keepdims=True)
        for w, g in zip(weights, grad_weights)
    )
    grad_scores = [
        (w.astype(jnp.float32) * (g - row_dot)).astype(jnp.bfloat16)
        for w, g in zip(weights, grad_weights)
    ]
    query_term = score_scale * sum(nn_dot(d, k) for d, k in zip(grad_scores, keys))
    key_terms = [score_scale * tn_dot(d, tile_query) for d in grad_scores]
    value_terms = [tn_dot(w, tile_grad) for w in weights]
    return query_term, key_terms, value_terms


def attention_kernel(
    bias_ref, q_ref, g_ref, k_ref, v_ref, left_ref, right_ref,
    dq_ref, dk_ref, dv_ref, to_left_ref, to_right_ref,
):
    q_a, q_b = q_ref[0, :TILE], q_ref[0, TILE:]
    g_a, g_b = g_ref[0, :TILE], g_ref[0, TILE:]
    k_a, k_b = k_ref[0, :TILE], k_ref[0, TILE:]
    v_a, v_b = v_ref[0, :TILE], v_ref[0, TILE:]
    k_l, v_l, k_r, v_r = left_ref[0, 0], left_ref[1, 0], right_ref[0, 0], right_ref[1, 0]
    dq_a, dk_a3, dv_a3 = tile_pass(bias_ref, 0, q_a, g_a, (k_l, k_a, k_b), (v_l, v_a, v_b))
    dq_b, dk_b3, dv_b3 = tile_pass(bias_ref, 3, q_b, g_b, (k_a, k_b, k_r), (v_a, v_b, v_r))
    dq_ref[0, :TILE] = dq_a.astype(jnp.bfloat16)
    dq_ref[0, TILE:] = dq_b.astype(jnp.bfloat16)
    dk_ref[0, :TILE] = (dk_a3[1] + dk_b3[0]).astype(jnp.bfloat16)
    dk_ref[0, TILE:] = (dk_a3[2] + dk_b3[1]).astype(jnp.bfloat16)
    dv_ref[0, :TILE] = (dv_a3[1] + dv_b3[0]).astype(jnp.bfloat16)
    dv_ref[0, TILE:] = (dv_a3[2] + dv_b3[1]).astype(jnp.bfloat16)
    to_left_ref[0, 0] = dk_a3[0].astype(jnp.bfloat16)
    to_left_ref[1, 0] = dv_a3[0].astype(jnp.bfloat16)
    to_right_ref[0, 0] = dk_b3[2].astype(jnp.bfloat16)
    to_right_ref[1, 0] = dv_b3[2].astype(jnp.bfloat16)


def attention_backward(bias, chunk, heads, queries, output_gradient, key_matrix, values, left, right):
    clip_count, block_len, _ = queries.shape
    whole = pl.BlockSpec((1, block_len, HEAD_SIZE), lambda c, h: (c, 0, h + chunk * heads))
    rim = pl.BlockSpec((2, 1, TILE, HEAD_SIZE), lambda c, h: (0, c, 0, h))
    out_whole = pl.BlockSpec((1, block_len, HEAD_SIZE), lambda c, h: (c, 0, h))
    whole_shape = jax.ShapeDtypeStruct((clip_count, block_len, heads * HEAD_SIZE), jnp.bfloat16)
    rim_shape = jax.ShapeDtypeStruct((2, clip_count, TILE, heads * HEAD_SIZE), jnp.bfloat16)
    return pl.pallas_call(
        attention_kernel,
        grid=(clip_count, heads),
        in_specs=[pl.BlockSpec(memory_space=pltpu.MemorySpace.SMEM)] + [whole] * 4 + [rim] * 2,
        out_specs=[out_whole] * 3 + [rim] * 2,
        out_shape=[whole_shape] * 3 + [rim_shape] * 2,
    )(bias, queries, output_gradient, key_matrix, values, left, right)


def on_device(
    queries,
    key_matrix,
    values,
    output_gradient,
    normed,
    adapter_down_weight,
    adapter_up_weight,
    listed_key_tiles,
    listed_tile_count,
):
    block_len = queries.shape[1]
    position = lax.axis_index("seq")
    first_tile = position * TILES_DEV

    down_piece = jnp.einsum(
        "pqg,gv->pqv", normed, adapter_down_weight, preferred_element_type=jnp.float32
    )
    lowered_rows = butterfly_sum(down_piece, "head").astype(jnp.bfloat16)

    tile_a, tile_b = first_tile, first_tile + 1
    allowed = chosen_pairs(
        listed_key_tiles,
        listed_tile_count,
        jnp.stack([tile_a, tile_a, tile_a, tile_b, tile_b, tile_b]).astype(jnp.int32),
        jnp.stack([tile_a - 1, tile_a, tile_b, tile_a, tile_b, tile_b + 1]).astype(jnp.int32),
    )
    bias = jnp.where(allowed, 0.0, masked_score).astype(jnp.float32)

    local_heads = queries.shape[2] // HEAD_SIZE
    chunks = 2 if local_heads % 2 == 0 else 1
    per_chunk = local_heads // chunks
    outs = []
    for chunk in range(chunks):
        cols = slice(chunk * per_chunk * HEAD_SIZE, (chunk + 1) * per_chunk * HEAD_SIZE)
        left_kv = shifted(
            jnp.stack((key_matrix[:, block_len - TILE:, cols], values[:, block_len - TILE:, cols])),
            "seq",
            1,
        )
        right_kv = shifted(
            jnp.stack((key_matrix[:, :TILE, cols], values[:, :TILE, cols]), 0), "seq", -1
        )
        dq, dk_own, dv_own, to_left, to_right = attention_backward(
            bias, chunk, per_chunk, queries, output_gradient, key_matrix, values, left_kv, right_kv
        )
        from_right = shifted(to_left, "seq", -1)
        from_left = shifted(to_right, "seq", 1)
        arrived = jnp.concatenate((from_left, from_right), 2).astype(jnp.float32)
        dk = (dk_own.astype(jnp.float32) + arrived[0]).astype(jnp.bfloat16)
        dv = (dv_own.astype(jnp.float32) + arrived[1]).astype(jnp.bfloat16)
        outs.append((dq, dk, dv))
    query_grad, key_grad, value_gradient = (
        jnp.concatenate([o[i] for o in outs], 2) for i in range(3)
    )

    backward_piece = jnp.einsum(
        "dsi,ji->dsj", value_gradient, adapter_up_weight, preferred_element_type=jnp.float32
    )
    backward_rows = butterfly_sum(backward_piece, "head").astype(jnp.bfloat16)
    gradient_down_local = adapter_scale * jnp.einsum(
        "yhm,yhz->mz", normed, backward_rows, preferred_element_type=jnp.float32
    )
    gradient_up_local = adapter_scale * jnp.einsum(
        "igb,igu->bu", lowered_rows, value_gradient, preferred_element_type=jnp.float32
    )
    both = jnp.stack((gradient_down_local, gradient_up_local.T), 0)
    both = all_sum(both, ("rep", "seq"))
    down_projection_grad, up_projection_grad = both[0], both[1].T
    return (query_grad, key_grad, value_gradient, down_projection_grad, up_projection_grad)


def solution(mesh):
    in_specs = (
        P(("groups", "rep"), "seq", "head"),
        P(("groups", "rep"), "seq", "head"),
        P(("groups", "rep"), "seq", "head"),
        P(("groups", "rep"), "seq", "head"),
        P(("groups", "rep"), "seq", "head"),
        P("head", None),
        P(None, "head"),
        P("groups", None),
        P("groups"),
    )
    out_specs = (
        P(("groups", "rep"), "seq", "head"),
        P(("groups", "rep"), "seq", "head"),
        P(("groups", "rep"), "seq", "head"),
        P(("groups", "head"), None),
        P("groups", "head"),
    )
    return jax.shard_map(
        on_device, mesh=mesh, in_specs=in_specs, out_specs=out_specs, check_vma=False
    )
```

```python
import jax
import jax.numpy as jnp
from jax import lax
from jax.sharding import PartitionSpec as P
from jax.experimental import pallas as pl
from jax.experimental.pallas import tpu as pltpu

TILE = 384
TILES_DEV = 2
REACH = 1
HEAD_SIZE = 128


adapter_scale = 0.0078125
masked_score = -1e30


def shifted(shard, axis, by):
    peers = lax.axis_size(axis)
    pairs = [(i, i + by) for i in range(peers) if 0 <= i + by < peers]
    return lax.ppermute(shard, axis, pairs)


def butterfly_sum(tree, axis):
    peers = lax.axis_size(axis)
    if peers & (peers - 1):
        return lax.psum(tree, axis)
    step = 1
    while step < peers:
        pairs = [(i, i ^ step) for i in range(peers)]
        other = lax.ppermute(tree, axis, pairs)
        tree = jax.tree.map(lambda a, b: a + b, tree, other)
        step *= 2
    return tree


def scatter_sum(flat, axis, distances):
    peers = lax.axis_size(axis)
    index = lax.axis_index(axis)
    for step in distances:
        half = flat.shape[0] // 2
        upper = (index & step) != 0
        keep = jnp.where(upper, flat[half:], flat[:half])
        send = jnp.where(upper, flat[:half], flat[half:])
        flat = keep + lax.ppermute(send, axis, [(i, i ^ step) for i in range(peers)])
    return flat


def gather_back(flat, axis, distances):
    peers = lax.axis_size(axis)
    index = lax.axis_index(axis)
    for step in reversed(distances):
        other = lax.ppermute(flat, axis, [(i, i ^ step) for i in range(peers)])
        upper = (index & step) != 0
        flat = jnp.where(upper, jnp.concatenate((other, flat)), jnp.concatenate((flat, other)))
    return flat


def one_round_sum(flat, axis):
    peers = lax.axis_size(axis)
    index = lax.axis_index(axis)
    pieces = flat.reshape(peers, -1)
    slot = lax.broadcasted_iota(jnp.int32, pieces.shape, 0)

    def piece(at):
        return lax.dynamic_index_in_dim(pieces, at % peers, 0, keepdims=False)

    total = piece(index)
    for step in range(1, peers):
        total = total + lax.ppermute(
            piece(index + step), axis, [(j, j + step) for j in range(peers - step)]
        )
        total = total + lax.ppermute(
            piece(index - step), axis, [(j, j - step) for j in range(step, peers)]
        )
    whole = jnp.where(slot == index, total[None], 0.0)
    for step in range(1, peers):
        up = lax.ppermute(total, axis, [(j, j + step) for j in range(peers - step)])
        down = lax.ppermute(total, axis, [(j, j - step) for j in range(step, peers)])
        whole = whole + jnp.where(slot == index - step, up[None], 0.0)
        whole = whole + jnp.where(slot == index + step, down[None], 0.0)
    return whole.reshape(-1)


def all_sum(array, axes):
    plan = []
    for axis in axes:
        peers = lax.axis_size(axis)
        if peers & (peers - 1):
            return lax.psum(array, axes)
        plan.append((axis, [1 << k for k in range(peers.bit_length() - 1)]))
    pieces = 1
    for _, distances in plan:
        pieces *= 1 << len(distances)
    flat = array.reshape(-1)
    if flat.shape[0] % pieces:
        return lax.psum(array, axes)
    inner, outer = plan[0], plan[1:]
    flat = scatter_sum(flat, inner[0], inner[1])
    for axis, distances in outer:
        if lax.axis_size(axis) <= 4:
            flat = one_round_sum(flat, axis)
        else:
            flat = scatter_sum(flat, axis, distances)
            flat = gather_back(flat, axis, distances)
    flat = gather_back(flat, inner[0], inner[1])
    return flat.reshape(array.shape)


def chosen_pairs(listed_key_tiles, listed_tile_count, query_tiles, key_tiles):
    total_tiles = listed_key_tiles.shape[0]
    clipped = jnp.clip(query_tiles, 0, total_tiles - 1)
    one_hot = (clipped[:, None] == jnp.arange(total_tiles, dtype=jnp.int32)[None, :]).astype(
        jnp.int32
    )
    key_lists = jnp.sum(one_hot[:, :, None] * listed_key_tiles[None, :, :], axis=1)
    counts = jnp.sum(one_hot * listed_tile_count[None, :], axis=1)
    slot_ids = jnp.arange(listed_key_tiles.shape[1], dtype=jnp.int32)
    matched = (key_lists == key_tiles[:, None]) & (slot_ids[None, :] < counts[:, None])
    inside = (query_tiles >= 0) & (query_tiles < total_tiles)
    return jnp.any(matched, axis=1) & inside


def nt_dot(a, b):
    return lax.dot_general(a, b, (((1,), (1,)), ((), ())), preferred_element_type=jnp.float32)


def tn_dot(a, b):
    return lax.dot_general(a, b, (((0,), (0,)), ((), ())), preferred_element_type=jnp.float32)


def nn_dot(a, b):
    return lax.dot_general(a, b, (((1,), (0,)), ((), ())), preferred_element_type=jnp.float32)


def tile_pass(bias_ref, first, tile_query, tile_grad, keys, values):
    score_scale = HEAD_SIZE ** (-0.5)
    scores = [
        score_scale * nt_dot(tile_query, k) + bias_ref[first + i] for i, k in enumerate(keys)
    ]
    row_max = jnp.max(scores[0], axis=-1, keepdims=True)
    for s in scores[1:]:
        row_max = jnp.maximum(row_max, jnp.max(s, axis=-1, keepdims=True))
    total = sum(jnp.sum(jnp.exp(s - row_max), axis=-1, keepdims=True) for s in scores)
    log_total = row_max + jnp.log(total)
    weights = [jnp.exp(s - log_total).astype(jnp.bfloat16) for s in scores]
    grad_weights = [nt_dot(tile_grad, v) for v in values]
    row_dot = sum(
        jnp.sum(w.astype(jnp.float32) * g, axis=-1, keepdims=True)
        for w, g in zip(weights, grad_weights)
    )
    grad_scores = [
        (w.astype(jnp.float32) * (g - row_dot)).astype(jnp.bfloat16)
        for w, g in zip(weights, grad_weights)
    ]
    query_term = score_scale * sum(nn_dot(d, k) for d, k in zip(grad_scores, keys))
    key_terms = [score_scale * tn_dot(d, tile_query) for d in grad_scores]
    value_terms = [tn_dot(w, tile_grad) for w in weights]
    return query_term, key_terms, value_terms


def attention_kernel(
    bias_ref, q_ref, g_ref, k_ref, v_ref, left_ref, right_ref,
    dq_ref, dk_ref, dv_ref, to_left_ref, to_right_ref,
):
    q_a, q_b = q_ref[0, :TILE], q_ref[0, TILE:]
    g_a, g_b = g_ref[0, :TILE], g_ref[0, TILE:]
    k_a, k_b = k_ref[0, :TILE], k_ref[0, TILE:]
    v_a, v_b = v_ref[0, :TILE], v_ref[0, TILE:]
    k_l, v_l, k_r, v_r = left_ref[0, 0], left_ref[1, 0], right_ref[0, 0], right_ref[1, 0]
    dq_a, dk_a3, dv_a3 = tile_pass(bias_ref, 0, q_a, g_a, (k_l, k_a, k_b), (v_l, v_a, v_b))
    dq_b, dk_b3, dv_b3 = tile_pass(bias_ref, 3, q_b, g_b, (k_a, k_b, k_r), (v_a, v_b, v_r))
    dq_ref[0, :TILE] = dq_a.astype(jnp.bfloat16)
    dq_ref[0, TILE:] = dq_b.astype(jnp.bfloat16)
    dk_ref[0, :TILE] = (dk_a3[1] + dk_b3[0]).astype(jnp.bfloat16)
    dk_ref[0, TILE:] = (dk_a3[2] + dk_b3[1]).astype(jnp.bfloat16)
    dv_ref[0, :TILE] = (dv_a3[1] + dv_b3[0]).astype(jnp.bfloat16)
    dv_ref[0, TILE:] = (dv_a3[2] + dv_b3[1]).astype(jnp.bfloat16)
    to_left_ref[0, 0] = dk_a3[0].astype(jnp.bfloat16)
    to_left_ref[1, 0] = dv_a3[0].astype(jnp.bfloat16)
    to_right_ref[0, 0] = dk_b3[2].astype(jnp.bfloat16)
    to_right_ref[1, 0] = dv_b3[2].astype(jnp.bfloat16)


def attention_backward(bias, chunk, heads, queries, output_gradient, key_matrix, values, left, right):
    clip_count, block_len, _ = queries.shape
    whole = pl.BlockSpec((1, block_len, HEAD_SIZE), lambda c, h: (c, 0, h + chunk * heads))
    rim = pl.BlockSpec((2, 1, TILE, HEAD_SIZE), lambda c, h: (0, c, 0, h))
    out_whole = pl.BlockSpec((1, block_len, HEAD_SIZE), lambda c, h: (c, 0, h))
    whole_shape = jax.ShapeDtypeStruct((clip_count, block_len, heads * HEAD_SIZE), jnp.bfloat16)
    rim_shape = jax.ShapeDtypeStruct((2, clip_count, TILE, heads * HEAD_SIZE), jnp.bfloat16)
    return pl.pallas_call(
        attention_kernel,
        grid=(clip_count, heads),
        in_specs=[pl.BlockSpec(memory_space=pltpu.MemorySpace.SMEM)] + [whole] * 4 + [rim] * 2,
        out_specs=[out_whole] * 3 + [rim] * 2,
        out_shape=[whole_shape] * 3 + [rim_shape] * 2,
    )(bias, queries, output_gradient, key_matrix, values, left, right)


def on_device(
    queries,
    key_matrix,
    values,
    output_gradient,
    normed,
    adapter_down_weight,
    adapter_up_weight,
    listed_key_tiles,
    listed_tile_count,
):
    block_len = queries.shape[1]
    position = lax.axis_index("seq")
    first_tile = position * TILES_DEV

    down_piece = jnp.einsum(
        "pqg,gv->pqv", normed, adapter_down_weight, preferred_element_type=jnp.float32
    )
    lowered_rows = butterfly_sum(down_piece, "head").astype(jnp.bfloat16)

    tile_a, tile_b = first_tile, first_tile + 1
    allowed = chosen_pairs(
        listed_key_tiles,
        listed_tile_count,
        jnp.stack([tile_a, tile_a, tile_a, tile_b, tile_b, tile_b]).astype(jnp.int32),
        jnp.stack([tile_a - 1, tile_a, tile_b, tile_a, tile_b, tile_b + 1]).astype(jnp.int32),
    )
    bias = jnp.where(allowed, 0.0, masked_score).astype(jnp.float32)

    local_heads = queries.shape[2] // HEAD_SIZE
    chunks = 2 if local_heads % 2 == 0 else 1
    per_chunk = local_heads // chunks
    outs = []
    for chunk in range(chunks):
        cols = slice(chunk * per_chunk * HEAD_SIZE, (chunk + 1) * per_chunk * HEAD_SIZE)
        left_kv = shifted(
            jnp.stack((key_matrix[:, block_len - TILE:, cols], values[:, block_len - TILE:, cols])),
            "seq",
            1,
        )
        right_kv = shifted(
            jnp.stack((key_matrix[:, :TILE, cols], values[:, :TILE, cols]), 0), "seq", -1
        )
        dq, dk_own, dv_own, to_left, to_right = attention_backward(
            bias, chunk, per_chunk, queries, output_gradient, key_matrix, values, left_kv, right_kv
        )
        from_right = shifted(to_left, "seq", -1)
        from_left = shifted(to_right, "seq", 1)
        arrived = jnp.concatenate((from_left, from_right), 2).astype(jnp.float32)
        dk = (dk_own.astype(jnp.float32) + arrived[0]).astype(jnp.bfloat16)
        dv = (dv_own.astype(jnp.float32) + arrived[1]).astype(jnp.bfloat16)
        outs.append((dq, dk, dv))
    query_grad, key_grad, value_gradient = (
        jnp.concatenate([o[i] for o in outs], 2) for i in range(3)
    )

    backward_piece = jnp.einsum(
        "dsi,ji->dsj", value_gradient, adapter_up_weight, preferred_element_type=jnp.float32
    )
    backward_rows = butterfly_sum(backward_piece, "head").astype(jnp.bfloat16)
    gradient_down_local = adapter_scale * jnp.einsum(
        "yhm,yhz->mz", normed, backward_rows, preferred_element_type=jnp.float32
    )
    gradient_up_local = adapter_scale * jnp.einsum(
        "igb,igu->bu", lowered_rows, value_gradient, preferred_element_type=jnp.float32
    )
    both = jnp.stack((gradient_down_local, gradient_up_local.T), 0)
    both = all_sum(both, ("rep", "seq"))
    down_projection_grad, up_projection_grad = both[0], both[1].T
    return (query_grad, key_grad, value_gradient, down_projection_grad, up_projection_grad)


def solution(mesh):
    in_specs = (
        P(("groups", "rep"), "seq", "head"),
        P(("groups", "rep"), "seq", "head"),
        P(("groups", "rep"), "seq", "head"),
        P(("groups", "rep"), "seq", "head"),
        P(("groups", "rep"), "seq", "head"),
        P("head", None),
        P(None, "head"),
        P("groups", None),
        P("groups"),
    )
    out_specs = (
        P(("groups", "rep"), "seq", "head"),
        P(("groups", "rep"), "seq", "head"),
        P(("groups", "rep"), "seq", "head"),
        P(("groups", "head"), None),
        P("groups", "head"),
    )
    return jax.shard_map(
        on_device, mesh=mesh, in_specs=in_specs, out_specs=out_specs, check_vma=False
    )
```

```python
import jax
import jax.numpy as jnp
from jax import lax
from jax.sharding import PartitionSpec as P
from jax.experimental import pallas as pl
from jax.experimental.pallas import tpu as pltpu

TILE = 384
TILES_DEV = 2
REACH = 1
HEAD_SIZE = 128


adapter_scale = 0.0078125
masked_score = -1e30


def shifted(shard, axis, by):
    peers = lax.axis_size(axis)
    pairs = [(i, i + by) for i in range(peers) if 0 <= i + by < peers]
    return lax.ppermute(shard, axis, pairs)


def butterfly_sum(tree, axis):
    peers = lax.axis_size(axis)
    if peers & (peers - 1):
        return lax.psum(tree, axis)
    step = 1
    while step < peers:
        pairs = [(i, i ^ step) for i in range(peers)]
        other = lax.ppermute(tree, axis, pairs)
        tree = jax.tree.map(lambda a, b: a + b, tree, other)
        step *= 2
    return tree


def scatter_sum(flat, axis, distances):
    peers = lax.axis_size(axis)
    index = lax.axis_index(axis)
    for step in distances:
        half = flat.shape[0] // 2
        upper = (index & step) != 0
        keep = jnp.where(upper, flat[half:], flat[:half])
        send = jnp.where(upper, flat[:half], flat[half:])
        flat = keep + lax.ppermute(send, axis, [(i, i ^ step) for i in range(peers)])
    return flat


def gather_back(flat, axis, distances):
    peers = lax.axis_size(axis)
    index = lax.axis_index(axis)
    for step in reversed(distances):
        other = lax.ppermute(flat, axis, [(i, i ^ step) for i in range(peers)])
        upper = (index & step) != 0
        flat = jnp.where(upper, jnp.concatenate((other, flat)), jnp.concatenate((flat, other)))
    return flat


def all_sum(array, axes):
    plan = []
    for axis in axes:
        peers = lax.axis_size(axis)
        if peers & (peers - 1):
            return lax.psum(array, axes)
        plan.append((axis, [1 << k for k in range(peers.bit_length() - 1)]))
    pieces = 1
    for _, distances in plan:
        pieces *= 1 << len(distances)
    flat = array.reshape(-1)
    if flat.shape[0] % pieces:
        return lax.psum(array, axes)
    inner, outer = plan[0], plan[1:]
    flat = scatter_sum(flat, inner[0], inner[1])
    for axis, distances in outer:
        flat = scatter_sum(flat, axis, distances[:-1])
        if distances:
            step = distances[-1]
            flat = flat + lax.ppermute(
                flat, axis, [(i, i ^ step) for i in range(lax.axis_size(axis))]
            )
        flat = gather_back(flat, axis, distances[:-1])
    flat = gather_back(flat, inner[0], inner[1])
    return flat.reshape(array.shape)


def chosen_pairs(listed_key_tiles, listed_tile_count, query_tiles, key_tiles):
    total_tiles = listed_key_tiles.shape[0]
    clipped = jnp.clip(query_tiles, 0, total_tiles - 1)
    one_hot = (clipped[:, None] == jnp.arange(total_tiles, dtype=jnp.int32)[None, :]).astype(
        jnp.int32
    )
    key_lists = jnp.sum(one_hot[:, :, None] * listed_key_tiles[None, :, :], axis=1)
    counts = jnp.sum(one_hot * listed_tile_count[None, :], axis=1)
    slot_ids = jnp.arange(listed_key_tiles.shape[1], dtype=jnp.int32)
    matched = (key_lists == key_tiles[:, None]) & (slot_ids[None, :] < counts[:, None])
    inside = (query_tiles >= 0) & (query_tiles < total_tiles)
    return jnp.any(matched, axis=1) & inside


def nt_dot(a, b):
    return lax.dot_general(a, b, (((1,), (1,)), ((), ())), preferred_element_type=jnp.float32)


def tn_dot(a, b):
    return lax.dot_general(a, b, (((0,), (0,)), ((), ())), preferred_element_type=jnp.float32)


def nn_dot(a, b):
    return lax.dot_general(a, b, (((1,), (0,)), ((), ())), preferred_element_type=jnp.float32)


def tile_pass(bias_ref, first, tile_query, tile_grad, keys, values):
    score_scale = HEAD_SIZE ** (-0.5)
    scores = [
        score_scale * nt_dot(tile_query, k) + bias_ref[first + i] for i, k in enumerate(keys)
    ]
    row_max = jnp.max(scores[0], axis=-1, keepdims=True)
    for s in scores[1:]:
        row_max = jnp.maximum(row_max, jnp.max(s, axis=-1, keepdims=True))
    total = sum(jnp.sum(jnp.exp(s - row_max), axis=-1, keepdims=True) for s in scores)
    log_total = row_max + jnp.log(total)
    weights = [jnp.exp(s - log_total).astype(jnp.bfloat16) for s in scores]
    grad_weights = [nt_dot(tile_grad, v) for v in values]
    row_dot = sum(
        jnp.sum(w.astype(jnp.float32) * g, axis=-1, keepdims=True)
        for w, g in zip(weights, grad_weights)
    )
    grad_scores = [
        (w.astype(jnp.float32) * (g - row_dot)).astype(jnp.bfloat16)
        for w, g in zip(weights, grad_weights)
    ]
    query_term = score_scale * sum(nn_dot(d, k) for d, k in zip(grad_scores, keys))
    key_terms = [score_scale * tn_dot(d, tile_query) for d in grad_scores]
    value_terms = [tn_dot(w, tile_grad) for w in weights]
    return query_term, key_terms, value_terms


def attention_kernel(
    bias_ref, q_ref, g_ref, k_ref, v_ref, left_ref, right_ref,
    dq_ref, dk_ref, dv_ref, to_left_ref, to_right_ref,
):
    q_a, q_b = q_ref[0, :TILE], q_ref[0, TILE:]
    g_a, g_b = g_ref[0, :TILE], g_ref[0, TILE:]
    k_a, k_b = k_ref[0, :TILE], k_ref[0, TILE:]
    v_a, v_b = v_ref[0, :TILE], v_ref[0, TILE:]
    k_l, v_l, k_r, v_r = left_ref[0, 0], left_ref[1, 0], right_ref[0, 0], right_ref[1, 0]
    dq_a, dk_a3, dv_a3 = tile_pass(bias_ref, 0, q_a, g_a, (k_l, k_a, k_b), (v_l, v_a, v_b))
    dq_b, dk_b3, dv_b3 = tile_pass(bias_ref, 3, q_b, g_b, (k_a, k_b, k_r), (v_a, v_b, v_r))
    dq_ref[0, :TILE] = dq_a.astype(jnp.bfloat16)
    dq_ref[0, TILE:] = dq_b.astype(jnp.bfloat16)
    dk_ref[0, :TILE] = (dk_a3[1] + dk_b3[0]).astype(jnp.bfloat16)
    dk_ref[0, TILE:] = (dk_a3[2] + dk_b3[1]).astype(jnp.bfloat16)
    dv_ref[0, :TILE] = (dv_a3[1] + dv_b3[0]).astype(jnp.bfloat16)
    dv_ref[0, TILE:] = (dv_a3[2] + dv_b3[1]).astype(jnp.bfloat16)
    to_left_ref[0, 0] = dk_a3[0].astype(jnp.bfloat16)
    to_left_ref[1, 0] = dv_a3[0].astype(jnp.bfloat16)
    to_right_ref[0, 0] = dk_b3[2].astype(jnp.bfloat16)
    to_right_ref[1, 0] = dv_b3[2].astype(jnp.bfloat16)


def attention_backward(bias, chunk, heads, queries, output_gradient, key_matrix, values, left, right):
    clip_count, block_len, _ = queries.shape
    whole = pl.BlockSpec((1, block_len, HEAD_SIZE), lambda c, h: (c, 0, h + chunk * heads))
    rim = pl.BlockSpec((2, 1, TILE, HEAD_SIZE), lambda c, h: (0, c, 0, h))
    out_whole = pl.BlockSpec((1, block_len, HEAD_SIZE), lambda c, h: (c, 0, h))
    whole_shape = jax.ShapeDtypeStruct((clip_count, block_len, heads * HEAD_SIZE), jnp.bfloat16)
    rim_shape = jax.ShapeDtypeStruct((2, clip_count, TILE, heads * HEAD_SIZE), jnp.bfloat16)
    return pl.pallas_call(
        attention_kernel,
        grid=(clip_count, heads),
        in_specs=[pl.BlockSpec(memory_space=pltpu.MemorySpace.SMEM)] + [whole] * 4 + [rim] * 2,
        out_specs=[out_whole] * 3 + [rim] * 2,
        out_shape=[whole_shape] * 3 + [rim_shape] * 2,
    )(bias, queries, output_gradient, key_matrix, values, left, right)


def on_device(
    queries,
    key_matrix,
    values,
    output_gradient,
    normed,
    adapter_down_weight,
    adapter_up_weight,
    listed_key_tiles,
    listed_tile_count,
):
    block_len = queries.shape[1]
    position = lax.axis_index("seq")
    first_tile = position * TILES_DEV

    down_piece = jnp.einsum(
        "pqg,gv->pqv", normed, adapter_down_weight, preferred_element_type=jnp.float32
    )
    lowered_rows = butterfly_sum(down_piece, "head").astype(jnp.bfloat16)

    tile_a, tile_b = first_tile, first_tile + 1
    allowed = chosen_pairs(
        listed_key_tiles,
        listed_tile_count,
        jnp.stack([tile_a, tile_a, tile_a, tile_b, tile_b, tile_b]).astype(jnp.int32),
        jnp.stack([tile_a - 1, tile_a, tile_b, tile_a, tile_b, tile_b + 1]).astype(jnp.int32),
    )
    bias = jnp.where(allowed, 0.0, masked_score).astype(jnp.float32)

    local_heads = queries.shape[2] // HEAD_SIZE
    chunks = 2 if local_heads % 2 == 0 else 1
    per_chunk = local_heads // chunks
    outs = []
    for chunk in range(chunks):
        cols = slice(chunk * per_chunk * HEAD_SIZE, (chunk + 1) * per_chunk * HEAD_SIZE)
        left_kv = shifted(
            jnp.stack((key_matrix[:, block_len - TILE:, cols], values[:, block_len - TILE:, cols])),
            "seq",
            1,
        )
        right_kv = shifted(
            jnp.stack((key_matrix[:, :TILE, cols], values[:, :TILE, cols]), 0), "seq", -1
        )
        dq, dk_own, dv_own, to_left, to_right = attention_backward(
            bias, chunk, per_chunk, queries, output_gradient, key_matrix, values, left_kv, right_kv
        )
        from_right = shifted(to_left, "seq", -1)
        from_left = shifted(to_right, "seq", 1)
        arrived = jnp.concatenate((from_left, from_right), 2).astype(jnp.float32)
        dk = (dk_own.astype(jnp.float32) + arrived[0]).astype(jnp.bfloat16)
        dv = (dv_own.astype(jnp.float32) + arrived[1]).astype(jnp.bfloat16)
        piece = jnp.einsum(
            "dsi,ji->dsj", dv, adapter_up_weight[:, cols], preferred_element_type=jnp.float32
        )
        up = jnp.einsum("igb,igu->bu", lowered_rows, dv, preferred_element_type=jnp.float32)
        outs.append((dq, dk, dv, piece, up))
    query_grad, key_grad, value_gradient = (
        jnp.concatenate([o[i] for o in outs], 2) for i in range(3)
    )

    backward_piece = outs[0][3]
    for o in outs[1:]:
        backward_piece = backward_piece + o[3]
    backward_rows = butterfly_sum(backward_piece, "head").astype(jnp.bfloat16)
    gradient_down_local = adapter_scale * jnp.einsum(
        "yhm,yhz->mz", normed, backward_rows, preferred_element_type=jnp.float32
    )
    gradient_up_local = adapter_scale * jnp.concatenate([o[4] for o in outs], 1)
    both = jnp.stack((gradient_down_local, gradient_up_local.T), 0)
    both = all_sum(both, ("rep", "seq"))
    down_projection_grad, up_projection_grad = both[0], both[1].T
    return (query_grad, key_grad, value_gradient, down_projection_grad, up_projection_grad)


def solution(mesh):
    in_specs = (
        P(("groups", "rep"), "seq", "head"),
        P(("groups", "rep"), "seq", "head"),
        P(("groups", "rep"), "seq", "head"),
        P(("groups", "rep"), "seq", "head"),
        P(("groups", "rep"), "seq", "head"),
        P("head", None),
        P(None, "head"),
        P("groups", None),
        P("groups"),
    )
    out_specs = (
        P(("groups", "rep"), "seq", "head"),
        P(("groups", "rep"), "seq", "head"),
        P(("groups", "rep"), "seq", "head"),
        P(("groups", "head"), None),
        P("groups", "head"),
    )
    return jax.shard_map(
        on_device, mesh=mesh, in_specs=in_specs, out_specs=out_specs, check_vma=False
    )
```

```python
import jax
import jax.numpy as jnp
from jax import lax
from jax.sharding import PartitionSpec as P
from jax.experimental import pallas as pl
from jax.experimental.pallas import tpu as pltpu

TILE = 384
TILES_DEV = 2
REACH = 1
HEAD_SIZE = 128


adapter_scale = 0.0078125
masked_score = -1e30


def shifted(shard, axis, by):
    peers = lax.axis_size(axis)
    pairs = [(i, i + by) for i in range(peers) if 0 <= i + by < peers]
    return lax.ppermute(shard, axis, pairs)


def butterfly_sum(tree, axis):
    peers = lax.axis_size(axis)
    if peers & (peers - 1):
        return lax.psum(tree, axis)
    step = 1
    while step < peers:
        pairs = [(i, i ^ step) for i in range(peers)]
        other = lax.ppermute(tree, axis, pairs)
        tree = jax.tree.map(lambda a, b: a + b, tree, other)
        step *= 2
    return tree


def scatter_sum(flat, axis, distances):
    peers = lax.axis_size(axis)
    index = lax.axis_index(axis)
    for step in distances:
        half = flat.shape[0] // 2
        upper = (index & step) != 0
        keep = jnp.where(upper, flat[half:], flat[:half])
        send = jnp.where(upper, flat[:half], flat[half:])
        flat = keep + lax.ppermute(send, axis, [(i, i ^ step) for i in range(peers)])
    return flat


def gather_back(flat, axis, distances):
    peers = lax.axis_size(axis)
    index = lax.axis_index(axis)
    for step in reversed(distances):
        other = lax.ppermute(flat, axis, [(i, i ^ step) for i in range(peers)])
        upper = (index & step) != 0
        flat = jnp.where(upper, jnp.concatenate((other, flat)), jnp.concatenate((flat, other)))
    return flat


def all_sum(array, axes):
    plan = []
    for axis in axes:
        peers = lax.axis_size(axis)
        if peers & (peers - 1):
            return lax.psum(array, axes)
        plan.append((axis, [1 << k for k in range(peers.bit_length() - 1)]))
    pieces = 1
    for _, distances in plan:
        pieces *= 1 << len(distances)
    flat = array.reshape(-1)
    if flat.shape[0] % pieces:
        return lax.psum(array, axes)
    inner, outer = plan[0], plan[1:]
    flat = scatter_sum(flat, inner[0], inner[1])
    for axis, distances in outer:
        flat = scatter_sum(flat, axis, distances[:-1])
        if distances:
            step = distances[-1]
            flat = flat + lax.ppermute(
                flat, axis, [(i, i ^ step) for i in range(lax.axis_size(axis))]
            )
        flat = gather_back(flat, axis, distances[:-1])
    flat = gather_back(flat, inner[0], inner[1])
    return flat.reshape(array.shape)


def chosen_pairs(listed_key_tiles, listed_tile_count, query_tiles, key_tiles):
    total_tiles = listed_key_tiles.shape[0]
    clipped = jnp.clip(query_tiles, 0, total_tiles - 1)
    one_hot = (clipped[:, None] == jnp.arange(total_tiles, dtype=jnp.int32)[None, :]).astype(
        jnp.int32
    )
    key_lists = jnp.sum(one_hot[:, :, None] * listed_key_tiles[None, :, :], axis=1)
    counts = jnp.sum(one_hot * listed_tile_count[None, :], axis=1)
    slot_ids = jnp.arange(listed_key_tiles.shape[1], dtype=jnp.int32)
    matched = (key_lists == key_tiles[:, None]) & (slot_ids[None, :] < counts[:, None])
    inside = (query_tiles >= 0) & (query_tiles < total_tiles)
    return jnp.any(matched, axis=1) & inside


def nt_dot(a, b):
    return lax.dot_general(a, b, (((1,), (1,)), ((), ())), preferred_element_type=jnp.float32)


def tn_dot(a, b):
    return lax.dot_general(a, b, (((0,), (0,)), ((), ())), preferred_element_type=jnp.float32)


def nn_dot(a, b):
    return lax.dot_general(a, b, (((1,), (0,)), ((), ())), preferred_element_type=jnp.float32)


def tile_pass(bias_ref, first, tile_query, tile_grad, keys, values):
    score_scale = HEAD_SIZE ** (-0.5)
    scores = [
        score_scale * nt_dot(tile_query, k) + bias_ref[first + i] for i, k in enumerate(keys)
    ]
    row_max = jnp.max(scores[0], axis=-1, keepdims=True)
    for s in scores[1:]:
        row_max = jnp.maximum(row_max, jnp.max(s, axis=-1, keepdims=True))
    total = sum(jnp.sum(jnp.exp(s - row_max), axis=-1, keepdims=True) for s in scores)
    log_total = row_max + jnp.log(total)
    weights = [jnp.exp(s - log_total).astype(jnp.bfloat16) for s in scores]
    grad_weights = [nt_dot(tile_grad, v) for v in values]
    row_dot = sum(
        jnp.sum(w.astype(jnp.float32) * g, axis=-1, keepdims=True)
        for w, g in zip(weights, grad_weights)
    )
    grad_scores = [
        (w.astype(jnp.float32) * (g - row_dot)).astype(jnp.bfloat16)
        for w, g in zip(weights, grad_weights)
    ]
    query_term = score_scale * sum(nn_dot(d, k) for d, k in zip(grad_scores, keys))
    key_terms = [score_scale * tn_dot(d, tile_query) for d in grad_scores]
    value_terms = [tn_dot(w, tile_grad) for w in weights]
    return query_term, key_terms, value_terms


def attention_kernel(
    bias_ref, q_ref, g_ref, k_ref, v_ref, left_ref, right_ref,
    dq_ref, dk_ref, dv_ref, to_left_ref, to_right_ref,
):
    q_a, q_b = q_ref[0, :TILE], q_ref[0, TILE:]
    g_a, g_b = g_ref[0, :TILE], g_ref[0, TILE:]
    k_a, k_b = k_ref[0, :TILE], k_ref[0, TILE:]
    v_a, v_b = v_ref[0, :TILE], v_ref[0, TILE:]
    k_l, v_l, k_r, v_r = left_ref[0, 0], left_ref[1, 0], right_ref[0, 0], right_ref[1, 0]
    dq_a, dk_a3, dv_a3 = tile_pass(bias_ref, 0, q_a, g_a, (k_l, k_a, k_b), (v_l, v_a, v_b))
    dq_b, dk_b3, dv_b3 = tile_pass(bias_ref, 3, q_b, g_b, (k_a, k_b, k_r), (v_a, v_b, v_r))
    dq_ref[0, :TILE] = dq_a.astype(jnp.bfloat16)
    dq_ref[0, TILE:] = dq_b.astype(jnp.bfloat16)
    dk_ref[0, :TILE] = (dk_a3[1] + dk_b3[0]).astype(jnp.bfloat16)
    dk_ref[0, TILE:] = (dk_a3[2] + dk_b3[1]).astype(jnp.bfloat16)
    dv_ref[0, :TILE] = (dv_a3[1] + dv_b3[0]).astype(jnp.bfloat16)
    dv_ref[0, TILE:] = (dv_a3[2] + dv_b3[1]).astype(jnp.bfloat16)
    to_left_ref[0, 0] = dk_a3[0].astype(jnp.bfloat16)
    to_left_ref[1, 0] = dv_a3[0].astype(jnp.bfloat16)
    to_right_ref[0, 0] = dk_b3[2].astype(jnp.bfloat16)
    to_right_ref[1, 0] = dv_b3[2].astype(jnp.bfloat16)


def attention_backward(bias, chunk, heads, queries, output_gradient, key_matrix, values, left, right):
    clip_count, block_len, _ = queries.shape
    whole = pl.BlockSpec((1, block_len, HEAD_SIZE), lambda c, h: (c, 0, h + chunk * heads))
    rim = pl.BlockSpec((2, 1, TILE, HEAD_SIZE), lambda c, h: (0, c, 0, h))
    out_whole = pl.BlockSpec((1, block_len, HEAD_SIZE), lambda c, h: (c, 0, h))
    whole_shape = jax.ShapeDtypeStruct((clip_count, block_len, heads * HEAD_SIZE), jnp.bfloat16)
    rim_shape = jax.ShapeDtypeStruct((2, clip_count, TILE, heads * HEAD_SIZE), jnp.bfloat16)
    return pl.pallas_call(
        attention_kernel,
        grid=(clip_count, heads),
        in_specs=[pl.BlockSpec(memory_space=pltpu.MemorySpace.SMEM)] + [whole] * 4 + [rim] * 2,
        out_specs=[out_whole] * 3 + [rim] * 2,
        out_shape=[whole_shape] * 3 + [rim_shape] * 2,
    )(bias, queries, output_gradient, key_matrix, values, left, right)


def on_device(
    queries,
    key_matrix,
    values,
    output_gradient,
    normed,
    adapter_down_weight,
    adapter_up_weight,
    listed_key_tiles,
    listed_tile_count,
):
    block_len = queries.shape[1]
    position = lax.axis_index("seq")
    first_tile = position * TILES_DEV

    down_piece = jnp.einsum(
        "pqg,gv->pqv", normed, adapter_down_weight, preferred_element_type=jnp.float32
    )
    lowered_rows = butterfly_sum(down_piece, "head").astype(jnp.bfloat16)

    tile_a, tile_b = first_tile, first_tile + 1
    allowed = chosen_pairs(
        listed_key_tiles,
        listed_tile_count,
        jnp.stack([tile_a, tile_a, tile_a, tile_b, tile_b, tile_b]).astype(jnp.int32),
        jnp.stack([tile_a - 1, tile_a, tile_b, tile_a, tile_b, tile_b + 1]).astype(jnp.int32),
    )
    bias = jnp.where(allowed, 0.0, masked_score).astype(jnp.float32)

    local_heads = queries.shape[2] // HEAD_SIZE
    chunks = 2 if local_heads % 2 == 0 else 1
    per_chunk = local_heads // chunks
    outs = []
    for chunk in range(chunks):
        cols = slice(chunk * per_chunk * HEAD_SIZE, (chunk + 1) * per_chunk * HEAD_SIZE)
        left_kv = shifted(
            jnp.stack((key_matrix[:, block_len - TILE:, cols], values[:, block_len - TILE:, cols])),
            "seq",
            1,
        )
        right_kv = shifted(
            jnp.stack((key_matrix[:, :TILE, cols], values[:, :TILE, cols]), 0), "seq", -1
        )
        dq, dk_own, dv_own, to_left, to_right = attention_backward(
            bias, chunk, per_chunk, queries, output_gradient, key_matrix, values, left_kv, right_kv
        )
        from_right = shifted(to_left, "seq", -1)
        from_left = shifted(to_right, "seq", 1)
        arrived = jnp.concatenate((from_left, from_right), 2).astype(jnp.float32)
        dk = (dk_own.astype(jnp.float32) + arrived[0]).astype(jnp.bfloat16)
        dv = (dv_own.astype(jnp.float32) + arrived[1]).astype(jnp.bfloat16)
        outs.append((dq, dk, dv))
    query_grad, key_grad, value_gradient = (
        jnp.concatenate([o[i] for o in outs], 2) for i in range(3)
    )

    backward_piece = jnp.einsum(
        "dsi,ji->dsj", value_gradient, adapter_up_weight, preferred_element_type=jnp.float32
    )
    backward_rows = butterfly_sum(backward_piece, "head").astype(jnp.bfloat16)
    gradient_down_local = adapter_scale * jnp.einsum(
        "yhm,yhz->mz", normed, backward_rows, preferred_element_type=jnp.float32
    )
    gradient_up_local = adapter_scale * jnp.einsum(
        "igb,igu->bu", lowered_rows, value_gradient, preferred_element_type=jnp.float32
    )
    both = jnp.stack((gradient_down_local, gradient_up_local.T), 0)
    both = all_sum(both, ("rep", "seq"))
    down_projection_grad, up_projection_grad = both[0], both[1].T
    return (query_grad, key_grad, value_gradient, down_projection_grad, up_projection_grad)


def solution(mesh):
    in_specs = (
        P(("groups", "rep"), "seq", "head"),
        P(("groups", "rep"), "seq", "head"),
        P(("groups", "rep"), "seq", "head"),
        P(("groups", "rep"), "seq", "head"),
        P(("groups", "rep"), "seq", "head"),
        P("head", None),
        P(None, "head"),
        P("groups", None),
        P("groups"),
    )
    out_specs = (
        P(("groups", "rep"), "seq", "head"),
        P(("groups", "rep"), "seq", "head"),
        P(("groups", "rep"), "seq", "head"),
        P(("groups", "head"), None),
        P("groups", "head"),
    )
    return jax.shard_map(
        on_device, mesh=mesh, in_specs=in_specs, out_specs=out_specs, check_vma=False
    )
```

```python
import jax
import jax.numpy as jnp
from jax import lax
from jax.sharding import PartitionSpec as P
from jax.experimental import pallas as pl
from jax.experimental.pallas import tpu as pltpu

TILE = 384
TILES_DEV = 2
REACH = 1
HEAD_SIZE = 128


adapter_scale = 0.0078125
masked_score = -1e30


def shifted(shard, axis, by):
    peers = lax.axis_size(axis)
    pairs = [(i, i + by) for i in range(peers) if 0 <= i + by < peers]
    return lax.ppermute(shard, axis, pairs)


def butterfly_sum(tree, axis):
    peers = lax.axis_size(axis)
    if peers & (peers - 1):
        return lax.psum(tree, axis)
    step = 1
    while step < peers:
        pairs = [(i, i ^ step) for i in range(peers)]
        other = lax.ppermute(tree, axis, pairs)
        tree = jax.tree.map(lambda a, b: a + b, tree, other)
        step *= 2
    return tree


def scatter_sum(flat, axis, distances):
    peers = lax.axis_size(axis)
    index = lax.axis_index(axis)
    for step in distances:
        half = flat.shape[0] // 2
        upper = (index & step) != 0
        keep = jnp.where(upper, flat[half:], flat[:half])
        send = jnp.where(upper, flat[:half], flat[half:])
        flat = keep + lax.ppermute(send, axis, [(i, i ^ step) for i in range(peers)])
    return flat


def gather_back(flat, axis, distances):
    peers = lax.axis_size(axis)
    index = lax.axis_index(axis)
    for step in reversed(distances):
        other = lax.ppermute(flat, axis, [(i, i ^ step) for i in range(peers)])
        upper = (index & step) != 0
        flat = jnp.where(upper, jnp.concatenate((other, flat)), jnp.concatenate((flat, other)))
    return flat


def all_sum(array, axes):
    plan = []
    for axis in axes:
        peers = lax.axis_size(axis)
        if peers & (peers - 1):
            return lax.psum(array, axes)
        plan.append((axis, [1 << k for k in range(peers.bit_length() - 1)]))
    pieces = 1
    for _, distances in plan:
        pieces *= 1 << len(distances)
    flat = array.reshape(-1)
    if flat.shape[0] % pieces:
        return lax.psum(array, axes)
    inner, outer = plan[0], plan[1:]
    flat = scatter_sum(flat, inner[0], inner[1])
    for axis, distances in outer:
        flat = scatter_sum(flat, axis, distances[:-1])
        if distances:
            step = distances[-1]
            flat = flat + lax.ppermute(
                flat, axis, [(i, i ^ step) for i in range(lax.axis_size(axis))]
            )
        flat = gather_back(flat, axis, distances[:-1])
    flat = gather_back(flat, inner[0], inner[1])
    return flat.reshape(array.shape)


def chosen_pairs(listed_key_tiles, listed_tile_count, query_tiles, key_tiles):
    total_tiles = listed_key_tiles.shape[0]
    clipped = jnp.clip(query_tiles, 0, total_tiles - 1)
    one_hot = (clipped[:, None] == jnp.arange(total_tiles, dtype=jnp.int32)[None, :]).astype(
        jnp.int32
    )
    key_lists = jnp.sum(one_hot[:, :, None] * listed_key_tiles[None, :, :], axis=1)
    counts = jnp.sum(one_hot * listed_tile_count[None, :], axis=1)
    slot_ids = jnp.arange(listed_key_tiles.shape[1], dtype=jnp.int32)
    matched = (key_lists == key_tiles[:, None]) & (slot_ids[None, :] < counts[:, None])
    inside = (query_tiles >= 0) & (query_tiles < total_tiles)
    return jnp.any(matched, axis=1) & inside


def nt_dot(a, b):
    return lax.dot_general(a, b, (((1,), (1,)), ((), ())), preferred_element_type=jnp.float32)


def tn_dot(a, b):
    return lax.dot_general(a, b, (((0,), (0,)), ((), ())), preferred_element_type=jnp.float32)


def nn_dot(a, b):
    return lax.dot_general(a, b, (((1,), (0,)), ((), ())), preferred_element_type=jnp.float32)


def tile_pass(bias_ref, first, tile_query, tile_grad, keys, values):
    score_scale = HEAD_SIZE ** (-0.5)
    scores = [score_scale * nt_dot(tile_query, k) for k in keys]
    row_max = jnp.max(scores[0], axis=-1, keepdims=True) + bias_ref[first]
    for i, s in enumerate(scores[1:], 1):
        row_max = jnp.maximum(row_max, jnp.max(s, axis=-1, keepdims=True) + bias_ref[first + i])
    probs = [jnp.exp(s - (row_max - bias_ref[first + i])) for i, s in enumerate(scores)]
    total = sum(jnp.sum(p, axis=-1, keepdims=True) for p in probs)
    inverse = 1.0 / total
    weights = [(p * inverse).astype(jnp.bfloat16) for p in probs]
    grad_weights = [nt_dot(tile_grad, v) for v in values]
    row_dot = sum(
        jnp.sum(w.astype(jnp.float32) * g, axis=-1, keepdims=True)
        for w, g in zip(weights, grad_weights)
    )
    grad_scores = [
        (w.astype(jnp.float32) * (g - row_dot)).astype(jnp.bfloat16)
        for w, g in zip(weights, grad_weights)
    ]
    query_term = score_scale * sum(nn_dot(d, k) for d, k in zip(grad_scores, keys))
    key_terms = [score_scale * tn_dot(d, tile_query) for d in grad_scores]
    value_terms = [tn_dot(w, tile_grad) for w in weights]
    return query_term, key_terms, value_terms


def attention_kernel(
    bias_ref, q_ref, g_ref, k_ref, v_ref, left_ref, right_ref,
    dq_ref, dk_ref, dv_ref, to_left_ref, to_right_ref,
):
    q_a, q_b = q_ref[0, :TILE], q_ref[0, TILE:]
    g_a, g_b = g_ref[0, :TILE], g_ref[0, TILE:]
    k_a, k_b = k_ref[0, :TILE], k_ref[0, TILE:]
    v_a, v_b = v_ref[0, :TILE], v_ref[0, TILE:]
    k_l, v_l, k_r, v_r = left_ref[0, 0], left_ref[1, 0], right_ref[0, 0], right_ref[1, 0]
    dq_a, dk_a3, dv_a3 = tile_pass(bias_ref, 0, q_a, g_a, (k_l, k_a, k_b), (v_l, v_a, v_b))
    dq_b, dk_b3, dv_b3 = tile_pass(bias_ref, 3, q_b, g_b, (k_a, k_b, k_r), (v_a, v_b, v_r))
    dq_ref[0, :TILE] = dq_a.astype(jnp.bfloat16)
    dq_ref[0, TILE:] = dq_b.astype(jnp.bfloat16)
    dk_ref[0, :TILE] = (dk_a3[1] + dk_b3[0]).astype(jnp.bfloat16)
    dk_ref[0, TILE:] = (dk_a3[2] + dk_b3[1]).astype(jnp.bfloat16)
    dv_ref[0, :TILE] = (dv_a3[1] + dv_b3[0]).astype(jnp.bfloat16)
    dv_ref[0, TILE:] = (dv_a3[2] + dv_b3[1]).astype(jnp.bfloat16)
    to_left_ref[0, 0] = dk_a3[0].astype(jnp.bfloat16)
    to_left_ref[1, 0] = dv_a3[0].astype(jnp.bfloat16)
    to_right_ref[0, 0] = dk_b3[2].astype(jnp.bfloat16)
    to_right_ref[1, 0] = dv_b3[2].astype(jnp.bfloat16)


def attention_backward(bias, chunk, heads, queries, output_gradient, key_matrix, values, left, right):
    clip_count, block_len, _ = queries.shape
    whole = pl.BlockSpec((1, block_len, HEAD_SIZE), lambda c, h: (c, 0, h + chunk * heads))
    rim = pl.BlockSpec((2, 1, TILE, HEAD_SIZE), lambda c, h: (0, c, 0, h))
    out_whole = pl.BlockSpec((1, block_len, HEAD_SIZE), lambda c, h: (c, 0, h))
    whole_shape = jax.ShapeDtypeStruct((clip_count, block_len, heads * HEAD_SIZE), jnp.bfloat16)
    rim_shape = jax.ShapeDtypeStruct((2, clip_count, TILE, heads * HEAD_SIZE), jnp.bfloat16)
    return pl.pallas_call(
        attention_kernel,
        grid=(clip_count, heads),
        in_specs=[pl.BlockSpec(memory_space=pltpu.MemorySpace.SMEM)] + [whole] * 4 + [rim] * 2,
        out_specs=[out_whole] * 3 + [rim] * 2,
        out_shape=[whole_shape] * 3 + [rim_shape] * 2,
    )(bias, queries, output_gradient, key_matrix, values, left, right)


def on_device(
    queries,
    key_matrix,
    values,
    output_gradient,
    normed,
    adapter_down_weight,
    adapter_up_weight,
    listed_key_tiles,
    listed_tile_count,
):
    block_len = queries.shape[1]
    position = lax.axis_index("seq")
    first_tile = position * TILES_DEV

    down_piece = jnp.einsum(
        "pqg,gv->pqv", normed, adapter_down_weight, preferred_element_type=jnp.float32
    )
    lowered_rows = butterfly_sum(down_piece, "head").astype(jnp.bfloat16)

    tile_a, tile_b = first_tile, first_tile + 1
    allowed = chosen_pairs(
        listed_key_tiles,
        listed_tile_count,
        jnp.stack([tile_a, tile_a, tile_a, tile_b, tile_b, tile_b]).astype(jnp.int32),
        jnp.stack([tile_a - 1, tile_a, tile_b, tile_a, tile_b, tile_b + 1]).astype(jnp.int32),
    )
    bias = jnp.where(allowed, 0.0, masked_score).astype(jnp.float32)

    local_heads = queries.shape[2] // HEAD_SIZE
    chunks = 2 if local_heads % 2 == 0 else 1
    per_chunk = local_heads // chunks
    outs = []
    for chunk in range(chunks):
        cols = slice(chunk * per_chunk * HEAD_SIZE, (chunk + 1) * per_chunk * HEAD_SIZE)
        left_kv = shifted(
            jnp.stack((key_matrix[:, block_len - TILE:, cols], values[:, block_len - TILE:, cols])),
            "seq",
            1,
        )
        right_kv = shifted(
            jnp.stack((key_matrix[:, :TILE, cols], values[:, :TILE, cols]), 0), "seq", -1
        )
        dq, dk_own, dv_own, to_left, to_right = attention_backward(
            bias, chunk, per_chunk, queries, output_gradient, key_matrix, values, left_kv, right_kv
        )
        from_right = shifted(to_left, "seq", -1)
        from_left = shifted(to_right, "seq", 1)
        arrived = jnp.concatenate((from_left, from_right), 2).astype(jnp.float32)
        dk = (dk_own.astype(jnp.float32) + arrived[0]).astype(jnp.bfloat16)
        dv = (dv_own.astype(jnp.float32) + arrived[1]).astype(jnp.bfloat16)
        outs.append((dq, dk, dv))
    query_grad, key_grad, value_gradient = (
        jnp.concatenate([o[i] for o in outs], 2) for i in range(3)
    )

    backward_piece = jnp.einsum(
        "dsi,ji->dsj", value_gradient, adapter_up_weight, preferred_element_type=jnp.float32
    )
    backward_rows = butterfly_sum(backward_piece, "head").astype(jnp.bfloat16)
    gradient_down_local = adapter_scale * jnp.einsum(
        "yhm,yhz->mz", normed, backward_rows, preferred_element_type=jnp.float32
    )
    gradient_up_local = adapter_scale * jnp.einsum(
        "igb,igu->bu", lowered_rows, value_gradient, preferred_element_type=jnp.float32
    )
    both = jnp.stack((gradient_down_local, gradient_up_local.T), 0)
    both = all_sum(both, ("rep", "seq"))
    down_projection_grad, up_projection_grad = both[0], both[1].T
    return (query_grad, key_grad, value_gradient, down_projection_grad, up_projection_grad)


def solution(mesh):
    in_specs = (
        P(("groups", "rep"), "seq", "head"),
        P(("groups", "rep"), "seq", "head"),
        P(("groups", "rep"), "seq", "head"),
        P(("groups", "rep"), "seq", "head"),
        P(("groups", "rep"), "seq", "head"),
        P("head", None),
        P(None, "head"),
        P("groups", None),
        P("groups"),
    )
    out_specs = (
        P(("groups", "rep"), "seq", "head"),
        P(("groups", "rep"), "seq", "head"),
        P(("groups", "rep"), "seq", "head"),
        P(("groups", "head"), None),
        P("groups", "head"),
    )
    return jax.shard_map(
        on_device, mesh=mesh, in_specs=in_specs, out_specs=out_specs, check_vma=False
    )
```

```python
import jax
import jax.numpy as jnp
from jax import lax
from jax.sharding import PartitionSpec as P
from jax.experimental import pallas as pl
from jax.experimental.pallas import tpu as pltpu

TILE = 384
TILES_DEV = 2
REACH = 1
HEAD_SIZE = 128


adapter_scale = 0.0078125
masked_score = -1e30


def shifted(shard, axis, by):
    peers = lax.axis_size(axis)
    pairs = [(i, i + by) for i in range(peers) if 0 <= i + by < peers]
    return lax.ppermute(shard, axis, pairs)


def butterfly_sum(tree, axis):
    peers = lax.axis_size(axis)
    if peers & (peers - 1):
        return lax.psum(tree, axis)
    step = 1
    while step < peers:
        pairs = [(i, i ^ step) for i in range(peers)]
        other = lax.ppermute(tree, axis, pairs)
        tree = jax.tree.map(lambda a, b: a + b, tree, other)
        step *= 2
    return tree


def scatter_sum(flat, axis, distances):
    peers = lax.axis_size(axis)
    index = lax.axis_index(axis)
    for step in distances:
        half = flat.shape[0] // 2
        upper = (index & step) != 0
        keep = jnp.where(upper, flat[half:], flat[:half])
        send = jnp.where(upper, flat[:half], flat[half:])
        flat = keep + lax.ppermute(send, axis, [(i, i ^ step) for i in range(peers)])
    return flat


def gather_back(flat, axis, distances):
    peers = lax.axis_size(axis)
    index = lax.axis_index(axis)
    for step in reversed(distances):
        other = lax.ppermute(flat, axis, [(i, i ^ step) for i in range(peers)])
        upper = (index & step) != 0
        flat = jnp.where(upper, jnp.concatenate((other, flat)), jnp.concatenate((flat, other)))
    return flat


def all_sum(array, axes):
    plan = []
    for axis in axes:
        peers = lax.axis_size(axis)
        if peers & (peers - 1):
            return lax.psum(array, axes)
        plan.append((axis, [1 << k for k in range(peers.bit_length() - 1)]))
    pieces = 1
    for _, distances in plan:
        pieces *= 1 << len(distances)
    flat = array.reshape(-1)
    if flat.shape[0] % pieces:
        return lax.psum(array, axes)
    inner, outer = plan[0], plan[1:]
    flat = scatter_sum(flat, inner[0], inner[1])
    for axis, distances in outer:
        flat = scatter_sum(flat, axis, distances[:-1])
        if distances:
            step = distances[-1]
            flat = flat + lax.ppermute(
                flat, axis, [(i, i ^ step) for i in range(lax.axis_size(axis))]
            )
        flat = gather_back(flat, axis, distances[:-1])
    flat = gather_back(flat, inner[0], inner[1])
    return flat.reshape(array.shape)


def chosen_pairs(listed_key_tiles, listed_tile_count, query_tiles, key_tiles):
    total_tiles = listed_key_tiles.shape[0]
    clipped = jnp.clip(query_tiles, 0, total_tiles - 1)
    one_hot = (clipped[:, None] == jnp.arange(total_tiles, dtype=jnp.int32)[None, :]).astype(
        jnp.int32
    )
    key_lists = jnp.sum(one_hot[:, :, None] * listed_key_tiles[None, :, :], axis=1)
    counts = jnp.sum(one_hot * listed_tile_count[None, :], axis=1)
    slot_ids = jnp.arange(listed_key_tiles.shape[1], dtype=jnp.int32)
    matched = (key_lists == key_tiles[:, None]) & (slot_ids[None, :] < counts[:, None])
    inside = (query_tiles >= 0) & (query_tiles < total_tiles)
    return jnp.any(matched, axis=1) & inside


def nt_dot(a, b):
    return lax.dot_general(a, b, (((1,), (1,)), ((), ())), preferred_element_type=jnp.float32)


def tn_dot(a, b):
    return lax.dot_general(a, b, (((0,), (0,)), ((), ())), preferred_element_type=jnp.float32)


def nn_dot(a, b):
    return lax.dot_general(a, b, (((1,), (0,)), ((), ())), preferred_element_type=jnp.float32)


def tile_pass(bias_ref, first, tile_query, tile_grad, keys, values):
    score_scale = HEAD_SIZE ** (-0.5)
    scores = [
        score_scale * nt_dot(tile_query, k) + bias_ref[first + i] for i, k in enumerate(keys)
    ]
    row_max = jnp.max(scores[0], axis=-1, keepdims=True)
    for s in scores[1:]:
        row_max = jnp.maximum(row_max, jnp.max(s, axis=-1, keepdims=True))
    total = sum(jnp.sum(jnp.exp(s - row_max), axis=-1, keepdims=True) for s in scores)
    log_total = row_max + jnp.log(total)
    weights = [jnp.exp(s - log_total).astype(jnp.bfloat16) for s in scores]
    grad_weights = [nt_dot(tile_grad, v) for v in values]
    row_dot = sum(
        jnp.sum(w.astype(jnp.float32) * g, axis=-1, keepdims=True)
        for w, g in zip(weights, grad_weights)
    )
    grad_scores = [
        (w.astype(jnp.float32) * (g - row_dot)).astype(jnp.bfloat16)
        for w, g in zip(weights, grad_weights)
    ]
    query_term = score_scale * sum(nn_dot(d, k) for d, k in zip(grad_scores, keys))
    key_terms = [score_scale * tn_dot(d, tile_query) for d in grad_scores]
    value_terms = [tn_dot(w, tile_grad) for w in weights]
    return query_term, key_terms, value_terms


def attention_kernel(
    bias_ref, q_ref, g_ref, k_ref, v_ref, left_ref, right_ref,
    dq_ref, dk_ref, dv_ref, to_left_ref, to_right_ref,
):
    q_a, q_b = q_ref[0, :TILE], q_ref[0, TILE:]
    g_a, g_b = g_ref[0, :TILE], g_ref[0, TILE:]
    k_a, k_b = k_ref[0, :TILE], k_ref[0, TILE:]
    v_a, v_b = v_ref[0, :TILE], v_ref[0, TILE:]
    k_l, v_l, k_r, v_r = left_ref[0, 0], left_ref[1, 0], right_ref[0, 0], right_ref[1, 0]
    dq_a, dk_a3, dv_a3 = tile_pass(bias_ref, 0, q_a, g_a, (k_l, k_a, k_b), (v_l, v_a, v_b))
    dq_b, dk_b3, dv_b3 = tile_pass(bias_ref, 3, q_b, g_b, (k_a, k_b, k_r), (v_a, v_b, v_r))
    dq_ref[0, :TILE] = dq_a.astype(jnp.bfloat16)
    dq_ref[0, TILE:] = dq_b.astype(jnp.bfloat16)
    dk_ref[0, :TILE] = (dk_a3[1] + dk_b3[0]).astype(jnp.bfloat16)
    dk_ref[0, TILE:] = (dk_a3[2] + dk_b3[1]).astype(jnp.bfloat16)
    dv_ref[0, :TILE] = (dv_a3[1] + dv_b3[0]).astype(jnp.bfloat16)
    dv_ref[0, TILE:] = (dv_a3[2] + dv_b3[1]).astype(jnp.bfloat16)
    to_left_ref[0, 0] = dk_a3[0].astype(jnp.bfloat16)
    to_left_ref[1, 0] = dv_a3[0].astype(jnp.bfloat16)
    to_right_ref[0, 0] = dk_b3[2].astype(jnp.bfloat16)
    to_right_ref[1, 0] = dv_b3[2].astype(jnp.bfloat16)


def attention_backward(bias, chunk, heads, queries, output_gradient, key_matrix, values, left, right):
    clip_count, block_len, _ = queries.shape
    whole = pl.BlockSpec((1, block_len, HEAD_SIZE), lambda c, h: (c, 0, h + chunk * heads))
    rim = pl.BlockSpec((2, 1, TILE, HEAD_SIZE), lambda c, h: (0, c, 0, h))
    out_whole = pl.BlockSpec((1, block_len, HEAD_SIZE), lambda c, h: (c, 0, h))
    whole_shape = jax.ShapeDtypeStruct((clip_count, block_len, heads * HEAD_SIZE), jnp.bfloat16)
    rim_shape = jax.ShapeDtypeStruct((2, clip_count, TILE, heads * HEAD_SIZE), jnp.bfloat16)
    return pl.pallas_call(
        attention_kernel,
        grid=(clip_count, heads),
        in_specs=[pl.BlockSpec(memory_space=pltpu.MemorySpace.SMEM)] + [whole] * 4 + [rim] * 2,
        out_specs=[out_whole] * 3 + [rim] * 2,
        out_shape=[whole_shape] * 3 + [rim_shape] * 2,
    )(bias, queries, output_gradient, key_matrix, values, left, right)


def on_device(
    queries,
    key_matrix,
    values,
    output_gradient,
    normed,
    adapter_down_weight,
    adapter_up_weight,
    listed_key_tiles,
    listed_tile_count,
):
    block_len = queries.shape[1]
    position = lax.axis_index("seq")
    first_tile = position * TILES_DEV

    down_piece = jnp.einsum(
        "pqg,gv->pqv", normed, adapter_down_weight, preferred_element_type=jnp.float32
    )
    lowered_rows = butterfly_sum(down_piece, "head").astype(jnp.bfloat16)

    tile_a, tile_b = first_tile, first_tile + 1
    allowed = chosen_pairs(
        listed_key_tiles,
        listed_tile_count,
        jnp.stack([tile_a, tile_a, tile_a, tile_b, tile_b, tile_b]).astype(jnp.int32),
        jnp.stack([tile_a - 1, tile_a, tile_b, tile_a, tile_b, tile_b + 1]).astype(jnp.int32),
    )
    bias = jnp.where(allowed, 0.0, masked_score).astype(jnp.float32)

    local_heads = queries.shape[2] // HEAD_SIZE
    chunks = 2 if local_heads % 2 == 0 else 1
    per_chunk = local_heads // chunks
    outs = []
    for chunk in range(chunks):
        cols = slice(chunk * per_chunk * HEAD_SIZE, (chunk + 1) * per_chunk * HEAD_SIZE)
        left_kv = shifted(
            jnp.stack((key_matrix[:, block_len - TILE:, cols], values[:, block_len - TILE:, cols])),
            "seq",
            1,
        )
        right_kv = shifted(
            jnp.stack((key_matrix[:, :TILE, cols], values[:, :TILE, cols]), 0), "seq", -1
        )
        dq, dk_own, dv_own, to_left, to_right = attention_backward(
            bias, chunk, per_chunk, queries, output_gradient, key_matrix, values, left_kv, right_kv
        )
        from_right = shifted(to_left, "seq", -1)
        from_left = shifted(to_right, "seq", 1)
        arrived = jnp.concatenate((from_left, from_right), 2).astype(jnp.float32)
        dk = (dk_own.astype(jnp.float32) + arrived[0]).astype(jnp.bfloat16)
        dv = (dv_own.astype(jnp.float32) + arrived[1]).astype(jnp.bfloat16)
        outs.append((dq, dk, dv))
    query_grad, key_grad, value_gradient = (
        jnp.concatenate([o[i] for o in outs], 2) for i in range(3)
    )

    backward_piece = jnp.einsum(
        "dsi,ji->dsj", value_gradient, adapter_up_weight, preferred_element_type=jnp.float32
    )
    backward_rows = butterfly_sum(backward_piece, "head").astype(jnp.bfloat16)
    gradient_down_local = adapter_scale * jnp.einsum(
        "yhm,yhz->mz", normed, backward_rows, preferred_element_type=jnp.float32
    )
    gradient_up_local = adapter_scale * jnp.einsum(
        "igb,igu->bu", lowered_rows, value_gradient, preferred_element_type=jnp.float32
    )
    both = jnp.stack((gradient_down_local.T, gradient_up_local), 0)
    both = all_sum(both, ("rep", "seq"))
    down_projection_grad, up_projection_grad = both[0].T, both[1]
    return (query_grad, key_grad, value_gradient, down_projection_grad, up_projection_grad)


def solution(mesh):
    in_specs = (
        P(("groups", "rep"), "seq", "head"),
        P(("groups", "rep"), "seq", "head"),
        P(("groups", "rep"), "seq", "head"),
        P(("groups", "rep"), "seq", "head"),
        P(("groups", "rep"), "seq", "head"),
        P("head", None),
        P(None, "head"),
        P("groups", None),
        P("groups"),
    )
    out_specs = (
        P(("groups", "rep"), "seq", "head"),
        P(("groups", "rep"), "seq", "head"),
        P(("groups", "rep"), "seq", "head"),
        P(("groups", "head"), None),
        P("groups", "head"),
    )
    return jax.shard_map(
        on_device, mesh=mesh, in_specs=in_specs, out_specs=out_specs, check_vma=False
    )
```

```python
import jax
import jax.numpy as jnp
from jax import lax
from jax.sharding import PartitionSpec as P
from jax.experimental import pallas as pl
from jax.experimental.pallas import tpu as pltpu

TILE = 384
TILES_DEV = 2
REACH = 1
HEAD_SIZE = 128


adapter_scale = 0.0078125
masked_score = -1e30


def shifted(shard, axis, by):
    peers = lax.axis_size(axis)
    pairs = [(i, i + by) for i in range(peers) if 0 <= i + by < peers]
    return lax.ppermute(shard, axis, pairs)


def butterfly_sum(tree, axis):
    peers = lax.axis_size(axis)
    if peers & (peers - 1):
        return lax.psum(tree, axis)
    step = 1
    while step < peers:
        pairs = [(i, i ^ step) for i in range(peers)]
        other = lax.ppermute(tree, axis, pairs)
        tree = jax.tree.map(lambda a, b: a + b, tree, other)
        step *= 2
    return tree


def scatter_sum(flat, axis, distances):
    peers = lax.axis_size(axis)
    index = lax.axis_index(axis)
    for step in distances:
        half = flat.shape[0] // 2
        upper = (index & step) != 0
        keep = jnp.where(upper, flat[half:], flat[:half])
        send = jnp.where(upper, flat[:half], flat[half:])
        flat = keep + lax.ppermute(send, axis, [(i, i ^ step) for i in range(peers)])
    return flat


def gather_back(flat, axis, distances):
    peers = lax.axis_size(axis)
    index = lax.axis_index(axis)
    for step in reversed(distances):
        other = lax.ppermute(flat, axis, [(i, i ^ step) for i in range(peers)])
        upper = (index & step) != 0
        flat = jnp.where(upper, jnp.concatenate((other, flat)), jnp.concatenate((flat, other)))
    return flat


def all_sum(array, axes):
    plan = []
    for axis in axes:
        peers = lax.axis_size(axis)
        if peers & (peers - 1):
            return lax.psum(array, axes)
        plan.append((axis, [1 << k for k in range(peers.bit_length() - 1)]))
    pieces = 1
    for _, distances in plan:
        pieces *= 1 << len(distances)
    flat = array.reshape(-1)
    if flat.shape[0] % pieces:
        return lax.psum(array, axes)
    inner, outer = plan[0], plan[1:]
    flat = scatter_sum(flat, inner[0], inner[1])
    for axis, distances in outer:
        flat = scatter_sum(flat, axis, distances[:-1])
        if distances:
            step = distances[-1]
            flat = flat + lax.ppermute(
                flat, axis, [(i, i ^ step) for i in range(lax.axis_size(axis))]
            )
        flat = gather_back(flat, axis, distances[:-1])
    flat = gather_back(flat, inner[0], inner[1])
    return flat.reshape(array.shape)


def chosen_pairs(listed_key_tiles, listed_tile_count, query_tiles, key_tiles):
    total_tiles = listed_key_tiles.shape[0]
    clipped = jnp.clip(query_tiles, 0, total_tiles - 1)
    one_hot = (clipped[:, None] == jnp.arange(total_tiles, dtype=jnp.int32)[None, :]).astype(
        jnp.int32
    )
    key_lists = jnp.sum(one_hot[:, :, None] * listed_key_tiles[None, :, :], axis=1)
    counts = jnp.sum(one_hot * listed_tile_count[None, :], axis=1)
    slot_ids = jnp.arange(listed_key_tiles.shape[1], dtype=jnp.int32)
    matched = (key_lists == key_tiles[:, None]) & (slot_ids[None, :] < counts[:, None])
    inside = (query_tiles >= 0) & (query_tiles < total_tiles)
    return jnp.any(matched, axis=1) & inside


def nt_dot(a, b):
    return lax.dot_general(a, b, (((1,), (1,)), ((), ())), preferred_element_type=jnp.float32)


def tn_dot(a, b):
    return lax.dot_general(a, b, (((0,), (0,)), ((), ())), preferred_element_type=jnp.float32)


def nn_dot(a, b):
    return lax.dot_general(a, b, (((1,), (0,)), ((), ())), preferred_element_type=jnp.float32)


def tile_pass(bias_ref, first, tile_query, tile_grad, keys, values):
    score_scale = HEAD_SIZE ** (-0.5)
    scores = [
        score_scale * nt_dot(tile_query, k) + bias_ref[first + i] for i, k in enumerate(keys)
    ]
    row_max = jnp.max(scores[0], axis=-1, keepdims=True)
    for s in scores[1:]:
        row_max = jnp.maximum(row_max, jnp.max(s, axis=-1, keepdims=True))
    total = sum(jnp.sum(jnp.exp(s - row_max), axis=-1, keepdims=True) for s in scores)
    log_total = row_max + jnp.log(total)
    weights = [jnp.exp(s - log_total).astype(jnp.bfloat16) for s in scores]
    grad_weights = [nt_dot(tile_grad, v) for v in values]
    row_dot = sum(
        jnp.sum(w.astype(jnp.float32) * g, axis=-1, keepdims=True)
        for w, g in zip(weights, grad_weights)
    )
    grad_scores = [
        (w.astype(jnp.float32) * (g - row_dot)).astype(jnp.bfloat16)
        for w, g in zip(weights, grad_weights)
    ]
    query_term = score_scale * sum(nn_dot(d, k) for d, k in zip(grad_scores, keys))
    key_terms = [score_scale * tn_dot(d, tile_query) for d in grad_scores]
    value_terms = [tn_dot(w, tile_grad) for w in weights]
    return query_term, key_terms, value_terms


def attention_kernel(
    bias_ref, q_ref, g_ref, k_ref, v_ref, left_ref, right_ref,
    dq_ref, dk_ref, dv_ref, to_left_ref, to_right_ref,
):
    q_a, q_b = q_ref[0, :TILE], q_ref[0, TILE:]
    g_a, g_b = g_ref[0, :TILE], g_ref[0, TILE:]
    k_a, k_b = k_ref[0, :TILE], k_ref[0, TILE:]
    v_a, v_b = v_ref[0, :TILE], v_ref[0, TILE:]
    k_l, v_l, k_r, v_r = left_ref[0, 0], left_ref[1, 0], right_ref[0, 0], right_ref[1, 0]
    dq_a, dk_a3, dv_a3 = tile_pass(bias_ref, 0, q_a, g_a, (k_l, k_a, k_b), (v_l, v_a, v_b))
    dq_b, dk_b3, dv_b3 = tile_pass(bias_ref, 3, q_b, g_b, (k_a, k_b, k_r), (v_a, v_b, v_r))
    dq_ref[0, :TILE] = dq_a.astype(jnp.bfloat16)
    dq_ref[0, TILE:] = dq_b.astype(jnp.bfloat16)
    dk_ref[0, :TILE] = (dk_a3[1] + dk_b3[0]).astype(jnp.bfloat16)
    dk_ref[0, TILE:] = (dk_a3[2] + dk_b3[1]).astype(jnp.bfloat16)
    dv_ref[0, :TILE] = (dv_a3[1] + dv_b3[0]).astype(jnp.bfloat16)
    dv_ref[0, TILE:] = (dv_a3[2] + dv_b3[1]).astype(jnp.bfloat16)
    to_left_ref[0, 0] = dk_a3[0].astype(jnp.bfloat16)
    to_left_ref[1, 0] = dv_a3[0].astype(jnp.bfloat16)
    to_right_ref[0, 0] = dk_b3[2].astype(jnp.bfloat16)
    to_right_ref[1, 0] = dv_b3[2].astype(jnp.bfloat16)


def attention_backward(bias, chunk, heads, queries, output_gradient, key_matrix, values, left, right):
    clip_count, block_len, _ = queries.shape
    whole = pl.BlockSpec((1, block_len, HEAD_SIZE), lambda c, h: (c, 0, h + chunk * heads))
    rim = pl.BlockSpec((2, 1, TILE, HEAD_SIZE), lambda c, h: (0, c, 0, h))
    out_whole = pl.BlockSpec((1, block_len, HEAD_SIZE), lambda c, h: (c, 0, h))
    whole_shape = jax.ShapeDtypeStruct((clip_count, block_len, heads * HEAD_SIZE), jnp.bfloat16)
    rim_shape = jax.ShapeDtypeStruct((2, clip_count, TILE, heads * HEAD_SIZE), jnp.bfloat16)
    return pl.pallas_call(
        attention_kernel,
        grid=(clip_count, heads),
        in_specs=[pl.BlockSpec(memory_space=pltpu.MemorySpace.SMEM)] + [whole] * 4 + [rim] * 2,
        out_specs=[out_whole] * 3 + [rim] * 2,
        out_shape=[whole_shape] * 3 + [rim_shape] * 2,
    )(bias, queries, output_gradient, key_matrix, values, left, right)


def on_device(
    queries,
    key_matrix,
    values,
    output_gradient,
    normed,
    adapter_down_weight,
    adapter_up_weight,
    listed_key_tiles,
    listed_tile_count,
):
    block_len = queries.shape[1]
    position = lax.axis_index("seq")
    first_tile = position * TILES_DEV

    down_piece = jnp.einsum(
        "pqg,gv->pqv", normed, adapter_down_weight, preferred_element_type=jnp.float32
    )
    lowered_rows = butterfly_sum(down_piece, "head").astype(jnp.bfloat16)

    tile_a, tile_b = first_tile, first_tile + 1
    allowed = chosen_pairs(
        listed_key_tiles,
        listed_tile_count,
        jnp.stack([tile_a, tile_a, tile_a, tile_b, tile_b, tile_b]).astype(jnp.int32),
        jnp.stack([tile_a - 1, tile_a, tile_b, tile_a, tile_b, tile_b + 1]).astype(jnp.int32),
    )
    bias = jnp.where(allowed, 0.0, masked_score).astype(jnp.float32)

    local_heads = queries.shape[2] // HEAD_SIZE
    chunks = 2 if local_heads % 2 == 0 else 1
    per_chunk = local_heads // chunks
    outs = []
    for chunk in range(chunks):
        cols = slice(chunk * per_chunk * HEAD_SIZE, (chunk + 1) * per_chunk * HEAD_SIZE)
        left_kv = shifted(
            jnp.stack((key_matrix[:, block_len - TILE:, cols], values[:, block_len - TILE:, cols])),
            "seq",
            1,
        )
        right_kv = shifted(
            jnp.stack((key_matrix[:, :TILE, cols], values[:, :TILE, cols]), 0), "seq", -1
        )
        dq, dk_own, dv_own, to_left, to_right = attention_backward(
            bias, chunk, per_chunk, queries, output_gradient, key_matrix, values, left_kv, right_kv
        )
        from_right = shifted(to_left, "seq", -1)
        from_left = shifted(to_right, "seq", 1)
        arrived = jnp.concatenate((from_left, from_right), 2).astype(jnp.float32)
        dk = (dk_own.astype(jnp.float32) + arrived[0]).astype(jnp.bfloat16)
        dv = (dv_own.astype(jnp.float32) + arrived[1]).astype(jnp.bfloat16)
        outs.append((dq, dk, dv))
    query_grad, key_grad, value_gradient = (
        jnp.concatenate([o[i] for o in outs], 2) for i in range(3)
    )

    backward_piece = jnp.einsum(
        "dsi,ji->dsj", value_gradient, adapter_up_weight, preferred_element_type=jnp.float32
    )
    backward_rows = butterfly_sum(backward_piece, "head").astype(jnp.bfloat16)
    gradient_down_local = adapter_scale * jnp.einsum(
        "yhm,yhz->mz", normed, backward_rows, preferred_element_type=jnp.float32
    )
    gradient_up_local = adapter_scale * jnp.einsum(
        "igb,igu->bu", lowered_rows, value_gradient, preferred_element_type=jnp.float32
    )
    up_projection_grad = all_sum(gradient_up_local, ("rep", "seq"))
    down_projection_grad = all_sum(gradient_down_local.T, ("rep", "seq")).T
    return (query_grad, key_grad, value_gradient, down_projection_grad, up_projection_grad)


def solution(mesh):
    in_specs = (
        P(("groups", "rep"), "seq", "head"),
        P(("groups", "rep"), "seq", "head"),
        P(("groups", "rep"), "seq", "head"),
        P(("groups", "rep"), "seq", "head"),
        P(("groups", "rep"), "seq", "head"),
        P("head", None),
        P(None, "head"),
        P("groups", None),
        P("groups"),
    )
    out_specs = (
        P(("groups", "rep"), "seq", "head"),
        P(("groups", "rep"), "seq", "head"),
        P(("groups", "rep"), "seq", "head"),
        P(("groups", "head"), None),
        P("groups", "head"),
    )
    return jax.shard_map(
        on_device, mesh=mesh, in_specs=in_specs, out_specs=out_specs, check_vma=False
    )
```

```python
import jax
import jax.numpy as jnp
from jax import lax
from jax.sharding import PartitionSpec as P
from jax.experimental import pallas as pl
from jax.experimental.pallas import tpu as pltpu

TILE = 384
TILES_DEV = 2
REACH = 1
HEAD_SIZE = 128


adapter_scale = 0.0078125
masked_score = -1e30


def shifted(shard, axis, by):
    peers = lax.axis_size(axis)
    pairs = [(i, i + by) for i in range(peers) if 0 <= i + by < peers]
    return lax.ppermute(shard, axis, pairs)


def butterfly_sum(tree, axis):
    peers = lax.axis_size(axis)
    if peers & (peers - 1):
        return lax.psum(tree, axis)
    step = 1
    while step < peers:
        pairs = [(i, i ^ step) for i in range(peers)]
        other = lax.ppermute(tree, axis, pairs)
        tree = jax.tree.map(lambda a, b: a + b, tree, other)
        step *= 2
    return tree


def scatter_sum(flat, axis, distances):
    peers = lax.axis_size(axis)
    index = lax.axis_index(axis)
    for step in distances:
        half = flat.shape[0] // 2
        upper = (index & step) != 0
        keep = jnp.where(upper, flat[half:], flat[:half])
        send = jnp.where(upper, flat[:half], flat[half:])
        flat = keep + lax.ppermute(send, axis, [(i, i ^ step) for i in range(peers)])
    return flat


def gather_back(flat, axis, distances):
    peers = lax.axis_size(axis)
    index = lax.axis_index(axis)
    for step in reversed(distances):
        other = lax.ppermute(flat, axis, [(i, i ^ step) for i in range(peers)])
        upper = (index & step) != 0
        flat = jnp.where(upper, jnp.concatenate((other, flat)), jnp.concatenate((flat, other)))
    return flat


def all_sum(array, axes):
    plan = []
    for axis in axes:
        peers = lax.axis_size(axis)
        if peers & (peers - 1):
            return lax.psum(array, axes)
        plan.append((axis, [1 << k for k in range(peers.bit_length() - 1)]))
    pieces = 1
    for _, distances in plan:
        pieces *= 1 << len(distances)
    flat = array.reshape(-1)
    if flat.shape[0] % pieces:
        return lax.psum(array, axes)
    inner, outer = plan[0], plan[1:]
    flat = scatter_sum(flat, inner[0], inner[1])
    for axis, distances in outer:
        flat = scatter_sum(flat, axis, distances[:-1])
        if distances:
            step = distances[-1]
            flat = flat + lax.ppermute(
                flat, axis, [(i, i ^ step) for i in range(lax.axis_size(axis))]
            )
        flat = gather_back(flat, axis, distances[:-1])
    flat = gather_back(flat, inner[0], inner[1])
    return flat.reshape(array.shape)


def chosen_pairs(listed_key_tiles, listed_tile_count, query_tiles, key_tiles):
    total_tiles = listed_key_tiles.shape[0]
    clipped = jnp.clip(query_tiles, 0, total_tiles - 1)
    one_hot = (clipped[:, None] == jnp.arange(total_tiles, dtype=jnp.int32)[None, :]).astype(
        jnp.int32
    )
    key_lists = jnp.sum(one_hot[:, :, None] * listed_key_tiles[None, :, :], axis=1)
    counts = jnp.sum(one_hot * listed_tile_count[None, :], axis=1)
    slot_ids = jnp.arange(listed_key_tiles.shape[1], dtype=jnp.int32)
    matched = (key_lists == key_tiles[:, None]) & (slot_ids[None, :] < counts[:, None])
    inside = (query_tiles >= 0) & (query_tiles < total_tiles)
    return jnp.any(matched, axis=1) & inside


def nt_dot(a, b):
    return lax.dot_general(a, b, (((1,), (1,)), ((), ())), preferred_element_type=jnp.float32)


def tn_dot(a, b):
    return lax.dot_general(a, b, (((0,), (0,)), ((), ())), preferred_element_type=jnp.float32)


def nn_dot(a, b):
    return lax.dot_general(a, b, (((1,), (0,)), ((), ())), preferred_element_type=jnp.float32)


def tile_pass(bias_ref, first, tile_query, tile_grad, keys, values):
    score_scale = HEAD_SIZE ** (-0.5)
    scores = [
        score_scale * nt_dot(tile_query, k) + bias_ref[first + i] for i, k in enumerate(keys)
    ]
    row_max = jnp.max(scores[0], axis=-1, keepdims=True)
    for s in scores[1:]:
        row_max = jnp.maximum(row_max, jnp.max(s, axis=-1, keepdims=True))
    total = sum(jnp.sum(jnp.exp(s - row_max), axis=-1, keepdims=True) for s in scores)
    log_total = row_max + jnp.log(total)
    weights = [jnp.exp(s - log_total).astype(jnp.bfloat16) for s in scores]
    grad_weights = [nt_dot(tile_grad, v) for v in values]
    row_dot = sum(
        jnp.sum(w.astype(jnp.float32) * g, axis=-1, keepdims=True)
        for w, g in zip(weights, grad_weights)
    )
    grad_scores = [
        (w.astype(jnp.float32) * (g - row_dot)).astype(jnp.bfloat16)
        for w, g in zip(weights, grad_weights)
    ]
    query_term = score_scale * sum(nn_dot(d, k) for d, k in zip(grad_scores, keys))
    key_terms = [score_scale * tn_dot(d, tile_query) for d in grad_scores]
    value_terms = [tn_dot(w, tile_grad) for w in weights]
    return query_term, key_terms, value_terms


def attention_kernel(
    bias_ref, q_ref, g_ref, k_ref, v_ref, left_ref, right_ref,
    dq_ref, dk_ref, dv_ref, to_left_ref, to_right_ref,
):
    q_a, q_b = q_ref[0, :TILE], q_ref[0, TILE:]
    g_a, g_b = g_ref[0, :TILE], g_ref[0, TILE:]
    k_a, k_b = k_ref[0, :TILE], k_ref[0, TILE:]
    v_a, v_b = v_ref[0, :TILE], v_ref[0, TILE:]
    k_l, v_l, k_r, v_r = left_ref[0, 0], left_ref[1, 0], right_ref[0, 0], right_ref[1, 0]
    dq_a, dk_a3, dv_a3 = tile_pass(bias_ref, 0, q_a, g_a, (k_l, k_a, k_b), (v_l, v_a, v_b))
    dq_b, dk_b3, dv_b3 = tile_pass(bias_ref, 3, q_b, g_b, (k_a, k_b, k_r), (v_a, v_b, v_r))
    dq_ref[0, :TILE] = dq_a.astype(jnp.bfloat16)
    dq_ref[0, TILE:] = dq_b.astype(jnp.bfloat16)
    dk_ref[0, :TILE] = (dk_a3[1] + dk_b3[0]).astype(jnp.bfloat16)
    dk_ref[0, TILE:] = (dk_a3[2] + dk_b3[1]).astype(jnp.bfloat16)
    dv_ref[0, :TILE] = (dv_a3[1] + dv_b3[0]).astype(jnp.bfloat16)
    dv_ref[0, TILE:] = (dv_a3[2] + dv_b3[1]).astype(jnp.bfloat16)
    to_left_ref[0, 0] = dk_a3[0].astype(jnp.bfloat16)
    to_left_ref[1, 0] = dv_a3[0].astype(jnp.bfloat16)
    to_right_ref[0, 0] = dk_b3[2].astype(jnp.bfloat16)
    to_right_ref[1, 0] = dv_b3[2].astype(jnp.bfloat16)


def attention_backward(bias, chunk, heads, queries, output_gradient, key_matrix, values, left, right):
    clip_count, block_len, _ = queries.shape
    whole = pl.BlockSpec((1, block_len, HEAD_SIZE), lambda c, h: (c, 0, h + chunk * heads))
    rim = pl.BlockSpec((2, 1, TILE, HEAD_SIZE), lambda c, h: (0, c, 0, h))
    out_whole = pl.BlockSpec((1, block_len, HEAD_SIZE), lambda c, h: (c, 0, h))
    whole_shape = jax.ShapeDtypeStruct((clip_count, block_len, heads * HEAD_SIZE), jnp.bfloat16)
    rim_shape = jax.ShapeDtypeStruct((2, clip_count, TILE, heads * HEAD_SIZE), jnp.bfloat16)
    return pl.pallas_call(
        attention_kernel,
        grid=(clip_count, heads),
        in_specs=[pl.BlockSpec(memory_space=pltpu.MemorySpace.SMEM)] + [whole] * 4 + [rim] * 2,
        out_specs=[out_whole] * 3 + [rim] * 2,
        out_shape=[whole_shape] * 3 + [rim_shape] * 2,
    )(bias, queries, output_gradient, key_matrix, values, left, right)


def on_device(
    queries,
    key_matrix,
    values,
    output_gradient,
    normed,
    adapter_down_weight,
    adapter_up_weight,
    listed_key_tiles,
    listed_tile_count,
):
    block_len = queries.shape[1]
    position = lax.axis_index("seq")
    first_tile = position * TILES_DEV

    down_piece = jnp.einsum(
        "pqg,gv->pqv", normed, adapter_down_weight, preferred_element_type=jnp.float32
    )
    lowered_rows = butterfly_sum(down_piece, "head").astype(jnp.bfloat16)

    tile_a, tile_b = first_tile, first_tile + 1
    allowed = chosen_pairs(
        listed_key_tiles,
        listed_tile_count,
        jnp.stack([tile_a, tile_a, tile_a, tile_b, tile_b, tile_b]).astype(jnp.int32),
        jnp.stack([tile_a - 1, tile_a, tile_b, tile_a, tile_b, tile_b + 1]).astype(jnp.int32),
    )
    bias = jnp.where(allowed, 0.0, masked_score).astype(jnp.float32)

    local_heads = queries.shape[2] // HEAD_SIZE
    chunks = 2 if local_heads % 2 == 0 else 1
    per_chunk = local_heads // chunks
    outs = []
    for chunk in range(chunks):
        cols = slice(chunk * per_chunk * HEAD_SIZE, (chunk + 1) * per_chunk * HEAD_SIZE)
        last_tile = jnp.stack(
            (key_matrix[:, block_len - TILE:, cols], values[:, block_len - TILE:, cols])
        )
        if chunk == 0:
            last_tile, lowered_rows = lax.optimization_barrier((last_tile, lowered_rows))
        left_kv = shifted(last_tile, "seq", 1)
        right_kv = shifted(
            jnp.stack((key_matrix[:, :TILE, cols], values[:, :TILE, cols]), 0), "seq", -1
        )
        dq, dk_own, dv_own, to_left, to_right = attention_backward(
            bias, chunk, per_chunk, queries, output_gradient, key_matrix, values, left_kv, right_kv
        )
        from_right = shifted(to_left, "seq", -1)
        from_left = shifted(to_right, "seq", 1)
        arrived = jnp.concatenate((from_left, from_right), 2).astype(jnp.float32)
        dk = (dk_own.astype(jnp.float32) + arrived[0]).astype(jnp.bfloat16)
        dv = (dv_own.astype(jnp.float32) + arrived[1]).astype(jnp.bfloat16)
        outs.append((dq, dk, dv))
    query_grad, key_grad, value_gradient = (
        jnp.concatenate([o[i] for o in outs], 2) for i in range(3)
    )

    backward_piece = jnp.einsum(
        "dsi,ji->dsj", value_gradient, adapter_up_weight, preferred_element_type=jnp.float32
    )
    backward_rows = butterfly_sum(backward_piece, "head").astype(jnp.bfloat16)
    gradient_down_local = adapter_scale * jnp.einsum(
        "yhm,yhz->mz", normed, backward_rows, preferred_element_type=jnp.float32
    )
    gradient_up_local = adapter_scale * jnp.einsum(
        "igb,igu->bu", lowered_rows, value_gradient, preferred_element_type=jnp.float32
    )
    both = jnp.stack((gradient_down_local.T, gradient_up_local), 0)
    both = all_sum(both, ("rep", "seq"))
    down_projection_grad, up_projection_grad = both[0].T, both[1]
    return (query_grad, key_grad, value_gradient, down_projection_grad, up_projection_grad)


def solution(mesh):
    in_specs = (
        P(("groups", "rep"), "seq", "head"),
        P(("groups", "rep"), "seq", "head"),
        P(("groups", "rep"), "seq", "head"),
        P(("groups", "rep"), "seq", "head"),
        P(("groups", "rep"), "seq", "head"),
        P("head", None),
        P(None, "head"),
        P("groups", None),
        P("groups"),
    )
    out_specs = (
        P(("groups", "rep"), "seq", "head"),
        P(("groups", "rep"), "seq", "head"),
        P(("groups", "rep"), "seq", "head"),
        P(("groups", "head"), None),
        P("groups", "head"),
    )
    return jax.shard_map(
        on_device, mesh=mesh, in_specs=in_specs, out_specs=out_specs, check_vma=False
    )
```

```python
import jax
import jax.numpy as jnp
from jax import lax
from jax.sharding import PartitionSpec as P
from jax.experimental import pallas as pl
from jax.experimental.pallas import tpu as pltpu

TILE = 384
TILES_DEV = 2
REACH = 1
HEAD_SIZE = 128


adapter_scale = 0.0078125
masked_score = -1e30


def shifted(shard, axis, by):
    peers = lax.axis_size(axis)
    pairs = [(i, i + by) for i in range(peers) if 0 <= i + by < peers]
    return lax.ppermute(shard, axis, pairs)


def butterfly_sum(tree, axis):
    peers = lax.axis_size(axis)
    if peers & (peers - 1):
        return lax.psum(tree, axis)
    step = 1
    while step < peers:
        pairs = [(i, i ^ step) for i in range(peers)]
        other = lax.ppermute(tree, axis, pairs)
        tree = jax.tree.map(lambda a, b: a + b, tree, other)
        step *= 2
    return tree


def scatter_sum(flat, axis, distances):
    peers = lax.axis_size(axis)
    index = lax.axis_index(axis)
    for step in distances:
        half = flat.shape[0] // 2
        upper = (index & step) != 0
        keep = jnp.where(upper, flat[half:], flat[:half])
        send = jnp.where(upper, flat[:half], flat[half:])
        flat = keep + lax.ppermute(send, axis, [(i, i ^ step) for i in range(peers)])
    return flat


def gather_back(flat, axis, distances):
    peers = lax.axis_size(axis)
    index = lax.axis_index(axis)
    for step in reversed(distances):
        other = lax.ppermute(flat, axis, [(i, i ^ step) for i in range(peers)])
        upper = (index & step) != 0
        flat = jnp.where(upper, jnp.concatenate((other, flat)), jnp.concatenate((flat, other)))
    return flat


def all_sum(array, axes):
    plan = []
    for axis in axes:
        peers = lax.axis_size(axis)
        if peers & (peers - 1):
            return lax.psum(array, axes)
        plan.append((axis, [1 << k for k in range(peers.bit_length() - 1)]))
    pieces = 1
    for _, distances in plan:
        pieces *= 1 << len(distances)
    flat = array.reshape(-1)
    if flat.shape[0] % pieces:
        return lax.psum(array, axes)
    inner, outer = plan[0], plan[1:]
    flat = scatter_sum(flat, inner[0], inner[1])
    for axis, distances in outer:
        flat = scatter_sum(flat, axis, distances[:-1])
        if distances:
            step = distances[-1]
            flat = flat + lax.ppermute(
                flat, axis, [(i, i ^ step) for i in range(lax.axis_size(axis))]
            )
        flat = gather_back(flat, axis, distances[:-1])
    flat = gather_back(flat, inner[0], inner[1])
    return flat.reshape(array.shape)


def chosen_pairs(listed_key_tiles, listed_tile_count, query_tiles, key_tiles):
    total_tiles = listed_key_tiles.shape[0]
    clipped = jnp.clip(query_tiles, 0, total_tiles - 1)
    one_hot = (clipped[:, None] == jnp.arange(total_tiles, dtype=jnp.int32)[None, :]).astype(
        jnp.int32
    )
    key_lists = jnp.sum(one_hot[:, :, None] * listed_key_tiles[None, :, :], axis=1)
    counts = jnp.sum(one_hot * listed_tile_count[None, :], axis=1)
    slot_ids = jnp.arange(listed_key_tiles.shape[1], dtype=jnp.int32)
    matched = (key_lists == key_tiles[:, None]) & (slot_ids[None, :] < counts[:, None])
    inside = (query_tiles >= 0) & (query_tiles < total_tiles)
    return jnp.any(matched, axis=1) & inside


def nt_dot(a, b):
    return lax.dot_general(a, b, (((1,), (1,)), ((), ())), preferred_element_type=jnp.float32)


def tn_dot(a, b):
    return lax.dot_general(a, b, (((0,), (0,)), ((), ())), preferred_element_type=jnp.float32)


def nn_dot(a, b):
    return lax.dot_general(a, b, (((1,), (0,)), ((), ())), preferred_element_type=jnp.float32)


def tile_pass(bias_ref, first, tile_query, tile_grad, keys, values):
    score_scale = HEAD_SIZE ** (-0.5)
    scores = [
        score_scale * nt_dot(tile_query, k) + bias_ref[first + i] for i, k in enumerate(keys)
    ]
    row_max = jnp.max(scores[0], axis=-1, keepdims=True)
    for s in scores[1:]:
        row_max = jnp.maximum(row_max, jnp.max(s, axis=-1, keepdims=True))
    total = sum(jnp.sum(jnp.exp(s - row_max), axis=-1, keepdims=True) for s in scores)
    log_total = row_max + jnp.log(total)
    weights = [jnp.exp(s - log_total).astype(jnp.bfloat16) for s in scores]
    grad_weights = [nt_dot(tile_grad, v) for v in values]
    row_dot = sum(
        jnp.sum(w.astype(jnp.float32) * g, axis=-1, keepdims=True)
        for w, g in zip(weights, grad_weights)
    )
    grad_scores = [
        (w.astype(jnp.float32) * (g - row_dot)).astype(jnp.bfloat16)
        for w, g in zip(weights, grad_weights)
    ]
    query_term = score_scale * sum(nn_dot(d, k) for d, k in zip(grad_scores, keys))
    key_terms = [score_scale * tn_dot(d, tile_query) for d in grad_scores]
    value_terms = [tn_dot(w, tile_grad) for w in weights]
    return query_term, key_terms, value_terms


def attention_kernel(
    bias_ref, q_ref, g_ref, k_ref, v_ref, left_ref, right_ref,
    dq_ref, dk_ref, dv_ref, to_left_ref, to_right_ref,
):
    q_a, q_b = q_ref[0, :TILE], q_ref[0, TILE:]
    g_a, g_b = g_ref[0, :TILE], g_ref[0, TILE:]
    k_a, k_b = k_ref[0, :TILE], k_ref[0, TILE:]
    v_a, v_b = v_ref[0, :TILE], v_ref[0, TILE:]
    k_l, v_l, k_r, v_r = left_ref[0, 0], left_ref[1, 0], right_ref[0, 0], right_ref[1, 0]
    dq_a, dk_a3, dv_a3 = tile_pass(bias_ref, 0, q_a, g_a, (k_l, k_a, k_b), (v_l, v_a, v_b))
    dq_b, dk_b3, dv_b3 = tile_pass(bias_ref, 3, q_b, g_b, (k_a, k_b, k_r), (v_a, v_b, v_r))
    dq_ref[0, :TILE] = dq_a.astype(jnp.bfloat16)
    dq_ref[0, TILE:] = dq_b.astype(jnp.bfloat16)
    dk_ref[0, :TILE] = (dk_a3[1] + dk_b3[0]).astype(jnp.bfloat16)
    dk_ref[0, TILE:] = (dk_a3[2] + dk_b3[1]).astype(jnp.bfloat16)
    dv_ref[0, :TILE] = (dv_a3[1] + dv_b3[0]).astype(jnp.bfloat16)
    dv_ref[0, TILE:] = (dv_a3[2] + dv_b3[1]).astype(jnp.bfloat16)
    to_left_ref[0, 0] = dk_a3[0].astype(jnp.bfloat16)
    to_left_ref[1, 0] = dv_a3[0].astype(jnp.bfloat16)
    to_right_ref[0, 0] = dk_b3[2].astype(jnp.bfloat16)
    to_right_ref[1, 0] = dv_b3[2].astype(jnp.bfloat16)


def attention_backward(bias, chunk, heads, queries, output_gradient, key_matrix, values, left, right):
    clip_count, block_len, _ = queries.shape
    whole = pl.BlockSpec((1, block_len, HEAD_SIZE), lambda c, h: (c, 0, h + chunk * heads))
    rim = pl.BlockSpec((2, 1, TILE, HEAD_SIZE), lambda c, h: (0, c, 0, h))
    out_whole = pl.BlockSpec((1, block_len, HEAD_SIZE), lambda c, h: (c, 0, h))
    whole_shape = jax.ShapeDtypeStruct((clip_count, block_len, heads * HEAD_SIZE), jnp.bfloat16)
    rim_shape = jax.ShapeDtypeStruct((2, clip_count, TILE, heads * HEAD_SIZE), jnp.bfloat16)
    return pl.pallas_call(
        attention_kernel,
        grid=(clip_count, heads),
        in_specs=[pl.BlockSpec(memory_space=pltpu.MemorySpace.SMEM)] + [whole] * 4 + [rim] * 2,
        out_specs=[out_whole] * 3 + [rim] * 2,
        out_shape=[whole_shape] * 3 + [rim_shape] * 2,
    )(bias, queries, output_gradient, key_matrix, values, left, right)


def on_device(
    queries,
    key_matrix,
    values,
    output_gradient,
    normed,
    adapter_down_weight,
    adapter_up_weight,
    listed_key_tiles,
    listed_tile_count,
):
    block_len = queries.shape[1]
    position = lax.axis_index("seq")
    first_tile = position * TILES_DEV

    down_piece = jnp.einsum(
        "pqg,gv->pqv", normed, adapter_down_weight, preferred_element_type=jnp.float32
    )
    lowered_rows = butterfly_sum(down_piece, "head").astype(jnp.bfloat16)

    tile_a, tile_b = first_tile, first_tile + 1
    allowed = chosen_pairs(
        listed_key_tiles,
        listed_tile_count,
        jnp.stack([tile_a, tile_a, tile_a, tile_b, tile_b, tile_b]).astype(jnp.int32),
        jnp.stack([tile_a - 1, tile_a, tile_b, tile_a, tile_b, tile_b + 1]).astype(jnp.int32),
    )
    bias = jnp.where(allowed, 0.0, masked_score).astype(jnp.float32)

    local_heads = queries.shape[2] // HEAD_SIZE
    chunks = 3 if local_heads % 3 == 0 else (2 if local_heads % 2 == 0 else 1)
    per_chunk = local_heads // chunks
    outs = []
    for chunk in range(chunks):
        cols = slice(chunk * per_chunk * HEAD_SIZE, (chunk + 1) * per_chunk * HEAD_SIZE)
        left_kv = shifted(
            jnp.stack((key_matrix[:, block_len - TILE:, cols], values[:, block_len - TILE:, cols])),
            "seq",
            1,
        )
        right_kv = shifted(
            jnp.stack((key_matrix[:, :TILE, cols], values[:, :TILE, cols]), 0), "seq", -1
        )
        dq, dk_own, dv_own, to_left, to_right = attention_backward(
            bias, chunk, per_chunk, queries, output_gradient, key_matrix, values, left_kv, right_kv
        )
        from_right = shifted(to_left, "seq", -1)
        from_left = shifted(to_right, "seq", 1)
        arrived = jnp.concatenate((from_left, from_right), 2).astype(jnp.float32)
        dk = (dk_own.astype(jnp.float32) + arrived[0]).astype(jnp.bfloat16)
        dv = (dv_own.astype(jnp.float32) + arrived[1]).astype(jnp.bfloat16)
        outs.append((dq, dk, dv))
    query_grad, key_grad, value_gradient = (
        jnp.concatenate([o[i] for o in outs], 2) for i in range(3)
    )

    backward_piece = jnp.einsum(
        "dsi,ji->dsj", value_gradient, adapter_up_weight, preferred_element_type=jnp.float32
    )
    backward_rows = butterfly_sum(backward_piece, "head").astype(jnp.bfloat16)
    gradient_down_local = adapter_scale * jnp.einsum(
        "yhm,yhz->mz", normed, backward_rows, preferred_element_type=jnp.float32
    )
    gradient_up_local = adapter_scale * jnp.einsum(
        "igb,igu->bu", lowered_rows, value_gradient, preferred_element_type=jnp.float32
    )
    both = jnp.stack((gradient_down_local.T, gradient_up_local), 0)
    both = all_sum(both, ("rep", "seq"))
    down_projection_grad, up_projection_grad = both[0].T, both[1]
    return (query_grad, key_grad, value_gradient, down_projection_grad, up_projection_grad)


def solution(mesh):
    in_specs = (
        P(("groups", "rep"), "seq", "head"),
        P(("groups", "rep"), "seq", "head"),
        P(("groups", "rep"), "seq", "head"),
        P(("groups", "rep"), "seq", "head"),
        P(("groups", "rep"), "seq", "head"),
        P("head", None),
        P(None, "head"),
        P("groups", None),
        P("groups"),
    )
    out_specs = (
        P(("groups", "rep"), "seq", "head"),
        P(("groups", "rep"), "seq", "head"),
        P(("groups", "rep"), "seq", "head"),
        P(("groups", "head"), None),
        P("groups", "head"),
    )
    return jax.shard_map(
        on_device, mesh=mesh, in_specs=in_specs, out_specs=out_specs, check_vma=False
    )
```

```python
import jax
import jax.numpy as jnp
from jax import lax
from jax.sharding import PartitionSpec as P
from jax.experimental import pallas as pl
from jax.experimental.pallas import tpu as pltpu

TILE = 384
TILES_DEV = 2
REACH = 1
HEAD_SIZE = 128


adapter_scale = 0.0078125
masked_score = -1e30


def shifted(shard, axis, by):
    peers = lax.axis_size(axis)
    pairs = [(i, i + by) for i in range(peers) if 0 <= i + by < peers]
    return lax.ppermute(shard, axis, pairs)


def butterfly_sum(tree, axis):
    peers = lax.axis_size(axis)
    if peers & (peers - 1):
        return lax.psum(tree, axis)
    step = 1
    while step < peers:
        pairs = [(i, i ^ step) for i in range(peers)]
        other = lax.ppermute(tree, axis, pairs)
        tree = jax.tree.map(lambda a, b: a + b, tree, other)
        step *= 2
    return tree


def scatter_sum(flat, axis, distances):
    peers = lax.axis_size(axis)
    index = lax.axis_index(axis)
    for step in distances:
        half = flat.shape[0] // 2
        upper = (index & step) != 0
        keep = jnp.where(upper, flat[half:], flat[:half])
        send = jnp.where(upper, flat[:half], flat[half:])
        flat = keep + lax.ppermute(send, axis, [(i, i ^ step) for i in range(peers)])
    return flat


def gather_back(flat, axis, distances):
    peers = lax.axis_size(axis)
    index = lax.axis_index(axis)
    for step in reversed(distances):
        other = lax.ppermute(flat, axis, [(i, i ^ step) for i in range(peers)])
        upper = (index & step) != 0
        flat = jnp.where(upper, jnp.concatenate((other, flat)), jnp.concatenate((flat, other)))
    return flat


def all_sum(array, axes):
    plan = []
    for axis in axes:
        peers = lax.axis_size(axis)
        if peers & (peers - 1):
            return lax.psum(array, axes)
        plan.append((axis, [1 << k for k in range(peers.bit_length() - 1)]))
    pieces = 1
    for _, distances in plan:
        pieces *= 1 << len(distances)
    flat = array.reshape(-1)
    if flat.shape[0] % pieces:
        return lax.psum(array, axes)
    inner, outer = plan[0], plan[1:]
    flat = scatter_sum(flat, inner[0], inner[1])
    for axis, distances in outer:
        flat = scatter_sum(flat, axis, distances[:-1])
        if distances:
            step = distances[-1]
            flat = flat + lax.ppermute(
                flat, axis, [(i, i ^ step) for i in range(lax.axis_size(axis))]
            )
        flat = gather_back(flat, axis, distances[:-1])
    flat = gather_back(flat, inner[0], inner[1])
    return flat.reshape(array.shape)


def chosen_pairs(listed_key_tiles, listed_tile_count, query_tiles, key_tiles):
    total_tiles = listed_key_tiles.shape[0]
    clipped = jnp.clip(query_tiles, 0, total_tiles - 1)
    one_hot = (clipped[:, None] == jnp.arange(total_tiles, dtype=jnp.int32)[None, :]).astype(
        jnp.int32
    )
    key_lists = jnp.sum(one_hot[:, :, None] * listed_key_tiles[None, :, :], axis=1)
    counts = jnp.sum(one_hot * listed_tile_count[None, :], axis=1)
    slot_ids = jnp.arange(listed_key_tiles.shape[1], dtype=jnp.int32)
    matched = (key_lists == key_tiles[:, None]) & (slot_ids[None, :] < counts[:, None])
    inside = (query_tiles >= 0) & (query_tiles < total_tiles)
    return jnp.any(matched, axis=1) & inside


def nt_dot(a, b):
    return lax.dot_general(a, b, (((1,), (1,)), ((), ())), preferred_element_type=jnp.float32)


def tn_dot(a, b):
    return lax.dot_general(a, b, (((0,), (0,)), ((), ())), preferred_element_type=jnp.float32)


def nn_dot(a, b):
    return lax.dot_general(a, b, (((1,), (0,)), ((), ())), preferred_element_type=jnp.float32)


def tile_pass(bias_ref, first, tile_query, tile_grad, keys, values):
    score_scale = HEAD_SIZE ** (-0.5)
    scores = [
        score_scale * nt_dot(tile_query, k) + bias_ref[first + i] for i, k in enumerate(keys)
    ]
    row_max = jnp.max(scores[0], axis=-1, keepdims=True)
    for s in scores[1:]:
        row_max = jnp.maximum(row_max, jnp.max(s, axis=-1, keepdims=True))
    total = sum(jnp.sum(jnp.exp(s - row_max), axis=-1, keepdims=True) for s in scores)
    log_total = row_max + jnp.log(total)
    weights = [jnp.exp(s - log_total).astype(jnp.bfloat16) for s in scores]
    grad_weights = [nt_dot(tile_grad, v) for v in values]
    row_dot = sum(
        jnp.sum(w.astype(jnp.float32) * g, axis=-1, keepdims=True)
        for w, g in zip(weights, grad_weights)
    )
    grad_scores = [
        (w.astype(jnp.float32) * (g - row_dot)).astype(jnp.bfloat16)
        for w, g in zip(weights, grad_weights)
    ]
    query_term = score_scale * sum(nn_dot(d, k) for d, k in zip(grad_scores, keys))
    key_terms = [score_scale * tn_dot(d, tile_query) for d in grad_scores]
    value_terms = [tn_dot(w, tile_grad) for w in weights]
    return query_term, key_terms, value_terms


def attention_kernel(
    bias_ref, q_ref, g_ref, k_ref, v_ref, left_ref, right_ref,
    dq_ref, dk_ref, dv_ref, to_left_ref, to_right_ref,
):
    q_a, q_b = q_ref[0, :TILE], q_ref[0, TILE:]
    g_a, g_b = g_ref[0, :TILE], g_ref[0, TILE:]
    k_a, k_b = k_ref[0, :TILE], k_ref[0, TILE:]
    v_a, v_b = v_ref[0, :TILE], v_ref[0, TILE:]
    k_l, v_l, k_r, v_r = left_ref[0, 0], left_ref[1, 0], right_ref[0, 0], right_ref[1, 0]
    dq_a, dk_a3, dv_a3 = tile_pass(bias_ref, 0, q_a, g_a, (k_l, k_a, k_b), (v_l, v_a, v_b))
    dq_b, dk_b3, dv_b3 = tile_pass(bias_ref, 3, q_b, g_b, (k_a, k_b, k_r), (v_a, v_b, v_r))
    dq_ref[0, :TILE] = dq_a.astype(jnp.bfloat16)
    dq_ref[0, TILE:] = dq_b.astype(jnp.bfloat16)
    dk_ref[0, :TILE] = (dk_a3[1] + dk_b3[0]).astype(jnp.bfloat16)
    dk_ref[0, TILE:] = (dk_a3[2] + dk_b3[1]).astype(jnp.bfloat16)
    dv_ref[0, :TILE] = (dv_a3[1] + dv_b3[0]).astype(jnp.bfloat16)
    dv_ref[0, TILE:] = (dv_a3[2] + dv_b3[1]).astype(jnp.bfloat16)
    to_left_ref[0, 0] = dk_a3[0].astype(jnp.bfloat16)
    to_left_ref[1, 0] = dv_a3[0].astype(jnp.bfloat16)
    to_right_ref[0, 0] = dk_b3[2].astype(jnp.bfloat16)
    to_right_ref[1, 0] = dv_b3[2].astype(jnp.bfloat16)


def attention_backward(bias, chunk, heads, queries, output_gradient, key_matrix, values, left, right):
    clip_count, block_len, _ = queries.shape
    whole = pl.BlockSpec((1, block_len, HEAD_SIZE), lambda c, h: (c, 0, h + chunk * heads))
    rim = pl.BlockSpec((2, 1, TILE, HEAD_SIZE), lambda c, h: (0, c, 0, h))
    out_whole = pl.BlockSpec((1, block_len, HEAD_SIZE), lambda c, h: (c, 0, h))
    whole_shape = jax.ShapeDtypeStruct((clip_count, block_len, heads * HEAD_SIZE), jnp.bfloat16)
    rim_shape = jax.ShapeDtypeStruct((2, clip_count, TILE, heads * HEAD_SIZE), jnp.bfloat16)
    return pl.pallas_call(
        attention_kernel,
        grid=(clip_count, heads),
        in_specs=[pl.BlockSpec(memory_space=pltpu.MemorySpace.SMEM)] + [whole] * 4 + [rim] * 2,
        out_specs=[out_whole] * 3 + [rim] * 2,
        out_shape=[whole_shape] * 3 + [rim_shape] * 2,
    )(bias, queries, output_gradient, key_matrix, values, left, right)


def on_device(
    queries,
    key_matrix,
    values,
    output_gradient,
    normed,
    adapter_down_weight,
    adapter_up_weight,
    listed_key_tiles,
    listed_tile_count,
):
    block_len = queries.shape[1]
    position = lax.axis_index("seq")
    first_tile = position * TILES_DEV

    down_piece = jnp.einsum(
        "pqg,gv->pqv", normed, adapter_down_weight, preferred_element_type=jnp.float32
    )
    lowered_rows = butterfly_sum(down_piece, "head").astype(jnp.bfloat16)

    tile_a, tile_b = first_tile, first_tile + 1
    allowed = chosen_pairs(
        listed_key_tiles,
        listed_tile_count,
        jnp.stack([tile_a, tile_a, tile_a, tile_b, tile_b, tile_b]).astype(jnp.int32),
        jnp.stack([tile_a - 1, tile_a, tile_b, tile_a, tile_b, tile_b + 1]).astype(jnp.int32),
    )
    bias = jnp.where(allowed, 0.0, masked_score).astype(jnp.float32)

    local_heads = queries.shape[2] // HEAD_SIZE
    chunks = 2 if local_heads % 2 == 0 else 1
    per_chunk = local_heads // chunks
    def project(term, up_cols):
        return jnp.einsum("dsi,ji->dsj", term, up_cols, preferred_element_type=jnp.float32)

    outs, pieces = [], []
    for chunk in range(chunks):
        cols = slice(chunk * per_chunk * HEAD_SIZE, (chunk + 1) * per_chunk * HEAD_SIZE)
        left_kv = shifted(
            jnp.stack((key_matrix[:, block_len - TILE:, cols], values[:, block_len - TILE:, cols])),
            "seq",
            1,
        )
        right_kv = shifted(
            jnp.stack((key_matrix[:, :TILE, cols], values[:, :TILE, cols]), 0), "seq", -1
        )
        dq, dk_own, dv_own, to_left, to_right = attention_backward(
            bias, chunk, per_chunk, queries, output_gradient, key_matrix, values, left_kv, right_kv
        )
        from_right = shifted(to_left, "seq", -1)
        from_left = shifted(to_right, "seq", 1)
        arrived = jnp.concatenate((from_left, from_right), 2).astype(jnp.float32)
        dk = (dk_own.astype(jnp.float32) + arrived[0]).astype(jnp.bfloat16)
        dv = (dv_own.astype(jnp.float32) + arrived[1]).astype(jnp.bfloat16)
        up_cols = adapter_up_weight[:, cols]
        if chunk < chunks - 1:
            pieces.append(project(dv, up_cols))
        else:
            pieces.append(project(dv_own, up_cols))
            sent = butterfly_sum(
                jnp.stack((project(to_left[1], up_cols), project(to_right[1], up_cols))), "head"
            )
            late = jnp.concatenate(
                (shifted(sent[1], "seq", 1), shifted(sent[0], "seq", -1)), 1
            )
        outs.append((dq, dk, dv))
    query_grad, key_grad, value_gradient = (
        jnp.concatenate([o[i] for o in outs], 2) for i in range(3)
    )

    backward_piece = pieces[0]
    for piece in pieces[1:]:
        backward_piece = backward_piece + piece
    backward_rows = (butterfly_sum(backward_piece, "head") + late).astype(jnp.bfloat16)
    gradient_down_local = adapter_scale * jnp.einsum(
        "yhm,yhz->mz", normed, backward_rows, preferred_element_type=jnp.float32
    )
    gradient_up_local = adapter_scale * jnp.einsum(
        "igb,igu->bu", lowered_rows, value_gradient, preferred_element_type=jnp.float32
    )
    both = jnp.stack((gradient_down_local.T, gradient_up_local), 0)
    both = all_sum(both, ("rep", "seq"))
    down_projection_grad, up_projection_grad = both[0].T, both[1]
    return (query_grad, key_grad, value_gradient, down_projection_grad, up_projection_grad)


def solution(mesh):
    in_specs = (
        P(("groups", "rep"), "seq", "head"),
        P(("groups", "rep"), "seq", "head"),
        P(("groups", "rep"), "seq", "head"),
        P(("groups", "rep"), "seq", "head"),
        P(("groups", "rep"), "seq", "head"),
        P("head", None),
        P(None, "head"),
        P("groups", None),
        P("groups"),
    )
    out_specs = (
        P(("groups", "rep"), "seq", "head"),
        P(("groups", "rep"), "seq", "head"),
        P(("groups", "rep"), "seq", "head"),
        P(("groups", "head"), None),
        P("groups", "head"),
    )
    return jax.shard_map(
        on_device, mesh=mesh, in_specs=in_specs, out_specs=out_specs, check_vma=False
    )
```

```python
import jax
import jax.numpy as jnp
from jax import lax
from jax.sharding import PartitionSpec as P
from jax.experimental import pallas as pl
from jax.experimental.pallas import tpu as pltpu

TILE = 384
TILES_DEV = 2
REACH = 1
HEAD_SIZE = 128


adapter_scale = 0.0078125
masked_score = -1e30


def shifted(shard, axis, by):
    peers = lax.axis_size(axis)
    pairs = [(i, i + by) for i in range(peers) if 0 <= i + by < peers]
    return lax.ppermute(shard, axis, pairs)


def butterfly_sum(tree, axis):
    peers = lax.axis_size(axis)
    if peers & (peers - 1):
        return lax.psum(tree, axis)
    step = 1
    while step < peers:
        pairs = [(i, i ^ step) for i in range(peers)]
        other = lax.ppermute(tree, axis, pairs)
        tree = jax.tree.map(lambda a, b: a + b, tree, other)
        step *= 2
    return tree


def scatter_sum(flat, axis, distances):
    peers = lax.axis_size(axis)
    index = lax.axis_index(axis)
    for step in distances:
        half = flat.shape[0] // 2
        upper = (index & step) != 0
        keep = jnp.where(upper, flat[half:], flat[:half])
        send = jnp.where(upper, flat[:half], flat[half:])
        flat = keep + lax.ppermute(send, axis, [(i, i ^ step) for i in range(peers)])
    return flat


def gather_back(flat, axis, distances):
    peers = lax.axis_size(axis)
    index = lax.axis_index(axis)
    for step in reversed(distances):
        other = lax.ppermute(flat, axis, [(i, i ^ step) for i in range(peers)])
        upper = (index & step) != 0
        flat = jnp.where(upper, jnp.concatenate((other, flat)), jnp.concatenate((flat, other)))
    return flat


def all_sum(array, axes):
    plan = []
    for axis in axes:
        peers = lax.axis_size(axis)
        if peers & (peers - 1):
            return lax.psum(array, axes)
        plan.append((axis, [1 << k for k in range(peers.bit_length() - 1)]))
    pieces = 1
    for _, distances in plan:
        pieces *= 1 << len(distances)
    flat = array.reshape(-1)
    if flat.shape[0] % pieces:
        return lax.psum(array, axes)
    inner, outer = plan[0], plan[1:]
    flat = scatter_sum(flat, inner[0], inner[1])
    for axis, distances in outer:
        flat = scatter_sum(flat, axis, distances[:-1])
        if distances:
            step = distances[-1]
            flat = flat + lax.ppermute(
                flat, axis, [(i, i ^ step) for i in range(lax.axis_size(axis))]
            )
        flat = gather_back(flat, axis, distances[:-1])
    flat = gather_back(flat, inner[0], inner[1])
    return flat.reshape(array.shape)


def chosen_pairs(listed_key_tiles, listed_tile_count, query_tiles, key_tiles):
    total_tiles = listed_key_tiles.shape[0]
    clipped = jnp.clip(query_tiles, 0, total_tiles - 1)
    one_hot = (clipped[:, None] == jnp.arange(total_tiles, dtype=jnp.int32)[None, :]).astype(
        jnp.int32
    )
    key_lists = jnp.sum(one_hot[:, :, None] * listed_key_tiles[None, :, :], axis=1)
    counts = jnp.sum(one_hot * listed_tile_count[None, :], axis=1)
    slot_ids = jnp.arange(listed_key_tiles.shape[1], dtype=jnp.int32)
    matched = (key_lists == key_tiles[:, None]) & (slot_ids[None, :] < counts[:, None])
    inside = (query_tiles >= 0) & (query_tiles < total_tiles)
    return jnp.any(matched, axis=1) & inside


def nt_dot(a, b):
    return lax.dot_general(a, b, (((1,), (1,)), ((), ())), preferred_element_type=jnp.float32)


def tn_dot(a, b):
    return lax.dot_general(a, b, (((0,), (0,)), ((), ())), preferred_element_type=jnp.float32)


def nn_dot(a, b):
    return lax.dot_general(a, b, (((1,), (0,)), ((), ())), preferred_element_type=jnp.float32)


def tile_pass(bias_ref, first, tile_query, tile_grad, keys, values):
    score_scale = HEAD_SIZE ** (-0.5)
    scores = [
        score_scale * nt_dot(tile_query, k) + bias_ref[first + i] for i, k in enumerate(keys)
    ]
    row_max = jnp.max(scores[0], axis=-1, keepdims=True)
    for s in scores[1:]:
        row_max = jnp.maximum(row_max, jnp.max(s, axis=-1, keepdims=True))
    total = sum(jnp.sum(jnp.exp(s - row_max), axis=-1, keepdims=True) for s in scores)
    log_total = row_max + jnp.log(total)
    weights = [jnp.exp(s - log_total).astype(jnp.bfloat16) for s in scores]
    grad_weights = [nt_dot(tile_grad, v) for v in values]
    row_dot = sum(
        jnp.sum(w.astype(jnp.float32) * g, axis=-1, keepdims=True)
        for w, g in zip(weights, grad_weights)
    )
    grad_scores = [
        (w.astype(jnp.float32) * (g - row_dot)).astype(jnp.bfloat16)
        for w, g in zip(weights, grad_weights)
    ]
    query_term = score_scale * sum(nn_dot(d, k) for d, k in zip(grad_scores, keys))
    key_terms = [score_scale * tn_dot(d, tile_query) for d in grad_scores]
    value_terms = [tn_dot(w, tile_grad) for w in weights]
    return query_term, key_terms, value_terms


def attention_kernel(
    bias_ref, q_ref, g_ref, k_ref, v_ref, left_ref, right_ref,
    dq_ref, dk_ref, dv_ref, to_left_ref, to_right_ref,
):
    q_a, q_b = q_ref[0, :TILE], q_ref[0, TILE:]
    g_a, g_b = g_ref[0, :TILE], g_ref[0, TILE:]
    k_a, k_b = k_ref[0, :TILE], k_ref[0, TILE:]
    v_a, v_b = v_ref[0, :TILE], v_ref[0, TILE:]
    k_l, v_l, k_r, v_r = left_ref[0, 0], left_ref[1, 0], right_ref[0, 0], right_ref[1, 0]
    dq_a, dk_a3, dv_a3 = tile_pass(bias_ref, 0, q_a, g_a, (k_l, k_a, k_b), (v_l, v_a, v_b))
    dq_b, dk_b3, dv_b3 = tile_pass(bias_ref, 3, q_b, g_b, (k_a, k_b, k_r), (v_a, v_b, v_r))
    dq_ref[0, :TILE] = dq_a.astype(jnp.bfloat16)
    dq_ref[0, TILE:] = dq_b.astype(jnp.bfloat16)
    dk_ref[0, :TILE] = (dk_a3[1] + dk_b3[0]).astype(jnp.bfloat16)
    dk_ref[0, TILE:] = (dk_a3[2] + dk_b3[1]).astype(jnp.bfloat16)
    dv_ref[0, :TILE] = (dv_a3[1] + dv_b3[0]).astype(jnp.bfloat16)
    dv_ref[0, TILE:] = (dv_a3[2] + dv_b3[1]).astype(jnp.bfloat16)
    to_left_ref[0, 0] = dk_a3[0].astype(jnp.bfloat16)
    to_left_ref[1, 0] = dv_a3[0].astype(jnp.bfloat16)
    to_right_ref[0, 0] = dk_b3[2].astype(jnp.bfloat16)
    to_right_ref[1, 0] = dv_b3[2].astype(jnp.bfloat16)


def attention_backward(bias, chunk, heads, queries, output_gradient, key_matrix, values, left, right):
    clip_count, block_len, _ = queries.shape
    whole = pl.BlockSpec((1, block_len, HEAD_SIZE), lambda c, h: (c, 0, h + chunk * heads))
    rim = pl.BlockSpec((2, 1, TILE, HEAD_SIZE), lambda c, h: (0, c, 0, h))
    out_whole = pl.BlockSpec((1, block_len, HEAD_SIZE), lambda c, h: (c, 0, h))
    whole_shape = jax.ShapeDtypeStruct((clip_count, block_len, heads * HEAD_SIZE), jnp.bfloat16)
    rim_shape = jax.ShapeDtypeStruct((2, clip_count, TILE, heads * HEAD_SIZE), jnp.bfloat16)
    return pl.pallas_call(
        attention_kernel,
        grid=(clip_count, heads),
        in_specs=[pl.BlockSpec(memory_space=pltpu.MemorySpace.SMEM)] + [whole] * 4 + [rim] * 2,
        out_specs=[out_whole] * 3 + [rim] * 2,
        out_shape=[whole_shape] * 3 + [rim_shape] * 2,
    )(bias, queries, output_gradient, key_matrix, values, left, right)


def on_device(
    queries,
    key_matrix,
    values,
    output_gradient,
    normed,
    adapter_down_weight,
    adapter_up_weight,
    listed_key_tiles,
    listed_tile_count,
):
    block_len = queries.shape[1]
    position = lax.axis_index("seq")
    first_tile = position * TILES_DEV

    down_piece = jnp.einsum(
        "pqg,gv->pqv", normed, adapter_down_weight, preferred_element_type=jnp.float32
    )
    lowered_rows = butterfly_sum(down_piece, "head").astype(jnp.bfloat16)

    tile_a, tile_b = first_tile, first_tile + 1
    allowed = chosen_pairs(
        listed_key_tiles,
        listed_tile_count,
        jnp.stack([tile_a, tile_a, tile_a, tile_b, tile_b, tile_b]).astype(jnp.int32),
        jnp.stack([tile_a - 1, tile_a, tile_b, tile_a, tile_b, tile_b + 1]).astype(jnp.int32),
    )
    bias = jnp.where(allowed, 0.0, masked_score).astype(jnp.float32)

    local_heads = queries.shape[2] // HEAD_SIZE
    chunks = 2 if local_heads % 2 == 0 else 1
    per_chunk = local_heads // chunks
    outs = []
    for chunk in range(chunks):
        cols = slice(chunk * per_chunk * HEAD_SIZE, (chunk + 1) * per_chunk * HEAD_SIZE)
        left_kv = shifted(
            jnp.stack((key_matrix[:, block_len - TILE:, cols], values[:, block_len - TILE:, cols])),
            "seq",
            1,
        )
        right_kv = shifted(
            jnp.stack((key_matrix[:, :TILE, cols], values[:, :TILE, cols]), 0), "seq", -1
        )
        dq, dk_own, dv_own, to_left, to_right = attention_backward(
            bias, chunk, per_chunk, queries, output_gradient, key_matrix, values, left_kv, right_kv
        )
        from_right = shifted(to_left, "seq", -1)
        from_left = shifted(to_right, "seq", 1)
        arrived = jnp.concatenate((from_left, from_right), 2).astype(jnp.float32)
        dk = (dk_own.astype(jnp.float32) + arrived[0]).astype(jnp.bfloat16)
        dv = (dv_own.astype(jnp.float32) + arrived[1]).astype(jnp.bfloat16)
        outs.append((dq, dk, dv))
    query_grad, key_grad, value_gradient = (
        jnp.concatenate([o[i] for o in outs], 2) for i in range(3)
    )

    backward_piece = jnp.einsum(
        "dsi,ji->dsj", value_gradient, adapter_up_weight, preferred_element_type=jnp.float32
    )
    head_peers = lax.axis_size("head")
    step = 1
    while step < head_peers:
        sent = backward_piece.astype(jnp.bfloat16)
        other = lax.ppermute(sent, "head", [(i, i ^ step) for i in range(head_peers)])
        backward_piece = sent.astype(jnp.float32) + other.astype(jnp.float32)
        step *= 2
    backward_rows = backward_piece.astype(jnp.bfloat16)
    gradient_down_local = adapter_scale * jnp.einsum(
        "yhm,yhz->mz", normed, backward_rows, preferred_element_type=jnp.float32
    )
    gradient_up_local = adapter_scale * jnp.einsum(
        "igb,igu->bu", lowered_rows, value_gradient, preferred_element_type=jnp.float32
    )
    both = jnp.stack((gradient_down_local.T, gradient_up_local), 0)
    both = all_sum(both, ("rep", "seq"))
    down_projection_grad, up_projection_grad = both[0].T, both[1]
    return (query_grad, key_grad, value_gradient, down_projection_grad, up_projection_grad)


def solution(mesh):
    in_specs = (
        P(("groups", "rep"), "seq", "head"),
        P(("groups", "rep"), "seq", "head"),
        P(("groups", "rep"), "seq", "head"),
        P(("groups", "rep"), "seq", "head"),
        P(("groups", "rep"), "seq", "head"),
        P("head", None),
        P(None, "head"),
        P("groups", None),
        P("groups"),
    )
    out_specs = (
        P(("groups", "rep"), "seq", "head"),
        P(("groups", "rep"), "seq", "head"),
        P(("groups", "rep"), "seq", "head"),
        P(("groups", "head"), None),
        P("groups", "head"),
    )
    return jax.shard_map(
        on_device, mesh=mesh, in_specs=in_specs, out_specs=out_specs, check_vma=False
    )
```
